32 devices in a mesh: groups: 2 (over y), seq: 4 (over x, core), fsdp: 4 (over z).
Axes of the slice: x: 2, y: 2, z: 4, core: 2. Of those that a mesh axis runs over, the one named last changes fastest.
Arguments:
- tokens: bfloat16 [16, 512, 1536], P(('groups', 'fsdp'), 'seq'), parts along dimension 0, may hold values from -6 to 6
- in_weight: bfloat16 [1536, 4608], P(None, 'fsdp'), may hold values from -0.15625 to 0.15625
- short_weight: float32 [3, 4608], replicated, may hold values from -3.5 to 3.5
- basis_in: float32 [17, 64], replicated, may hold values from -4 to 4
- basis_bias: float32 [64], replicated, may hold values from -3.140625 to 3.140625
- basis_mid: float32 [64, 64], replicated, may hold values from -1.5 to 1.5
- basis_shift: float32 [64], replicated, may hold values from -3.140625 to 3.140625
- response_out: float32 [2, 64, 1536], P(None, None, 'fsdp'), may hold values from -0.0234375 to 0.0234375
- skip_gain: float32 [1536], P('fsdp'), may hold values from -4 to 4
- block_counts: int32 [16, 4], P(('groups', 'fsdp'), 'seq'), parts along dimension 0, may hold values from 1 to 128, as said below
Outputs:
- mixed: bfloat16 [16, 512, 1536], P(('groups', 'fsdp'), 'seq'), parts along dimension 0
The draws below stay inside these ranges and needn't reach their ends.
There are 2 independent parts, one for each index of `groups`. The reference program is written for one: setup_inputs(seed, part) draws one part's arguments, and reference() takes and returns one part's arrays. A program takes and returns all parts, laid end to end along the dimension named above; an argument that names none is the same for every part. Nothing has to cross between parts.
Inputs may be any that keep to these rules, and one draw needn't show every extreme that they name: `block_counts`: in every table one block holds all 128 tokens and another holds a single token.
All inputs are finite; a program needn't handle non-finite values.
Results may differ from the reference program's by a relative error of at most 0.007.
Values may be sent and summed in bfloat16 or wider, within the bound.
No kernel may reach another device: no remote copies, remote signals or barrier semaphores. Data moves between devices by JAX's collectives and lax.ppermute only.
A program may use at most 128 MiB of HBM per device.

```python
import jax
import jax.numpy as jnp
from jax import lax

D = 1536
ORDER = 64
EMB = 17
BLK = 128
SEQS = 8
LEN = 512
N_SEQ = 4


def draw_block_counts(key, part):
    key_base, key_full, key_step = jax.random.split(key, 3)
    drawn = jax.random.randint(key_base, (SEQS, N_SEQ), 1, BLK + 1)
    full_at = jax.random.randint(key_full, (SEQS, 1), 0, N_SEQ)
    single_at = (full_at + jax.random.randint(key_step, (SEQS, 1), 1, N_SEQ)) % N_SEQ
    column = jnp.arange(N_SEQ)[None, :]
    return jnp.where(column == full_at, BLK, jnp.where(column == single_at, 1, drawn)).astype(jnp.int32)


def block_scale(own_key, extent, pieces, low, top_value):
    gain, own = 1.0, jax.random.fold_in(own_key, 6)
    for position, shards_of in pieces:
        steps = jnp.exp(jax.random.uniform(jax.random.fold_in(own, position), (shards_of,), jnp.float32, low / len(pieces), top_value / len(pieces)))
        gain = gain * jnp.repeat(steps, extent[position] // shards_of).reshape([-1 if axis == position else 1 for axis in range(len(extent))])
    return gain


def noise(stream_key, dims, scale, limit, cuts=(), kind=jnp.bfloat16):
    entries = scale * jax.random.normal(stream_key, dims, jnp.float32)
    if cuts:
        entries = entries * block_scale(stream_key, dims, cuts, -0.22, 0.18)
    return jnp.clip(entries, -limit, limit).astype(kind)


def setup_inputs(seed: int = 0, part: int = 0) -> dict:
    key_list = jax.random.split(jax.random.key(seed), 11)
    own_keys = jax.random.split(jax.random.fold_in(key_list[10], part), 11)
    return {
        "tokens": noise(own_keys[0], (SEQS, LEN, D), 1.0, 6.0, ((0, 4), (1, 4))),
        "in_weight": noise(key_list[1], (D, 3 * D), D ** -0.5, 0.15625, ((1, 4),)),
        "short_weight": noise(key_list[2], (3, 3 * D), 3 ** -0.5, 3.5, (), jnp.float32),
        "basis_in": noise(key_list[3], (EMB, ORDER), 1.0, 4.0, (), jnp.float32),
        "basis_bias": jnp.clip(jax.random.uniform(key_list[4], (ORDER,), jnp.float32, -3.140625, 3.140625), -3.140625, 3.140625),
        "basis_mid": noise(key_list[5], (ORDER, ORDER), 0.3, 1.5, (), jnp.float32),
        "basis_shift": jnp.clip(jax.random.uniform(key_list[6], (ORDER,), jnp.float32, -3.140625, 3.140625), -3.140625, 3.140625),
        "response_out": noise(key_list[7], (2, ORDER, D), (2 * ORDER * LEN) ** -0.5, 0.0234375, ((2, 4),), jnp.float32),
        "skip_gain": noise(key_list[8], (D,), 1.0, 4.0, ((0, 4),), jnp.float32),
        "block_counts": draw_block_counts(jax.random.fold_in(jax.random.fold_in(key_list[10], part), 71), part),
    }


def filter_basis(lag_values, total_len, basis_in, basis_bias, basis_mid, basis_shift):
    band_count = (basis_in.shape[0] - 1) // 2
    distance = jnp.abs(lag_values).astype(jnp.int32)
    periods = (2 ** (jnp.arange(band_count, dtype=jnp.int32) + 2) + 1).astype(jnp.int32)
    angles = (2.0 * jnp.pi) * (distance[:, None] % periods[None, :]).astype(jnp.float32) / periods[None, :].astype(jnp.float32)
    linear = distance.astype(jnp.float32)[:, None] / total_len
    encoded = jnp.concatenate([linear, jnp.cos(angles), jnp.sin(angles)], axis=1)
    hidden = jnp.sin(jnp.dot(encoded, basis_in, precision=lax.Precision.HIGHEST) + basis_bias)
    return jnp.sin(jnp.dot(hidden, basis_mid, precision=lax.Precision.HIGHEST) + basis_shift)


def reference(tokens, in_weight, short_weight, basis_in, basis_bias, basis_mid, basis_shift, response_out, skip_gain, block_counts):
    places = jnp.arange(2 * LEN, dtype=jnp.int32)
    lag_values = jnp.where(places < LEN, places, places - 2 * LEN).astype(jnp.int32)
    basis_rows = filter_basis(lag_values, float(LEN), basis_in, basis_bias, basis_mid, basis_shift)
    ahead_part = jnp.dot(basis_rows, response_out[0], precision=lax.Precision.HIGHEST)
    behind_part = jnp.dot(basis_rows, response_out[1], precision=lax.Precision.HIGHEST)
    kernel = jnp.where((lag_values >= 0)[:, None], ahead_part, behind_part)
    kernel = jnp.where((places == LEN)[:, None], 0.0, kernel)
    kernel_spec = jnp.fft.rfft(kernel, axis=0)

    def one_table(pair):
        table, counts = pair
        projected = jnp.dot(table, in_weight, preferred_element_type=jnp.float32).astype(jnp.bfloat16)
        padded = jnp.pad(projected, ((1, 1), (0, 0)))
        shorted = short_weight[0] * padded[:-2] + short_weight[1] * padded[1:-1] + short_weight[2] * padded[2:]
        query_gate = shorted[:, :D]
        key_part = shorted[:, D:2 * D]
        value_part = shorted[:, 2 * D:]
        valid_mask = (jnp.arange(BLK, dtype=jnp.int32)[None, :] < counts[:, None]).reshape(LEN)
        carried = (key_part * value_part * valid_mask[:, None].astype(jnp.float32)).astype(jnp.bfloat16)
        carried_wide = carried.astype(jnp.float32)
        spectrum = jnp.fft.rfft(carried_wide, n=2 * LEN, axis=0)
        conv = jnp.fft.irfft(spectrum * kernel_spec, n=2 * LEN, axis=0)[:LEN]
        return (query_gate * (conv + skip_gain * carried_wide)).astype(jnp.bfloat16)

    return lax.map(one_table, (tokens, block_counts))
```

```python
import jax
import jax.numpy as jnp
from jax import lax
from jax.sharding import PartitionSpec as P


def padded_2(cells, sides, width):
    for axis, dim in sides:
        count = lax.axis_size(axis)
        ends = count - 1
        head = lax.slice_in_dim(cells, 0, width, axis=dim)
        tail = lax.slice_in_dim(cells, cells.shape[dim] - width, cells.shape[dim], axis=dim)
        cells = jnp.concatenate(
            [
                lax.ppermute(tail, axis, [(i, (i + 1) % count) for i in range(ends)]),
                cells,
                lax.ppermute(head, axis, [((i + 1) % count, i) for i in range(ends)]),
            ],
            axis=dim,
        )
    return cells


def filter_basis(lag_values, total_len, basis_in, basis_bias, basis_mid, basis_shift):
    band_count = (basis_in.shape[0] - 1) // 2
    distance = jnp.abs(lag_values)
    periods = (2 ** (jnp.arange(band_count, dtype=jnp.int32) + 2) + 1).astype(jnp.int32)
    angles = (
        2.0
        * jnp.pi
        * (distance[:, None] % periods[None, :]).astype(jnp.float32)
        / periods[None, :].astype(jnp.float32)
    )
    linear = distance.astype(jnp.float32)[:, None] / total_len
    encoded = jnp.concatenate([linear, jnp.cos(angles), jnp.sin(angles)], axis=1)
    hidden = jnp.sin(jnp.dot(encoded, basis_in, precision=lax.Precision.HIGHEST) + basis_bias)
    return jnp.sin(jnp.dot(hidden, basis_mid, precision=lax.Precision.HIGHEST) + basis_shift)


def forward_table(block_len):
    period = 2 * block_len
    frequency = jnp.arange(block_len, dtype=jnp.int32)[:, None]
    samples = jnp.arange(period, dtype=jnp.int32)[None, :]
    phases = 2.0 * jnp.pi / period * (frequency * samples % period).astype(jnp.float32)
    alternate = (1 - 2 * (samples % 2)).astype(jnp.float32)
    real_rows = jnp.cos(phases)
    imag_rows = jnp.where(frequency == 0, alternate, -jnp.sin(phases))
    return jnp.concatenate([real_rows, imag_rows], axis=0)


def inverse_table(block_len):
    period = 2 * block_len
    places = jnp.arange(block_len, dtype=jnp.int32)[:, None]
    frequency = jnp.arange(block_len, dtype=jnp.int32)[None, :]
    phases = 2.0 * jnp.pi / period * (places * frequency % period).astype(jnp.float32)
    alternate = (1 - 2 * (places % 2)).astype(jnp.float32)
    real_cols = jnp.where(frequency == 0, 1.0, 2.0 * jnp.cos(phases)) / period
    imag_cols = jnp.where(frequency == 0, alternate, -2.0 * jnp.sin(phases)) / period
    return jnp.concatenate([real_cols, imag_cols], axis=1)


def packed_product(response, signal, block_len):
    first_slot = (jnp.arange(block_len) == 0)[:, None]
    resp_real = response[..., :block_len, :]
    resp_imag = response[..., block_len:, :]
    sig_real = signal[..., :block_len, :]
    sig_imag = signal[..., block_len:, :]
    cross_term = resp_imag * sig_imag
    prod_real = resp_real * sig_real - jnp.where(first_slot, 0.0, cross_term)
    prod_imag = jnp.where(first_slot, cross_term, resp_real * sig_imag + resp_imag * sig_real)
    return jnp.concatenate([prod_real, prod_imag], axis=-2)


def shards(
    tokens,
    in_weight,
    short_weight,
    basis_in,
    basis_bias,
    basis_mid,
    basis_shift,
    response_out,
    skip_gain,
    block_counts,
):
    seq_dev, block_len, width = tokens.shape
    group_tokens = lax.all_gather(tokens, "fsdp", axis=0, tiled=True)
    group_rows = group_tokens.shape[0]
    local_cols = in_weight.shape[1]
    partial = jnp.dot(
        group_tokens.reshape(group_rows * block_len, width),
        in_weight,
        preferred_element_type=jnp.float32,
    ).astype(jnp.bfloat16)
    partial = partial.reshape(group_rows, block_len, local_cols)
    projected = lax.all_to_all(partial, "fsdp", 0, 2, tiled=True)
    padded = padded_2(projected, (("seq", 1),), 1)
    shorted = (
        short_weight[0] * padded[:, :-2]
        + short_weight[1] * padded[:, 1:-1]
        + short_weight[2] * padded[:, 2:]
    )
    query_gate = shorted[:, :, :width]
    key_part = shorted[:, :, width : 2 * width]
    value_part = shorted[:, :, 2 * width :]
    valid_mask = (jnp.arange(block_len, dtype=jnp.int32)[None, :] < block_counts).astype(
        jnp.float32
    )
    carried = (key_part * value_part * valid_mask[:, :, None]).astype(jnp.bfloat16)
    full_out, full_skip = (
        lax.all_gather(response_out, "fsdp", axis=2, tiled=True),
        lax.all_gather(skip_gain, "fsdp", axis=0, tiled=True),
    )
    stacked_out = full_out.reshape(2 * full_out.shape[1], width)
    seq_count = lax.axis_size("seq")
    position = lax.axis_index("seq")
    total_len = float(seq_count * block_len)
    forward = forward_table(block_len)
    forward_half = forward[:, :block_len]
    inverse = inverse_table(block_len)
    circular = jnp.arange(2 * block_len, dtype=jnp.int32)
    wrapped = jnp.where(circular < block_len, circular, circular - 2 * block_len)

    def kernel_response(offset, out_cols):
        lag_values = offset + wrapped
        basis_rows = filter_basis(
            lag_values, total_len, basis_in, basis_bias, basis_mid, basis_shift
        )
        ahead_mask = (lag_values >= 0).astype(jnp.float32)[:, None]
        paired = jnp.concatenate([basis_rows * ahead_mask, basis_rows * (1.0 - ahead_mask)], axis=1)
        return jnp.dot(
            jnp.dot(forward, paired, precision=lax.Precision.HIGHEST),
            out_cols,
            precision=lax.Precision.HIGHEST,
        )

    def add_block(spectrum, block_rows, start):
        offset = position * block_len - start
        response = kernel_response(offset, stacked_out)
        signal = jnp.einsum(
            "fc,scd->sfd",
            forward_half,
            block_rows.astype(jnp.float32),
            precision=lax.Precision.HIGHEST,
        )
        return spectrum + packed_product(response[None], signal, block_len)

    initial = jnp.zeros((seq_dev, 2 * block_len, width), jnp.float32)
    piece = lax.all_gather(carried, "seq", axis=1, tiled=True)
    piece_rows = piece.shape[1]
    block_total = piece_rows // block_len

    def one_block(block_index, carry):
        block_rows = lax.dynamic_slice_in_dim(piece, block_index * block_len, block_len, 1)
        return add_block(carry, block_rows, block_index * block_len)

    spectrum = lax.fori_loop(0, block_total, one_block, initial)
    conv = jnp.einsum("if,sfd->sid", inverse, spectrum, precision=lax.Precision.HIGHEST)
    return (query_gate * (conv + full_skip * carried.astype(jnp.float32))).astype(jnp.bfloat16)


def solution(mesh):
    placed = (
        P(("groups", "fsdp"), "seq", None),
        P(None, "fsdp"),
        P(),
        P(),
        P(),
        P(),
        P(),
        P(None, None, "fsdp"),
        P("fsdp"),
        P(("groups", "fsdp"), "seq"),
    )
    return jax.shard_map(
        shards,
        mesh=mesh,
        in_specs=placed,
        out_specs=P(("groups", "fsdp"), "seq", None),
        check_vma=False,
    )
```

```python
import jax
import jax.numpy as jnp
from jax import lax
from jax.sharding import PartitionSpec as P


def padded_2(cells, sides, width):
    for axis, dim in sides:
        count = lax.axis_size(axis)
        ends = count - 1
        head = lax.slice_in_dim(cells, 0, width, axis=dim)
        tail = lax.slice_in_dim(cells, cells.shape[dim] - width, cells.shape[dim], axis=dim)
        cells = jnp.concatenate(
            [
                lax.ppermute(tail, axis, [(i, (i + 1) % count) for i in range(ends)]),
                cells,
                lax.ppermute(head, axis, [((i + 1) % count, i) for i in range(ends)]),
            ],
            axis=dim,
        )
    return cells


def filter_basis(lag_values, total_len, basis_in, basis_bias, basis_mid, basis_shift):
    band_count = (basis_in.shape[0] - 1) // 2
    distance = jnp.abs(lag_values)
    periods = (2 ** (jnp.arange(band_count, dtype=jnp.int32) + 2) + 1).astype(jnp.int32)
    angles = (
        2.0
        * jnp.pi
        * (distance[:, None] % periods[None, :]).astype(jnp.float32)
        / periods[None, :].astype(jnp.float32)
    )
    linear = distance.astype(jnp.float32)[:, None] / total_len
    encoded = jnp.concatenate([linear, jnp.cos(angles), jnp.sin(angles)], axis=1)
    hidden = jnp.sin(jnp.dot(encoded, basis_in, precision=lax.Precision.HIGHEST) + basis_bias)
    return jnp.sin(jnp.dot(hidden, basis_mid, precision=lax.Precision.HIGHEST) + basis_shift)


def forward_table(block_len):
    period = 2 * block_len
    frequency = jnp.arange(block_len, dtype=jnp.int32)[:, None]
    samples = jnp.arange(period, dtype=jnp.int32)[None, :]
    phases = 2.0 * jnp.pi / period * (frequency * samples % period).astype(jnp.float32)
    alternate = (1 - 2 * (samples % 2)).astype(jnp.float32)
    real_rows = jnp.cos(phases)
    imag_rows = jnp.where(frequency == 0, alternate, -jnp.sin(phases))
    return jnp.concatenate([real_rows, imag_rows], axis=0)


def inverse_table(block_len):
    period = 2 * block_len
    places = jnp.arange(block_len, dtype=jnp.int32)[:, None]
    frequency = jnp.arange(block_len, dtype=jnp.int32)[None, :]
    phases = 2.0 * jnp.pi / period * (places * frequency % period).astype(jnp.float32)
    alternate = (1 - 2 * (places % 2)).astype(jnp.float32)
    real_cols = jnp.where(frequency == 0, 1.0, 2.0 * jnp.cos(phases)) / period
    imag_cols = jnp.where(frequency == 0, alternate, -2.0 * jnp.sin(phases)) / period
    return jnp.concatenate([real_cols, imag_cols], axis=1)


def packed_product(response, signal, block_len):
    first_slot = (jnp.arange(block_len) == 0)[:, None]
    resp_real = response[..., :block_len, :]
    resp_imag = response[..., block_len:, :]
    sig_real = signal[..., :block_len, :]
    sig_imag = signal[..., block_len:, :]
    cross_term = resp_imag * sig_imag
    prod_real = resp_real * sig_real - jnp.where(first_slot, 0.0, cross_term)
    prod_imag = jnp.where(first_slot, cross_term, resp_real * sig_imag + resp_imag * sig_real)
    return jnp.concatenate([prod_real, prod_imag], axis=-2)


def shards(
    tokens,
    in_weight,
    short_weight,
    basis_in,
    basis_bias,
    basis_mid,
    basis_shift,
    response_out,
    skip_gain,
    block_counts,
):
    seq_dev, block_len, width = tokens.shape
    group_tokens = lax.all_gather(tokens, "fsdp", axis=0, tiled=True)
    group_rows = group_tokens.shape[0]
    local_cols = in_weight.shape[1]
    partial = jnp.dot(
        group_tokens.reshape(group_rows * block_len, width),
        in_weight,
        preferred_element_type=jnp.float32,
    ).astype(jnp.bfloat16)
    partial = partial.reshape(group_rows, block_len, local_cols)
    projected = lax.all_to_all(partial, "fsdp", 0, 2, tiled=True)
    padded = padded_2(projected, (("seq", 1),), 1)
    shorted = (
        short_weight[0] * padded[:, :-2]
        + short_weight[1] * padded[:, 1:-1]
        + short_weight[2] * padded[:, 2:]
    )
    query_gate = shorted[:, :, :width]
    key_part = shorted[:, :, width : 2 * width]
    value_part = shorted[:, :, 2 * width :]
    valid_mask = (jnp.arange(block_len, dtype=jnp.int32)[None, :] < block_counts).astype(
        jnp.float32
    )
    carried = (key_part * value_part * valid_mask[:, :, None]).astype(jnp.bfloat16)
    local_ch = skip_gain.shape[0]
    params = jnp.concatenate(
        [response_out.reshape(2 * response_out.shape[1], local_ch), skip_gain[None, :]], axis=0
    )
    gathered = lax.all_gather(params, "fsdp", axis=0, tiled=False)
    gathered = jnp.transpose(gathered, (1, 0, 2)).reshape(params.shape[0], width)
    stacked_out = gathered[:-1]
    full_skip = gathered[-1]
    seq_count = lax.axis_size("seq")
    position = lax.axis_index("seq")
    total_len = float(seq_count * block_len)
    forward = forward_table(block_len)
    forward_half = forward[:, :block_len]
    half_hi = forward_half.astype(jnp.bfloat16)
    half_lo = (forward_half - half_hi.astype(jnp.float32)).astype(jnp.bfloat16)
    inverse = inverse_table(block_len)
    circular = jnp.arange(2 * block_len, dtype=jnp.int32)
    wrapped = jnp.where(circular < block_len, circular, circular - 2 * block_len)

    piece = lax.all_gather(carried, "seq", axis=1, tiled=True)
    block_total = piece.shape[1] // block_len

    chunk = min(block_total, 4)

    def chunk_spectrum(first, rows):
        offsets = (position - first - jnp.arange(chunk, dtype=jnp.int32)) * block_len
        lag_values = (offsets[:, None] + wrapped[None, :]).reshape(-1)
        basis_rows = filter_basis(
            lag_values, total_len, basis_in, basis_bias, basis_mid, basis_shift
        )
        ahead_mask = (lag_values >= 0).astype(jnp.float32)[:, None]
        paired = jnp.concatenate(
            [basis_rows * ahead_mask, basis_rows * (1.0 - ahead_mask)], axis=1
        )
        paired = paired.reshape(chunk, 2 * block_len, paired.shape[-1])
        paired_spec = jnp.einsum("gf,bfk->bgk", forward, paired, precision=lax.Precision.HIGHEST)
        response = jnp.einsum("bgk,kd->bgd", paired_spec, stacked_out, precision=lax.Precision.HIGH)
        blocks = rows.reshape(seq_dev, chunk, block_len, width)
        signal = jnp.einsum(
            "fc,sbcd->sbfd", half_hi, blocks, preferred_element_type=jnp.float32
        ) + jnp.einsum("fc,sbcd->sbfd", half_lo, blocks, preferred_element_type=jnp.float32)
        total = packed_product(response[None, 0], signal[:, 0], block_len)
        for index in range(1, chunk):
            total = total + packed_product(response[None, index], signal[:, index], block_len)
        return total

    if chunk == block_total:
        spectrum = chunk_spectrum(0, piece)
    else:

        def one_chunk(chunk_index, carry):
            rows = lax.dynamic_slice_in_dim(piece, chunk_index * chunk * block_len, chunk * block_len, 1)
            return carry + chunk_spectrum(chunk_index * chunk, rows)

        spectrum = lax.fori_loop(
            0,
            block_total // chunk,
            one_chunk,
            jnp.zeros((seq_dev, 2 * block_len, width), jnp.float32),
        )
    conv = jnp.einsum("if,sfd->sid", inverse, spectrum, precision=lax.Precision.HIGH)
    return (query_gate * (conv + full_skip * carried.astype(jnp.float32))).astype(jnp.bfloat16)


def solution(mesh):
    placed = (
        P(("groups", "fsdp"), "seq", None),
        P(None, "fsdp"),
        P(),
        P(),
        P(),
        P(),
        P(),
        P(None, None, "fsdp"),
        P("fsdp"),
        P(("groups", "fsdp"), "seq"),
    )
    return jax.shard_map(
        shards,
        mesh=mesh,
        in_specs=placed,
        out_specs=P(("groups", "fsdp"), "seq", None),
        check_vma=False,
    )
```

```python
import jax
import jax.numpy as jnp
from jax import lax
from jax.sharding import PartitionSpec as P


def padded_2(cells, sides, width):
    for axis, dim in sides:
        count = lax.axis_size(axis)
        ends = count - 1
        head = lax.slice_in_dim(cells, 0, width, axis=dim)
        tail = lax.slice_in_dim(cells, cells.shape[dim] - width, cells.shape[dim], axis=dim)
        cells = jnp.concatenate(
            [
                lax.ppermute(tail, axis, [(i, (i + 1) % count) for i in range(ends)]),
                cells,
                lax.ppermute(head, axis, [((i + 1) % count, i) for i in range(ends)]),
            ],
            axis=dim,
        )
    return cells


def filter_basis(lag_values, total_len, basis_in, basis_bias, basis_mid, basis_shift):
    band_count = (basis_in.shape[0] - 1) // 2
    distance = jnp.abs(lag_values)
    periods = (2 ** (jnp.arange(band_count, dtype=jnp.int32) + 2) + 1).astype(jnp.int32)
    angles = (
        2.0
        * jnp.pi
        * (distance[:, None] % periods[None, :]).astype(jnp.float32)
        / periods[None, :].astype(jnp.float32)
    )
    linear = distance.astype(jnp.float32)[:, None] / total_len
    encoded = jnp.concatenate([linear, jnp.cos(angles), jnp.sin(angles)], axis=1)
    hidden = jnp.sin(jnp.dot(encoded, basis_in, precision=lax.Precision.HIGHEST) + basis_bias)
    return jnp.sin(jnp.dot(hidden, basis_mid, precision=lax.Precision.HIGHEST) + basis_shift)


def forward_table(block_len):
    period = 2 * block_len
    frequency = jnp.arange(block_len, dtype=jnp.int32)[:, None]
    samples = jnp.arange(period, dtype=jnp.int32)[None, :]
    phases = 2.0 * jnp.pi / period * (frequency * samples % period).astype(jnp.float32)
    alternate = (1 - 2 * (samples % 2)).astype(jnp.float32)
    real_rows = jnp.cos(phases)
    imag_rows = jnp.where(frequency == 0, alternate, -jnp.sin(phases))
    return jnp.concatenate([real_rows, imag_rows], axis=0)


def inverse_table(block_len):
    period = 2 * block_len
    places = jnp.arange(block_len, dtype=jnp.int32)[:, None]
    frequency = jnp.arange(block_len, dtype=jnp.int32)[None, :]
    phases = 2.0 * jnp.pi / period * (places * frequency % period).astype(jnp.float32)
    alternate = (1 - 2 * (places % 2)).astype(jnp.float32)
    real_cols = jnp.where(frequency == 0, 1.0, 2.0 * jnp.cos(phases)) / period
    imag_cols = jnp.where(frequency == 0, alternate, -2.0 * jnp.sin(phases)) / period
    return jnp.concatenate([real_cols, imag_cols], axis=1)


def packed_product(response, signal, block_len):
    first_slot = (jnp.arange(block_len) == 0)[:, None]
    resp_real = response[..., :block_len, :]
    resp_imag = response[..., block_len:, :]
    sig_real = signal[..., :block_len, :]
    sig_imag = signal[..., block_len:, :]
    cross_term = resp_imag * sig_imag
    prod_real = resp_real * sig_real - jnp.where(first_slot, 0.0, cross_term)
    prod_imag = jnp.where(first_slot, cross_term, resp_real * sig_imag + resp_imag * sig_real)
    return jnp.concatenate([prod_real, prod_imag], axis=-2)


def shards(
    tokens,
    in_weight,
    short_weight,
    basis_in,
    basis_bias,
    basis_mid,
    basis_shift,
    response_out,
    skip_gain,
    block_counts,
):
    seq_dev, block_len, width = tokens.shape
    local_ch = skip_gain.shape[0]
    params = jnp.concatenate(
        [response_out.reshape(2 * response_out.shape[1], local_ch), skip_gain[None, :]], axis=0
    )
    gathered = lax.all_gather(params, "fsdp", axis=0, tiled=False)
    gathered = jnp.transpose(gathered, (1, 0, 2)).reshape(params.shape[0], width)
    stacked_out = gathered[:-1]
    full_skip = gathered[-1]
    seq_count = lax.axis_size("seq")
    position = lax.axis_index("seq")
    total_len = float(seq_count * block_len)
    forward = forward_table(block_len)
    forward_half = forward[:, :block_len]
    half_hi = forward_half.astype(jnp.bfloat16)
    half_lo = (forward_half - half_hi.astype(jnp.float32)).astype(jnp.bfloat16)
    inverse = inverse_table(block_len)
    circular = jnp.arange(2 * block_len, dtype=jnp.int32)
    wrapped = jnp.where(circular < block_len, circular, circular - 2 * block_len)

    block_total = seq_count
    chunk = min(block_total, 4)

    def chunk_response(first):
        offsets = (position - first - jnp.arange(chunk, dtype=jnp.int32)) * block_len
        lag_values = (offsets[:, None] + wrapped[None, :]).reshape(-1)
        basis_rows = filter_basis(
            lag_values, total_len, basis_in, basis_bias, basis_mid, basis_shift
        )
        ahead_mask = (lag_values >= 0).astype(jnp.float32)[:, None]
        paired = jnp.concatenate(
            [basis_rows * ahead_mask, basis_rows * (1.0 - ahead_mask)], axis=1
        )
        paired = paired.reshape(chunk, 2 * block_len, paired.shape[-1])
        paired_spec = jnp.einsum("gf,bfk->bgk", forward, paired, precision=lax.Precision.HIGHEST)
        return jnp.einsum("bgk,kd->bgd", paired_spec, stacked_out, precision=lax.Precision.HIGH)

    def chunk_apply(response, rows):
        blocks = rows.reshape(seq_dev, chunk, block_len, width)
        signal = jnp.einsum(
            "fc,sbcd->sbfd", half_hi, blocks, preferred_element_type=jnp.float32
        ) + jnp.einsum("fc,sbcd->sbfd", half_lo, blocks, preferred_element_type=jnp.float32)
        total = packed_product(response[None, 0], signal[:, 0], block_len)
        for index in range(1, chunk):
            total = total + packed_product(response[None, index], signal[:, index], block_len)
        return total

    group_tokens = lax.all_gather(tokens, "fsdp", axis=0, tiled=True)
    single = chunk == block_total
    if single:
        early_response = chunk_response(0)
        group_tokens, early_response, full_skip = lax.optimization_barrier(
            (group_tokens, early_response, full_skip)
        )
    group_rows = group_tokens.shape[0]
    local_cols = in_weight.shape[1]
    partial = jnp.dot(
        group_tokens.reshape(group_rows * block_len, width),
        in_weight,
        preferred_element_type=jnp.float32,
    ).astype(jnp.bfloat16)
    partial = partial.reshape(group_rows, block_len, local_cols)
    projected = lax.all_to_all(partial, "fsdp", 0, 2, tiled=True)
    padded = padded_2(projected, (("seq", 1),), 1)
    shorted = (
        short_weight[0] * padded[:, :-2]
        + short_weight[1] * padded[:, 1:-1]
        + short_weight[2] * padded[:, 2:]
    )
    query_gate = shorted[:, :, :width]
    key_part = shorted[:, :, width : 2 * width]
    value_part = shorted[:, :, 2 * width :]
    valid_mask = (jnp.arange(block_len, dtype=jnp.int32)[None, :] < block_counts).astype(
        jnp.float32
    )
    carried = (key_part * value_part * valid_mask[:, :, None]).astype(jnp.bfloat16)
    piece = lax.all_gather(carried, "seq", axis=1, tiled=True)

    if single:
        spectrum = chunk_apply(early_response, piece)
    else:

        def one_chunk(chunk_index, carry):
            rows = lax.dynamic_slice_in_dim(piece, chunk_index * chunk * block_len, chunk * block_len, 1)
            return carry + chunk_apply(chunk_response(chunk_index * chunk), rows)

        spectrum = lax.fori_loop(
            0,
            block_total // chunk,
            one_chunk,
            jnp.zeros((seq_dev, 2 * block_len, width), jnp.float32),
        )
    conv = jnp.einsum("if,sfd->sid", inverse, spectrum, precision=lax.Precision.HIGH)
    return (query_gate * (conv + full_skip * carried.astype(jnp.float32))).astype(jnp.bfloat16)


def solution(mesh):
    placed = (
        P(("groups", "fsdp"), "seq", None),
        P(None, "fsdp"),
        P(),
        P(),
        P(),
        P(),
        P(),
        P(None, None, "fsdp"),
        P("fsdp"),
        P(("groups", "fsdp"), "seq"),
    )
    return jax.shard_map(
        shards,
        mesh=mesh,
        in_specs=placed,
        out_specs=P(("groups", "fsdp"), "seq", None),
        check_vma=False,
    )
```

```python
import jax
import jax.numpy as jnp
from jax import lax
from jax.sharding import PartitionSpec as P


def padded_2(cells, sides, width):
    for axis, dim in sides:
        count = lax.axis_size(axis)
        ends = count - 1
        head = lax.slice_in_dim(cells, 0, width, axis=dim)
        tail = lax.slice_in_dim(cells, cells.shape[dim] - width, cells.shape[dim], axis=dim)
        cells = jnp.concatenate(
            [
                lax.ppermute(tail, axis, [(i, (i + 1) % count) for i in range(ends)]),
                cells,
                lax.ppermute(head, axis, [((i + 1) % count, i) for i in range(ends)]),
            ],
            axis=dim,
        )
    return cells


def filter_basis(lag_values, total_len, basis_in, basis_bias, basis_mid, basis_shift):
    band_count = (basis_in.shape[0] - 1) // 2
    distance = jnp.abs(lag_values)
    periods = (2 ** (jnp.arange(band_count, dtype=jnp.int32) + 2) + 1).astype(jnp.int32)
    angles = (
        2.0
        * jnp.pi
        * (distance[:, None] % periods[None, :]).astype(jnp.float32)
        / periods[None, :].astype(jnp.float32)
    )
    linear = distance.astype(jnp.float32)[:, None] / total_len
    encoded = jnp.concatenate([linear, jnp.cos(angles), jnp.sin(angles)], axis=1)
    hidden = jnp.sin(jnp.dot(encoded, basis_in, precision=lax.Precision.HIGHEST) + basis_bias)
    return jnp.sin(jnp.dot(hidden, basis_mid, precision=lax.Precision.HIGHEST) + basis_shift)


def forward_table(block_len):
    period = 2 * block_len
    frequency = jnp.arange(block_len, dtype=jnp.int32)[:, None]
    samples = jnp.arange(period, dtype=jnp.int32)[None, :]
    phases = 2.0 * jnp.pi / period * (frequency * samples % period).astype(jnp.float32)
    alternate = (1 - 2 * (samples % 2)).astype(jnp.float32)
    real_rows = jnp.cos(phases)
    imag_rows = jnp.where(frequency == 0, alternate, -jnp.sin(phases))
    return jnp.concatenate([real_rows, imag_rows], axis=0)


def inverse_table(block_len):
    period = 2 * block_len
    places = jnp.arange(block_len, dtype=jnp.int32)[:, None]
    frequency = jnp.arange(block_len, dtype=jnp.int32)[None, :]
    phases = 2.0 * jnp.pi / period * (places * frequency % period).astype(jnp.float32)
    alternate = (1 - 2 * (places % 2)).astype(jnp.float32)
    real_cols = jnp.where(frequency == 0, 1.0, 2.0 * jnp.cos(phases)) / period
    imag_cols = jnp.where(frequency == 0, alternate, -2.0 * jnp.sin(phases)) / period
    return jnp.concatenate([real_cols, imag_cols], axis=1)


def packed_product(response, signal, block_len):
    first_slot = (jnp.arange(block_len) == 0)[:, None]
    resp_real = response[..., :block_len, :]
    resp_imag = response[..., block_len:, :]
    sig_real = signal[..., :block_len, :]
    sig_imag = signal[..., block_len:, :]
    cross_term = resp_imag * sig_imag
    prod_real = resp_real * sig_real - jnp.where(first_slot, 0.0, cross_term)
    prod_imag = jnp.where(first_slot, cross_term, resp_real * sig_imag + resp_imag * sig_real)
    return jnp.concatenate([prod_real, prod_imag], axis=-2)


def shards(
    tokens,
    in_weight,
    short_weight,
    basis_in,
    basis_bias,
    basis_mid,
    basis_shift,
    response_out,
    skip_gain,
    block_counts,
):
    seq_dev, block_len, width = tokens.shape
    local_ch = skip_gain.shape[0]
    params = jnp.concatenate(
        [response_out.reshape(2 * response_out.shape[1], local_ch), skip_gain[None, :]], axis=0
    )
    gathered = lax.all_gather(params, "fsdp", axis=0, tiled=False)
    gathered = jnp.transpose(gathered, (1, 0, 2)).reshape(params.shape[0], width)
    stacked_out = gathered[:-1]
    full_skip = gathered[-1]
    seq_count = lax.axis_size("seq")
    position = lax.axis_index("seq")
    total_len = float(seq_count * block_len)
    forward = forward_table(block_len)
    forward_half = forward[:, :block_len]
    half_hi = forward_half.astype(jnp.bfloat16)
    half_lo = (forward_half - half_hi.astype(jnp.float32)).astype(jnp.bfloat16)
    inverse = inverse_table(block_len)
    circular = jnp.arange(2 * block_len, dtype=jnp.int32)
    wrapped = jnp.where(circular < block_len, circular, circular - 2 * block_len)

    block_total = seq_count
    chunk = min(block_total, 4)

    def chunk_response(first):
        offsets = (position - first - jnp.arange(chunk, dtype=jnp.int32)) * block_len
        lag_values = (offsets[:, None] + wrapped[None, :]).reshape(-1)
        basis_rows = filter_basis(
            lag_values, total_len, basis_in, basis_bias, basis_mid, basis_shift
        )
        ahead_mask = (lag_values >= 0).astype(jnp.float32)[:, None]
        paired = jnp.concatenate(
            [basis_rows * ahead_mask, basis_rows * (1.0 - ahead_mask)], axis=1
        )
        paired = paired.reshape(chunk, 2 * block_len, paired.shape[-1])
        paired_spec = jnp.einsum("gf,bfk->bgk", forward, paired, precision=lax.Precision.HIGHEST)
        return jnp.einsum("bgk,kd->bgd", paired_spec, stacked_out, precision=lax.Precision.HIGH)

    def chunk_apply(response, rows):
        blocks = rows.reshape(rows.shape[0], chunk, block_len, width)
        signal = jnp.einsum(
            "fc,sbcd->sbfd", half_hi, blocks, preferred_element_type=jnp.float32
        ) + jnp.einsum("fc,sbcd->sbfd", half_lo, blocks, preferred_element_type=jnp.float32)
        total = packed_product(response[None, 0], signal[:, 0], block_len)
        for index in range(1, chunk):
            total = total + packed_product(response[None, index], signal[:, index], block_len)
        return total

    single = chunk == block_total
    if single:
        early_response = chunk_response(0)
    local_cols = in_weight.shape[1]
    outputs = []
    for table in range(seq_dev):
        table_tokens = lax.all_gather(tokens[table : table + 1], "fsdp", axis=0, tiled=True)
        if single and table == 0:
            table_tokens, early_response, full_skip = lax.optimization_barrier(
                (table_tokens, early_response, full_skip)
            )
        group_rows = table_tokens.shape[0]
        partial = jnp.dot(
            table_tokens.reshape(group_rows * block_len, width),
            in_weight,
            preferred_element_type=jnp.float32,
        ).astype(jnp.bfloat16)
        partial = partial.reshape(group_rows, block_len, local_cols)
        projected = lax.all_to_all(partial, "fsdp", 0, 2, tiled=True)
        padded = padded_2(projected, (("seq", 1),), 1)
        shorted = (
            short_weight[0] * padded[:, :-2]
            + short_weight[1] * padded[:, 1:-1]
            + short_weight[2] * padded[:, 2:]
        )
        query_gate = shorted[:, :, :width]
        key_part = shorted[:, :, width : 2 * width]
        value_part = shorted[:, :, 2 * width :]
        valid_mask = (
            jnp.arange(block_len, dtype=jnp.int32)[None, :] < block_counts[table : table + 1]
        ).astype(jnp.float32)
        carried = (key_part * value_part * valid_mask[:, :, None]).astype(jnp.bfloat16)
        piece = lax.all_gather(carried, "seq", axis=1, tiled=True)
        rows_dev = carried.shape[0]

        if single:
            spectrum = chunk_apply(early_response, piece)
        else:

            def one_chunk(chunk_index, carry):
                rows = lax.dynamic_slice_in_dim(
                    piece, chunk_index * chunk * block_len, chunk * block_len, 1
                )
                return carry + chunk_apply(chunk_response(chunk_index * chunk), rows)

            spectrum = lax.fori_loop(
                0,
                block_total // chunk,
                one_chunk,
                jnp.zeros((rows_dev, 2 * block_len, width), jnp.float32),
            )
        conv = jnp.einsum("if,sfd->sid", inverse, spectrum, precision=lax.Precision.HIGH)
        outputs.append(
            (query_gate * (conv + full_skip * carried.astype(jnp.float32))).astype(jnp.bfloat16)
        )
    return jnp.concatenate(outputs, axis=0)


def solution(mesh):
    placed = (
        P(("groups", "fsdp"), "seq", None),
        P(None, "fsdp"),
        P(),
        P(),
        P(),
        P(),
        P(),
        P(None, None, "fsdp"),
        P("fsdp"),
        P(("groups", "fsdp"), "seq"),
    )
    return jax.shard_map(
        shards,
        mesh=mesh,
        in_specs=placed,
        out_specs=P(("groups", "fsdp"), "seq", None),
        check_vma=False,
    )
```

```python
import jax
import jax.numpy as jnp
from jax import lax
from jax.sharding import PartitionSpec as P
from jax.experimental import pallas as pl
from jax.experimental.pallas import tpu as pltpu


def padded_2(cells, sides, width):
    for axis, dim in sides:
        count = lax.axis_size(axis)
        ends = count - 1
        head = lax.slice_in_dim(cells, 0, width, axis=dim)
        tail = lax.slice_in_dim(cells, cells.shape[dim] - width, cells.shape[dim], axis=dim)
        cells = jnp.concatenate(
            [
                lax.ppermute(tail, axis, [(i, (i + 1) % count) for i in range(ends)]),
                cells,
                lax.ppermute(head, axis, [((i + 1) % count, i) for i in range(ends)]),
            ],
            axis=dim,
        )
    return cells


def filter_basis(lag_values, total_len, basis_in, basis_bias, basis_mid, basis_shift):
    band_count = (basis_in.shape[0] - 1) // 2
    distance = jnp.abs(lag_values)
    periods = (2 ** (jnp.arange(band_count, dtype=jnp.int32) + 2) + 1).astype(jnp.int32)
    angles = (
        2.0
        * jnp.pi
        * (distance[:, None] % periods[None, :]).astype(jnp.float32)
        / periods[None, :].astype(jnp.float32)
    )
    linear = distance.astype(jnp.float32)[:, None] / total_len
    encoded = jnp.concatenate([linear, jnp.cos(angles), jnp.sin(angles)], axis=1)
    hidden = jnp.sin(jnp.dot(encoded, basis_in, precision=lax.Precision.HIGHEST) + basis_bias)
    return jnp.sin(jnp.dot(hidden, basis_mid, precision=lax.Precision.HIGHEST) + basis_shift)


def forward_table(block_len):
    period = 2 * block_len
    frequency = jnp.arange(block_len, dtype=jnp.int32)[:, None]
    samples = jnp.arange(period, dtype=jnp.int32)[None, :]
    phases = 2.0 * jnp.pi / period * (frequency * samples % period).astype(jnp.float32)
    alternate = (1 - 2 * (samples % 2)).astype(jnp.float32)
    real_rows = jnp.cos(phases)
    imag_rows = jnp.where(frequency == 0, alternate, -jnp.sin(phases))
    return jnp.concatenate([real_rows, imag_rows], axis=0)


def inverse_table(block_len):
    period = 2 * block_len
    places = jnp.arange(block_len, dtype=jnp.int32)[:, None]
    frequency = jnp.arange(block_len, dtype=jnp.int32)[None, :]
    phases = 2.0 * jnp.pi / period * (places * frequency % period).astype(jnp.float32)
    alternate = (1 - 2 * (places % 2)).astype(jnp.float32)
    real_cols = jnp.where(frequency == 0, 1.0, 2.0 * jnp.cos(phases)) / period
    imag_cols = jnp.where(frequency == 0, alternate, -2.0 * jnp.sin(phases)) / period
    return jnp.concatenate([real_cols, imag_cols], axis=1)


def packed_product(response, signal, block_len):
    first_slot = (jnp.arange(block_len) == 0)[:, None]
    resp_real = response[..., :block_len, :]
    resp_imag = response[..., block_len:, :]
    sig_real = signal[..., :block_len, :]
    sig_imag = signal[..., block_len:, :]
    cross_term = resp_imag * sig_imag
    prod_real = resp_real * sig_real - jnp.where(first_slot, 0.0, cross_term)
    prod_imag = jnp.where(first_slot, cross_term, resp_real * sig_imag + resp_imag * sig_real)
    return jnp.concatenate([prod_real, prod_imag], axis=-2)


def split_bf16(values):
    high = values.astype(jnp.bfloat16)
    return high, (values - high.astype(jnp.float32)).astype(jnp.bfloat16)


def conv_kernel(
    piece_ref, resp_ref, query_ref, carried_ref, skip_ref,
    fwd_hi_ref, fwd_lo_ref, inv_hi_ref, inv_lo_ref, out_ref,
):
    tables, rows, lanes = carried_ref.shape
    block_total = resp_ref.shape[0]
    first = lax.broadcasted_iota(jnp.int32, (rows, lanes), 0) == 0
    fwd_hi = fwd_hi_ref[...]
    fwd_lo = fwd_lo_ref[...]

    def dot(a, b):
        return jnp.dot(a, b, preferred_element_type=jnp.float32)

    for table in range(tables):

        def one_block(block, acc):
            acc_real, acc_imag = acc
            block_rows = piece_ref[table, pl.ds(pl.multiple_of(block * rows, rows), rows), :]
            signal = dot(fwd_hi, block_rows) + dot(fwd_lo, block_rows)
            response = resp_ref[block]
            resp_real = response[:rows]
            resp_imag = response[rows:]
            sig_real = signal[:rows]
            sig_imag = signal[rows:]
            cross = resp_imag * sig_imag
            acc_real = acc_real + (resp_real * sig_real - jnp.where(first, 0.0, cross))
            acc_imag = acc_imag + jnp.where(first, cross, resp_real * sig_imag + resp_imag * sig_real)
            return acc_real, acc_imag

        zeros = jnp.zeros((rows, lanes), jnp.float32)
        acc_real, acc_imag = lax.fori_loop(0, block_total, one_block, (zeros, zeros))
        spectrum = jnp.concatenate([acc_real, acc_imag], axis=0)
        spec_hi, spec_lo = split_bf16(spectrum)
        inv_hi = inv_hi_ref[...]
        conv = dot(inv_hi, spec_hi) + dot(inv_hi, spec_lo) + dot(inv_lo_ref[...], spec_hi)
        gated = query_ref[table] * (conv + skip_ref[...] * carried_ref[table].astype(jnp.float32))
        out_ref[table] = gated.astype(out_ref.dtype)


def fused_conv(piece, response, query_gate, carried, skip, fwd_half, inverse):
    tables, rows, width = carried.shape
    block_total = response.shape[0]
    lanes = 256 if width % 256 == 0 else width
    fwd_hi, fwd_lo = split_bf16(fwd_half)
    inv_hi, inv_lo = split_bf16(inverse)
    tile3 = lambda i: (0, 0, i)
    whole2 = lambda i: (0, 0)
    return pl.pallas_call(
        conv_kernel,
        grid=(width // lanes,),
        in_specs=[
            pl.BlockSpec((tables, piece.shape[1], lanes), tile3),
            pl.BlockSpec((block_total, 2 * rows, lanes), tile3),
            pl.BlockSpec((tables, rows, lanes), tile3),
            pl.BlockSpec((tables, rows, lanes), tile3),
            pl.BlockSpec((1, lanes), lambda i: (0, i)),
            pl.BlockSpec(fwd_hi.shape, whole2),
            pl.BlockSpec(fwd_lo.shape, whole2),
            pl.BlockSpec(inv_hi.shape, whole2),
            pl.BlockSpec(inv_lo.shape, whole2),
        ],
        out_specs=pl.BlockSpec((tables, rows, lanes), tile3),
        out_shape=jax.ShapeDtypeStruct((tables, rows, width), jnp.bfloat16),
        compiler_params=pltpu.CompilerParams(vmem_limit_bytes=48 * 1024 * 1024),
    )(piece, response, query_gate, carried, skip.reshape(1, width), fwd_hi, fwd_lo, inv_hi, inv_lo)


def shards(
    tokens,
    in_weight,
    short_weight,
    basis_in,
    basis_bias,
    basis_mid,
    basis_shift,
    response_out,
    skip_gain,
    block_counts,
):
    seq_dev, block_len, width = tokens.shape
    group_tokens = lax.all_gather(tokens, "fsdp", axis=0, tiled=True)
    group_rows = group_tokens.shape[0]
    local_cols = in_weight.shape[1]
    partial = jnp.dot(
        group_tokens.reshape(group_rows * block_len, width),
        in_weight,
        preferred_element_type=jnp.float32,
    ).astype(jnp.bfloat16)
    partial = partial.reshape(group_rows, block_len, local_cols)
    projected = lax.all_to_all(partial, "fsdp", 0, 2, tiled=True)
    padded = padded_2(projected, (("seq", 1),), 1)
    shorted = (
        short_weight[0] * padded[:, :-2]
        + short_weight[1] * padded[:, 1:-1]
        + short_weight[2] * padded[:, 2:]
    )
    query_gate = shorted[:, :, :width]
    key_part = shorted[:, :, width : 2 * width]
    value_part = shorted[:, :, 2 * width :]
    valid_mask = (jnp.arange(block_len, dtype=jnp.int32)[None, :] < block_counts).astype(
        jnp.float32
    )
    carried = (key_part * value_part * valid_mask[:, :, None]).astype(jnp.bfloat16)
    local_ch = skip_gain.shape[0]
    params = jnp.concatenate(
        [response_out.reshape(2 * response_out.shape[1], local_ch), skip_gain[None, :]], axis=0
    )
    gathered = lax.all_gather(params, "fsdp", axis=0, tiled=False)
    gathered = jnp.transpose(gathered, (1, 0, 2)).reshape(params.shape[0], width)
    stacked_out = gathered[:-1]
    full_skip = gathered[-1]
    seq_count = lax.axis_size("seq")
    position = lax.axis_index("seq")
    total_len = float(seq_count * block_len)
    forward = forward_table(block_len)
    forward_half = forward[:, :block_len]
    half_hi = forward_half.astype(jnp.bfloat16)
    half_lo = (forward_half - half_hi.astype(jnp.float32)).astype(jnp.bfloat16)
    inverse = inverse_table(block_len)
    circular = jnp.arange(2 * block_len, dtype=jnp.int32)
    wrapped = jnp.where(circular < block_len, circular, circular - 2 * block_len)

    piece = lax.all_gather(carried, "seq", axis=1, tiled=True)
    block_total = piece.shape[1] // block_len

    offsets = (position - jnp.arange(block_total, dtype=jnp.int32)) * block_len
    lag_values = (offsets[:, None] + wrapped[None, :]).reshape(-1)
    basis_rows = filter_basis(lag_values, total_len, basis_in, basis_bias, basis_mid, basis_shift)
    ahead_mask = (lag_values >= 0).astype(jnp.float32)[:, None]
    paired = jnp.concatenate([basis_rows * ahead_mask, basis_rows * (1.0 - ahead_mask)], axis=1)
    paired = paired.reshape(block_total, 2 * block_len, paired.shape[-1])
    paired_spec = jnp.einsum("gf,bfk->bgk", forward, paired, precision=lax.Precision.HIGHEST)
    response = jnp.einsum("bgk,kd->bgd", paired_spec, stacked_out, precision=lax.Precision.HIGH)
    return fused_conv(piece, response, query_gate, carried, full_skip, forward_half, inverse)


def solution(mesh):
    placed = (
        P(("groups", "fsdp"), "seq", None),
        P(None, "fsdp"),
        P(),
        P(),
        P(),
        P(),
        P(),
        P(None, None, "fsdp"),
        P("fsdp"),
        P(("groups", "fsdp"), "seq"),
    )
    return jax.shard_map(
        shards,
        mesh=mesh,
        in_specs=placed,
        out_specs=P(("groups", "fsdp"), "seq", None),
        check_vma=False,
    )
```

```python
import jax
import jax.numpy as jnp
from jax import lax
from jax.sharding import PartitionSpec as P
from jax.experimental import pallas as pl
from jax.experimental.pallas import tpu as pltpu


def padded_2(cells, sides, width):
    for axis, dim in sides:
        count = lax.axis_size(axis)
        ends = count - 1
        head = lax.slice_in_dim(cells, 0, width, axis=dim)
        tail = lax.slice_in_dim(cells, cells.shape[dim] - width, cells.shape[dim], axis=dim)
        cells = jnp.concatenate(
            [
                lax.ppermute(tail, axis, [(i, (i + 1) % count) for i in range(ends)]),
                cells,
                lax.ppermute(head, axis, [((i + 1) % count, i) for i in range(ends)]),
            ],
            axis=dim,
        )
    return cells


def gather_by_permutes(values, axis):
    count = lax.axis_size(axis)
    own = lax.axis_index(axis)
    received = [values]
    for shift in range(1, count):
        received.append(
            lax.ppermute(values, axis, [(i, (i + shift) % count) for i in range(count)])
        )
    stacked = jnp.stack(received)
    sources = (own - jnp.arange(count, dtype=jnp.int32)) % count
    order = jnp.argsort(sources)
    return jnp.take(stacked, order, axis=0)


def filter_basis(lag_values, total_len, basis_in, basis_bias, basis_mid, basis_shift):
    band_count = (basis_in.shape[0] - 1) // 2
    distance = jnp.abs(lag_values)
    periods = (2 ** (jnp.arange(band_count, dtype=jnp.int32) + 2) + 1).astype(jnp.int32)
    angles = (
        2.0
        * jnp.pi
        * (distance[:, None] % periods[None, :]).astype(jnp.float32)
        / periods[None, :].astype(jnp.float32)
    )
    linear = distance.astype(jnp.float32)[:, None] / total_len
    encoded = jnp.concatenate([linear, jnp.cos(angles), jnp.sin(angles)], axis=1)
    hidden = jnp.sin(jnp.dot(encoded, basis_in, precision=lax.Precision.HIGHEST) + basis_bias)
    return jnp.sin(jnp.dot(hidden, basis_mid, precision=lax.Precision.HIGHEST) + basis_shift)


def forward_table(block_len):
    period = 2 * block_len
    frequency = jnp.arange(block_len, dtype=jnp.int32)[:, None]
    samples = jnp.arange(period, dtype=jnp.int32)[None, :]
    phases = 2.0 * jnp.pi / period * (frequency * samples % period).astype(jnp.float32)
    alternate = (1 - 2 * (samples % 2)).astype(jnp.float32)
    real_rows = jnp.cos(phases)
    imag_rows = jnp.where(frequency == 0, alternate, -jnp.sin(phases))
    return jnp.concatenate([real_rows, imag_rows], axis=0)


def inverse_table(block_len):
    period = 2 * block_len
    places = jnp.arange(block_len, dtype=jnp.int32)[:, None]
    frequency = jnp.arange(block_len, dtype=jnp.int32)[None, :]
    phases = 2.0 * jnp.pi / period * (places * frequency % period).astype(jnp.float32)
    alternate = (1 - 2 * (places % 2)).astype(jnp.float32)
    real_cols = jnp.where(frequency == 0, 1.0, 2.0 * jnp.cos(phases)) / period
    imag_cols = jnp.where(frequency == 0, alternate, -2.0 * jnp.sin(phases)) / period
    return jnp.concatenate([real_cols, imag_cols], axis=1)


def packed_product(response, signal, block_len):
    first_slot = (jnp.arange(block_len) == 0)[:, None]
    resp_real = response[..., :block_len, :]
    resp_imag = response[..., block_len:, :]
    sig_real = signal[..., :block_len, :]
    sig_imag = signal[..., block_len:, :]
    cross_term = resp_imag * sig_imag
    prod_real = resp_real * sig_real - jnp.where(first_slot, 0.0, cross_term)
    prod_imag = jnp.where(first_slot, cross_term, resp_real * sig_imag + resp_imag * sig_real)
    return jnp.concatenate([prod_real, prod_imag], axis=-2)


def split_bf16(values):
    high = values.astype(jnp.bfloat16)
    return high, (values - high.astype(jnp.float32)).astype(jnp.bfloat16)


def conv_kernel(
    piece_ref, basis_hi_ref, basis_lo_ref, out_cols_ref, query_ref, carried_ref, skip_ref,
    fwd_hi_ref, fwd_lo_ref, inv_hi_ref, inv_lo_ref, out_ref, resp_ref,
):
    tables, rows, lanes = carried_ref.shape
    block_total = resp_ref.shape[0]
    cols_hi, cols_lo = split_bf16(out_cols_ref[...])

    def fill(block, carry):
        basis_hi = basis_hi_ref[block]
        resp_ref[block] = (
            jnp.dot(basis_hi, cols_hi, preferred_element_type=jnp.float32)
            + jnp.dot(basis_hi, cols_lo, preferred_element_type=jnp.float32)
            + jnp.dot(basis_lo_ref[block], cols_hi, preferred_element_type=jnp.float32)
        )
        return carry

    lax.fori_loop(0, block_total, fill, 0)
    first = lax.broadcasted_iota(jnp.int32, (rows, lanes), 0) == 0
    fwd_hi = fwd_hi_ref[...]
    fwd_lo = fwd_lo_ref[...]

    def dot(a, b):
        return jnp.dot(a, b, preferred_element_type=jnp.float32)

    for table in range(tables):

        def one_block(block, acc):
            acc_real, acc_imag = acc
            block_rows = piece_ref[table, pl.ds(pl.multiple_of(block * rows, rows), rows), :]
            signal = dot(fwd_hi, block_rows) + dot(fwd_lo, block_rows)
            response = resp_ref[block]
            resp_real = response[:rows]
            resp_imag = response[rows:]
            sig_real = signal[:rows]
            sig_imag = signal[rows:]
            cross = resp_imag * sig_imag
            acc_real = acc_real + (resp_real * sig_real - jnp.where(first, 0.0, cross))
            acc_imag = acc_imag + jnp.where(first, cross, resp_real * sig_imag + resp_imag * sig_real)
            return acc_real, acc_imag

        zeros = jnp.zeros((rows, lanes), jnp.float32)
        acc_real, acc_imag = lax.fori_loop(0, block_total, one_block, (zeros, zeros))
        spectrum = jnp.concatenate([acc_real, acc_imag], axis=0)
        spec_hi, spec_lo = split_bf16(spectrum)
        inv_hi = inv_hi_ref[...]
        conv = dot(inv_hi, spec_hi) + dot(inv_hi, spec_lo) + dot(inv_lo_ref[...], spec_hi)
        gated = query_ref[table] * (conv + skip_ref[...] * carried_ref[table].astype(jnp.float32))
        out_ref[table] = gated.astype(out_ref.dtype)


def fused_conv(piece, basis_spec, out_cols, query_gate, carried, skip, fwd_half, inverse):
    tables, rows, width = carried.shape
    block_total = basis_spec.shape[0]
    basis_hi, basis_lo = split_bf16(basis_spec)
    lanes = 256 if width % 256 == 0 else width
    fwd_hi, fwd_lo = split_bf16(fwd_half)
    inv_hi, inv_lo = split_bf16(inverse)
    tile3 = lambda i: (0, 0, i)
    whole2 = lambda i: (0, 0)
    return pl.pallas_call(
        conv_kernel,
        grid=(width // lanes,),
        in_specs=[
            pl.BlockSpec((tables, piece.shape[1], lanes), tile3),
            pl.BlockSpec(basis_hi.shape, lambda i: (0, 0, 0)),
            pl.BlockSpec(basis_lo.shape, lambda i: (0, 0, 0)),
            pl.BlockSpec((out_cols.shape[0], lanes), lambda i: (0, i)),
            pl.BlockSpec((tables, rows, lanes), tile3),
            pl.BlockSpec((tables, rows, lanes), tile3),
            pl.BlockSpec((1, lanes), lambda i: (0, i)),
            pl.BlockSpec(fwd_hi.shape, whole2),
            pl.BlockSpec(fwd_lo.shape, whole2),
            pl.BlockSpec(inv_hi.shape, whole2),
            pl.BlockSpec(inv_lo.shape, whole2),
        ],
        out_specs=pl.BlockSpec((tables, rows, lanes), tile3),
        out_shape=jax.ShapeDtypeStruct((tables, rows, width), jnp.bfloat16),
        scratch_shapes=[pltpu.VMEM((block_total, 2 * rows, lanes), jnp.float32)],
        compiler_params=pltpu.CompilerParams(vmem_limit_bytes=48 * 1024 * 1024),
    )(piece, basis_hi, basis_lo, out_cols, query_gate, carried, skip.reshape(1, width), fwd_hi, fwd_lo, inv_hi, inv_lo)


def shards(
    tokens,
    in_weight,
    short_weight,
    basis_in,
    basis_bias,
    basis_mid,
    basis_shift,
    response_out,
    skip_gain,
    block_counts,
):
    seq_dev, block_len, width = tokens.shape
    local_ch = skip_gain.shape[0]
    params = jnp.concatenate(
        [response_out.reshape(2 * response_out.shape[1], local_ch), skip_gain[None, :]], axis=0
    )
    gathered = gather_by_permutes(params, "fsdp")
    gathered = jnp.transpose(gathered, (1, 0, 2)).reshape(params.shape[0], width)
    stacked_out = gathered[:-1]
    full_skip = gathered[-1]
    seq_count = lax.axis_size("seq")
    position = lax.axis_index("seq")
    total_len = float(seq_count * block_len)
    forward = forward_table(block_len)
    forward_half = forward[:, :block_len]
    inverse = inverse_table(block_len)
    circular = jnp.arange(2 * block_len, dtype=jnp.int32)
    wrapped = jnp.where(circular < block_len, circular, circular - 2 * block_len)

    block_total = seq_count
    offsets = (position - jnp.arange(block_total, dtype=jnp.int32)) * block_len
    lag_values = (offsets[:, None] + wrapped[None, :]).reshape(-1)
    basis_rows = filter_basis(lag_values, total_len, basis_in, basis_bias, basis_mid, basis_shift)
    ahead_mask = (lag_values >= 0).astype(jnp.float32)[:, None]
    paired = jnp.concatenate([basis_rows * ahead_mask, basis_rows * (1.0 - ahead_mask)], axis=1)
    paired = paired.reshape(block_total, 2 * block_len, paired.shape[-1])
    basis_spec = jnp.einsum("gf,bfk->bgk", forward, paired, precision=lax.Precision.HIGHEST)
    group_tokens = lax.all_gather(tokens, "fsdp", axis=0, tiled=True)
    group_tokens, basis_spec = lax.optimization_barrier((group_tokens, basis_spec))
    group_rows = group_tokens.shape[0]
    local_cols = in_weight.shape[1]
    partial = jnp.dot(
        group_tokens.reshape(group_rows * block_len, width),
        in_weight,
        preferred_element_type=jnp.float32,
    ).astype(jnp.bfloat16)
    partial = partial.reshape(group_rows, block_len, local_cols)
    projected = lax.all_to_all(partial, "fsdp", 0, 2, tiled=True)
    padded = padded_2(projected, (("seq", 1),), 1)
    shorted = (
        short_weight[0] * padded[:, :-2]
        + short_weight[1] * padded[:, 1:-1]
        + short_weight[2] * padded[:, 2:]
    )
    query_gate = shorted[:, :, :width]
    key_part = shorted[:, :, width : 2 * width]
    value_part = shorted[:, :, 2 * width :]
    valid_mask = (jnp.arange(block_len, dtype=jnp.int32)[None, :] < block_counts).astype(
        jnp.float32
    )
    carried = (key_part * value_part * valid_mask[:, :, None]).astype(jnp.bfloat16)
    piece = lax.all_gather(carried, "seq", axis=1, tiled=True)

    return fused_conv(piece, basis_spec, stacked_out, query_gate, carried, full_skip, forward_half, inverse)


def solution(mesh):
    placed = (
        P(("groups", "fsdp"), "seq", None),
        P(None, "fsdp"),
        P(),
        P(),
        P(),
        P(),
        P(),
        P(None, None, "fsdp"),
        P("fsdp"),
        P(("groups", "fsdp"), "seq"),
    )
    return jax.shard_map(
        shards,
        mesh=mesh,
        in_specs=placed,
        out_specs=P(("groups", "fsdp"), "seq", None),
        check_vma=False,
    )
```

```python
import jax
import ml_dtypes
import numpy as np
import jax.numpy as jnp
from jax import lax
from jax.sharding import PartitionSpec as P
from jax.experimental import pallas as pl
from jax.experimental.pallas import tpu as pltpu


def padded_2(cells, sides, width):
    for axis, dim in sides:
        count = lax.axis_size(axis)
        ends = count - 1
        head = lax.slice_in_dim(cells, 0, width, axis=dim)
        tail = lax.slice_in_dim(cells, cells.shape[dim] - width, cells.shape[dim], axis=dim)
        cells = jnp.concatenate(
            [
                lax.ppermute(tail, axis, [(i, (i + 1) % count) for i in range(ends)]),
                cells,
                lax.ppermute(head, axis, [((i + 1) % count, i) for i in range(ends)]),
            ],
            axis=dim,
        )
    return cells


def gather_by_permutes(values, axis):
    count = lax.axis_size(axis)
    own = lax.axis_index(axis)
    received = [values]
    for shift in range(1, count):
        received.append(
            lax.ppermute(values, axis, [(i, (i + shift) % count) for i in range(count)])
        )
    stacked = jnp.stack(received)
    sources = (own - jnp.arange(count, dtype=jnp.int32)) % count
    order = jnp.argsort(sources)
    return jnp.take(stacked, order, axis=0)


def filter_basis(lag_values, total_len, basis_in, basis_bias, basis_mid, basis_shift):
    band_count = (basis_in.shape[0] - 1) // 2
    distance = jnp.abs(lag_values)
    periods = (2 ** (jnp.arange(band_count, dtype=jnp.int32) + 2) + 1).astype(jnp.int32)
    angles = (
        2.0
        * jnp.pi
        * (distance[:, None] % periods[None, :]).astype(jnp.float32)
        / periods[None, :].astype(jnp.float32)
    )
    linear = distance.astype(jnp.float32)[:, None] / total_len
    encoded = jnp.concatenate([linear, jnp.cos(angles), jnp.sin(angles)], axis=1)
    hidden = jnp.sin(jnp.dot(encoded, basis_in, precision=lax.Precision.HIGHEST) + basis_bias)
    return jnp.sin(jnp.dot(hidden, basis_mid, precision=lax.Precision.HIGHEST) + basis_shift)


def forward_table(block_len):
    period = 2 * block_len
    frequency = jnp.arange(block_len, dtype=jnp.int32)[:, None]
    samples = jnp.arange(period, dtype=jnp.int32)[None, :]
    phases = 2.0 * jnp.pi / period * (frequency * samples % period).astype(jnp.float32)
    alternate = (1 - 2 * (samples % 2)).astype(jnp.float32)
    real_rows = jnp.cos(phases)
    imag_rows = jnp.where(frequency == 0, alternate, -jnp.sin(phases))
    return jnp.concatenate([real_rows, imag_rows], axis=0)


def inverse_table(block_len):
    period = 2 * block_len
    places = jnp.arange(block_len, dtype=jnp.int32)[:, None]
    frequency = jnp.arange(block_len, dtype=jnp.int32)[None, :]
    phases = 2.0 * jnp.pi / period * (places * frequency % period).astype(jnp.float32)
    alternate = (1 - 2 * (places % 2)).astype(jnp.float32)
    real_cols = jnp.where(frequency == 0, 1.0, 2.0 * jnp.cos(phases)) / period
    imag_cols = jnp.where(frequency == 0, alternate, -2.0 * jnp.sin(phases)) / period
    return jnp.concatenate([real_cols, imag_cols], axis=1)


def packed_product(response, signal, block_len):
    first_slot = (jnp.arange(block_len) == 0)[:, None]
    resp_real = response[..., :block_len, :]
    resp_imag = response[..., block_len:, :]
    sig_real = signal[..., :block_len, :]
    sig_imag = signal[..., block_len:, :]
    cross_term = resp_imag * sig_imag
    prod_real = resp_real * sig_real - jnp.where(first_slot, 0.0, cross_term)
    prod_imag = jnp.where(first_slot, cross_term, resp_real * sig_imag + resp_imag * sig_real)
    return jnp.concatenate([prod_real, prod_imag], axis=-2)


def split_bf16(values):
    high = values.astype(jnp.bfloat16)
    return high, (values - high.astype(jnp.float32)).astype(jnp.bfloat16)


def split_table(values):
    high = values.astype(ml_dtypes.bfloat16)
    low = (values - high.astype(np.float64)).astype(ml_dtypes.bfloat16)
    return np.stack([high, low])


def dft_tables(block_len):
    period = 2 * block_len
    frequency = np.arange(block_len)[:, None]
    samples = np.arange(block_len)[None, :]
    phases = 2.0 * np.pi / period * (frequency * samples % period)
    alternate = (1 - 2 * (samples % 2)).astype(np.float64)
    real_rows = np.cos(phases)
    imag_rows = np.where(frequency == 0, alternate, -np.sin(phases))
    forward = np.concatenate([real_rows, imag_rows], axis=0)
    places = np.arange(block_len)[:, None]
    freq = np.arange(block_len)[None, :]
    phases = 2.0 * np.pi / period * (places * freq % period)
    alt = (1 - 2 * (places % 2)).astype(np.float64)
    real_cols = np.where(freq == 0, 1.0, 2.0 * np.cos(phases)) / period
    imag_cols = np.where(freq == 0, alt, -2.0 * np.sin(phases)) / period
    inverse = np.concatenate([np.broadcast_to(real_cols, (block_len, block_len)), imag_cols], axis=1)
    return split_table(forward), split_table(inverse)


def conv_kernel(
    piece_ref, basis_ref, out_cols_ref, query_ref, carried_ref, skip_ref, fwd_ref, inv_ref,
    out_ref, resp_ref,
):
    tables, rows, lanes = carried_ref.shape
    block_total = resp_ref.shape[0]
    cols_hi, cols_lo = split_bf16(out_cols_ref[...])

    def fill(block, carry):
        basis_hi = basis_ref[0, block]
        resp_ref[block] = (
            jnp.dot(basis_hi, cols_hi, preferred_element_type=jnp.float32)
            + jnp.dot(basis_hi, cols_lo, preferred_element_type=jnp.float32)
            + jnp.dot(basis_ref[1, block], cols_hi, preferred_element_type=jnp.float32)
        )
        return carry

    lax.fori_loop(0, block_total, fill, 0)
    first = lax.broadcasted_iota(jnp.int32, (rows, lanes), 0) == 0
    fwd_hi = fwd_ref[0]
    fwd_lo = fwd_ref[1]

    def dot(a, b):
        return jnp.dot(a, b, preferred_element_type=jnp.float32)

    for table in range(tables):

        def one_block(block, acc):
            acc_real, acc_imag = acc
            block_rows = piece_ref[table, pl.ds(pl.multiple_of(block * rows, rows), rows), :]
            signal = dot(fwd_hi, block_rows) + dot(fwd_lo, block_rows)
            response = resp_ref[block]
            resp_real = response[:rows]
            resp_imag = response[rows:]
            sig_real = signal[:rows]
            sig_imag = signal[rows:]
            cross = resp_imag * sig_imag
            acc_real = acc_real + (resp_real * sig_real - jnp.where(first, 0.0, cross))
            acc_imag = acc_imag + jnp.where(first, cross, resp_real * sig_imag + resp_imag * sig_real)
            return acc_real, acc_imag

        zeros = jnp.zeros((rows, lanes), jnp.float32)
        acc_real, acc_imag = lax.fori_loop(0, block_total, one_block, (zeros, zeros))
        spectrum = jnp.concatenate([acc_real, acc_imag], axis=0)
        spec_hi, spec_lo = split_bf16(spectrum)
        inv_hi = inv_ref[0]
        conv = dot(inv_hi, spec_hi) + dot(inv_hi, spec_lo) + dot(inv_ref[1], spec_hi)
        gated = query_ref[table] * (conv + skip_ref[...] * carried_ref[table].astype(jnp.float32))
        out_ref[table] = gated.astype(out_ref.dtype)


def fused_conv(piece, basis_spec, out_cols, query_gate, carried, skip):
    tables, rows, width = carried.shape
    block_total = basis_spec.shape[0]
    basis = jnp.stack(split_bf16(basis_spec))
    fwd, inv = dft_tables(rows)
    lanes = 256 if width % 256 == 0 else width
    tile3 = lambda i: (0, 0, i)
    return pl.pallas_call(
        conv_kernel,
        grid=(width // lanes,),
        in_specs=[
            pl.BlockSpec((tables, piece.shape[1], lanes), tile3),
            pl.BlockSpec(basis.shape, lambda i: (0, 0, 0, 0)),
            pl.BlockSpec((out_cols.shape[0], lanes), lambda i: (0, i)),
            pl.BlockSpec((tables, rows, lanes), tile3),
            pl.BlockSpec((tables, rows, lanes), tile3),
            pl.BlockSpec((1, lanes), lambda i: (0, i)),
            pl.BlockSpec(fwd.shape, lambda i: (0, 0, 0)),
            pl.BlockSpec(inv.shape, lambda i: (0, 0, 0)),
        ],
        out_specs=pl.BlockSpec((tables, rows, lanes), tile3),
        out_shape=jax.ShapeDtypeStruct((tables, rows, width), jnp.bfloat16),
        scratch_shapes=[pltpu.VMEM((block_total, 2 * rows, lanes), jnp.float32)],
        compiler_params=pltpu.CompilerParams(vmem_limit_bytes=48 * 1024 * 1024),
    )(piece, basis, out_cols, query_gate, carried, skip.reshape(1, width), jnp.asarray(fwd), jnp.asarray(inv))


def shards(
    tokens,
    in_weight,
    short_weight,
    basis_in,
    basis_bias,
    basis_mid,
    basis_shift,
    response_out,
    skip_gain,
    block_counts,
):
    seq_dev, block_len, width = tokens.shape
    local_ch = skip_gain.shape[0]
    params = jnp.concatenate(
        [response_out.reshape(2 * response_out.shape[1], local_ch), skip_gain[None, :]], axis=0
    )
    gathered = gather_by_permutes(params, "fsdp")
    gathered = jnp.transpose(gathered, (1, 0, 2)).reshape(params.shape[0], width)
    stacked_out = gathered[:-1]
    full_skip = gathered[-1]
    seq_count = lax.axis_size("seq")
    position = lax.axis_index("seq")
    total_len = float(seq_count * block_len)
    forward = forward_table(block_len)
    forward_half = forward[:, :block_len]
    inverse = inverse_table(block_len)
    circular = jnp.arange(2 * block_len, dtype=jnp.int32)
    wrapped = jnp.where(circular < block_len, circular, circular - 2 * block_len)

    block_total = seq_count
    offsets = (position - jnp.arange(block_total, dtype=jnp.int32)) * block_len
    lag_values = (offsets[:, None] + wrapped[None, :]).reshape(-1)
    basis_rows = filter_basis(lag_values, total_len, basis_in, basis_bias, basis_mid, basis_shift)
    ahead_mask = (lag_values >= 0).astype(jnp.float32)[:, None]
    paired = jnp.concatenate([basis_rows * ahead_mask, basis_rows * (1.0 - ahead_mask)], axis=1)
    paired = paired.reshape(block_total, 2 * block_len, paired.shape[-1])
    basis_spec = jnp.einsum("gf,bfk->bgk", forward, paired, precision=lax.Precision.HIGHEST)
    group_tokens = lax.all_gather(tokens, "fsdp", axis=0, tiled=True)
    group_tokens, basis_spec, stacked_out, full_skip = lax.optimization_barrier(
        (group_tokens, basis_spec, stacked_out, full_skip)
    )
    group_rows = group_tokens.shape[0]
    local_cols = in_weight.shape[1]
    partial = jnp.dot(
        group_tokens.reshape(group_rows * block_len, width),
        in_weight,
        preferred_element_type=jnp.float32,
    ).astype(jnp.bfloat16)
    partial = partial.reshape(group_rows, block_len, local_cols)
    projected = lax.all_to_all(partial, "fsdp", 0, 2, tiled=True)
    padded = padded_2(projected, (("seq", 1),), 1)
    shorted = (
        short_weight[0] * padded[:, :-2]
        + short_weight[1] * padded[:, 1:-1]
        + short_weight[2] * padded[:, 2:]
    )
    query_gate = shorted[:, :, :width]
    key_part = shorted[:, :, width : 2 * width]
    value_part = shorted[:, :, 2 * width :]
    valid_mask = (jnp.arange(block_len, dtype=jnp.int32)[None, :] < block_counts).astype(
        jnp.float32
    )
    carried = (key_part * value_part * valid_mask[:, :, None]).astype(jnp.bfloat16)
    piece = lax.all_gather(carried, "seq", axis=1, tiled=True)

    return fused_conv(piece, basis_spec, stacked_out, query_gate, carried, full_skip)


def solution(mesh):
    placed = (
        P(("groups", "fsdp"), "seq", None),
        P(None, "fsdp"),
        P(),
        P(),
        P(),
        P(),
        P(),
        P(None, None, "fsdp"),
        P("fsdp"),
        P(("groups", "fsdp"), "seq"),
    )
    return jax.shard_map(
        shards,
        mesh=mesh,
        in_specs=placed,
        out_specs=P(("groups", "fsdp"), "seq", None),
        check_vma=False,
    )
```

```python
import jax
import ml_dtypes
import numpy as np
import jax.numpy as jnp
from jax import lax
from jax.sharding import PartitionSpec as P
from jax.experimental import pallas as pl
from jax.experimental.pallas import tpu as pltpu


def padded_2(cells, sides, width):
    for axis, dim in sides:
        count = lax.axis_size(axis)
        ends = count - 1
        head = lax.slice_in_dim(cells, 0, width, axis=dim)
        tail = lax.slice_in_dim(cells, cells.shape[dim] - width, cells.shape[dim], axis=dim)
        cells = jnp.concatenate(
            [
                lax.ppermute(tail, axis, [(i, (i + 1) % count) for i in range(ends)]),
                cells,
                lax.ppermute(head, axis, [((i + 1) % count, i) for i in range(ends)]),
            ],
            axis=dim,
        )
    return cells


def gather_by_permutes(values, axis):
    count = lax.axis_size(axis)
    own = lax.axis_index(axis)
    received = [values]
    for shift in range(1, count):
        received.append(
            lax.ppermute(values, axis, [(i, (i + shift) % count) for i in range(count)])
        )
    stacked = jnp.stack(received)
    sources = (own - jnp.arange(count, dtype=jnp.int32)) % count
    order = jnp.argsort(sources)
    return jnp.take(stacked, order, axis=0)


def filter_basis(lag_values, total_len, basis_in, basis_bias, basis_mid, basis_shift):
    band_count = (basis_in.shape[0] - 1) // 2
    distance = jnp.abs(lag_values)
    periods = (2 ** (jnp.arange(band_count, dtype=jnp.int32) + 2) + 1).astype(jnp.int32)
    angles = (
        2.0
        * jnp.pi
        * (distance[:, None] % periods[None, :]).astype(jnp.float32)
        / periods[None, :].astype(jnp.float32)
    )
    linear = distance.astype(jnp.float32)[:, None] / total_len
    encoded = jnp.concatenate([linear, jnp.cos(angles), jnp.sin(angles)], axis=1)
    hidden = jnp.sin(jnp.dot(encoded, basis_in, precision=lax.Precision.HIGHEST) + basis_bias)
    return jnp.sin(jnp.dot(hidden, basis_mid, precision=lax.Precision.HIGHEST) + basis_shift)


def forward_table(block_len):
    period = 2 * block_len
    frequency = jnp.arange(block_len, dtype=jnp.int32)[:, None]
    samples = jnp.arange(period, dtype=jnp.int32)[None, :]
    phases = 2.0 * jnp.pi / period * (frequency * samples % period).astype(jnp.float32)
    alternate = (1 - 2 * (samples % 2)).astype(jnp.float32)
    real_rows = jnp.cos(phases)
    imag_rows = jnp.where(frequency == 0, alternate, -jnp.sin(phases))
    return jnp.concatenate([real_rows, imag_rows], axis=0)


def inverse_table(block_len):
    period = 2 * block_len
    places = jnp.arange(block_len, dtype=jnp.int32)[:, None]
    frequency = jnp.arange(block_len, dtype=jnp.int32)[None, :]
    phases = 2.0 * jnp.pi / period * (places * frequency % period).astype(jnp.float32)
    alternate = (1 - 2 * (places % 2)).astype(jnp.float32)
    real_cols = jnp.where(frequency == 0, 1.0, 2.0 * jnp.cos(phases)) / period
    imag_cols = jnp.where(frequency == 0, alternate, -2.0 * jnp.sin(phases)) / period
    return jnp.concatenate([real_cols, imag_cols], axis=1)


def packed_product(response, signal, block_len):
    first_slot = (jnp.arange(block_len) == 0)[:, None]
    resp_real = response[..., :block_len, :]
    resp_imag = response[..., block_len:, :]
    sig_real = signal[..., :block_len, :]
    sig_imag = signal[..., block_len:, :]
    cross_term = resp_imag * sig_imag
    prod_real = resp_real * sig_real - jnp.where(first_slot, 0.0, cross_term)
    prod_imag = jnp.where(first_slot, cross_term, resp_real * sig_imag + resp_imag * sig_real)
    return jnp.concatenate([prod_real, prod_imag], axis=-2)


def split_bf16(values):
    high = values.astype(jnp.bfloat16)
    return high, (values - high.astype(jnp.float32)).astype(jnp.bfloat16)


def split_table(values):
    high = values.astype(ml_dtypes.bfloat16)
    low = (values - high.astype(np.float64)).astype(ml_dtypes.bfloat16)
    return np.stack([high, low])


def dft_tables(block_len):
    period = 2 * block_len
    frequency = np.arange(block_len)[:, None]
    samples = np.arange(block_len)[None, :]
    phases = 2.0 * np.pi / period * (frequency * samples % period)
    alternate = (1 - 2 * (samples % 2)).astype(np.float64)
    real_rows = np.cos(phases)
    imag_rows = np.where(frequency == 0, alternate, -np.sin(phases))
    forward = np.concatenate([real_rows, imag_rows], axis=0)
    places = np.arange(block_len)[:, None]
    freq = np.arange(block_len)[None, :]
    phases = 2.0 * np.pi / period * (places * freq % period)
    alt = (1 - 2 * (places % 2)).astype(np.float64)
    real_cols = np.where(freq == 0, 1.0, 2.0 * np.cos(phases)) / period
    imag_cols = np.where(freq == 0, alt, -2.0 * np.sin(phases)) / period
    inverse = np.concatenate([np.broadcast_to(real_cols, (block_len, block_len)), imag_cols], axis=1)
    return split_table(forward), split_table(inverse)


def conv_kernel(
    piece_ref, basis_ref, out_cols_ref, query_ref, carried_ref, skip_ref, fwd_ref, inv_ref,
    out_ref, resp_ref,
):
    tables, rows, lanes = carried_ref.shape
    block_total = resp_ref.shape[0]
    cols_hi, cols_lo = split_bf16(out_cols_ref[...])

    def fill(block, carry):
        basis_hi = basis_ref[0, block]
        resp_ref[block] = (
            jnp.dot(basis_hi, cols_hi, preferred_element_type=jnp.float32)
            + jnp.dot(basis_hi, cols_lo, preferred_element_type=jnp.float32)
            + jnp.dot(basis_ref[1, block], cols_hi, preferred_element_type=jnp.float32)
        )
        return carry

    lax.fori_loop(0, block_total, fill, 0)
    first = lax.broadcasted_iota(jnp.int32, (rows, lanes), 0) == 0
    fwd_hi = fwd_ref[0]
    fwd_lo = fwd_ref[1]

    def dot(a, b):
        return jnp.dot(a, b, preferred_element_type=jnp.float32)

    for table in range(tables):

        def one_block(block, acc):
            acc_real, acc_imag = acc
            block_rows = piece_ref[table, pl.ds(pl.multiple_of(block * rows, rows), rows), :]
            signal = dot(fwd_hi, block_rows) + dot(fwd_lo, block_rows)
            response = resp_ref[block]
            resp_real = response[:rows]
            resp_imag = response[rows:]
            sig_real = signal[:rows]
            sig_imag = signal[rows:]
            cross = resp_imag * sig_imag
            acc_real = acc_real + (resp_real * sig_real - jnp.where(first, 0.0, cross))
            acc_imag = acc_imag + jnp.where(first, cross, resp_real * sig_imag + resp_imag * sig_real)
            return acc_real, acc_imag

        zeros = jnp.zeros((rows, lanes), jnp.float32)
        acc_real, acc_imag = lax.fori_loop(0, block_total, one_block, (zeros, zeros))
        spectrum = jnp.concatenate([acc_real, acc_imag], axis=0)
        spec_hi, spec_lo = split_bf16(spectrum)
        inv_hi = inv_ref[0]
        conv = dot(inv_hi, spec_hi) + dot(inv_hi, spec_lo) + dot(inv_ref[1], spec_hi)
        gated = query_ref[table] * (conv + skip_ref[...] * carried_ref[table].astype(jnp.float32))
        out_ref[table] = gated.astype(out_ref.dtype)


def fused_conv(piece, basis_spec, out_cols, query_gate, carried, skip):
    tables, rows, width = carried.shape
    block_total = basis_spec.shape[0]
    basis = jnp.stack(split_bf16(basis_spec))
    fwd, inv = dft_tables(rows)
    lanes = 256 if width % 256 == 0 else width
    tile3 = lambda i: (0, 0, i)
    return pl.pallas_call(
        conv_kernel,
        grid=(width // lanes,),
        in_specs=[
            pl.BlockSpec((tables, piece.shape[1], lanes), tile3),
            pl.BlockSpec(basis.shape, lambda i: (0, 0, 0, 0)),
            pl.BlockSpec((out_cols.shape[0], lanes), lambda i: (0, i)),
            pl.BlockSpec((tables, rows, lanes), tile3),
            pl.BlockSpec((tables, rows, lanes), tile3),
            pl.BlockSpec((1, lanes), lambda i: (0, i)),
            pl.BlockSpec(fwd.shape, lambda i: (0, 0, 0)),
            pl.BlockSpec(inv.shape, lambda i: (0, 0, 0)),
        ],
        out_specs=pl.BlockSpec((tables, rows, lanes), tile3),
        out_shape=jax.ShapeDtypeStruct((tables, rows, width), jnp.bfloat16),
        scratch_shapes=[pltpu.VMEM((block_total, 2 * rows, lanes), jnp.float32)],
        compiler_params=pltpu.CompilerParams(vmem_limit_bytes=48 * 1024 * 1024),
    )(piece, basis, out_cols, query_gate, carried, skip.reshape(1, width), jnp.asarray(fwd), jnp.asarray(inv))


def shards(
    tokens,
    in_weight,
    short_weight,
    basis_in,
    basis_bias,
    basis_mid,
    basis_shift,
    response_out,
    skip_gain,
    block_counts,
):
    seq_dev, block_len, width = tokens.shape
    local_ch = skip_gain.shape[0]
    params = jnp.concatenate(
        [response_out.reshape(2 * response_out.shape[1], local_ch), skip_gain[None, :]], axis=0
    )
    gathered = gather_by_permutes(params, "fsdp")
    gathered = jnp.transpose(gathered, (1, 0, 2)).reshape(params.shape[0], width)
    stacked_out = gathered[:-1]
    full_skip = gathered[-1]
    seq_count = lax.axis_size("seq")
    position = lax.axis_index("seq")
    total_len = float(seq_count * block_len)
    forward = forward_table(block_len)
    forward_half = forward[:, :block_len]
    inverse = inverse_table(block_len)
    circular = jnp.arange(2 * block_len, dtype=jnp.int32)
    wrapped = jnp.where(circular < block_len, circular, circular - 2 * block_len)

    block_total = seq_count
    offsets = (position - jnp.arange(block_total, dtype=jnp.int32)) * block_len
    lag_values = (offsets[:, None] + wrapped[None, :]).reshape(-1)
    basis_rows = filter_basis(lag_values, total_len, basis_in, basis_bias, basis_mid, basis_shift)
    ahead_mask = (lag_values >= 0).astype(jnp.float32)[:, None]
    paired = jnp.concatenate([basis_rows * ahead_mask, basis_rows * (1.0 - ahead_mask)], axis=1)
    paired = paired.reshape(block_total, 2 * block_len, paired.shape[-1])
    basis_spec = jnp.einsum("gf,bfk->bgk", forward, paired, precision=lax.Precision.HIGHEST)
    group_tokens = lax.all_gather(tokens, "fsdp", axis=0, tiled=True)
    group_tokens, basis_spec = lax.optimization_barrier((group_tokens, basis_spec))
    group_rows = group_tokens.shape[0]
    local_cols = in_weight.shape[1]
    partial = jnp.dot(
        group_tokens.reshape(group_rows * block_len, width),
        in_weight,
        preferred_element_type=jnp.float32,
    ).astype(jnp.bfloat16)
    partial = partial.reshape(group_rows, block_len, local_cols)
    projected = lax.all_to_all(partial, "fsdp", 0, 2, tiled=True)
    padded = padded_2(projected, (("seq", 1),), 1)
    shorted = (
        short_weight[0] * padded[:, :-2]
        + short_weight[1] * padded[:, 1:-1]
        + short_weight[2] * padded[:, 2:]
    )
    query_gate = shorted[:, :, :width]
    key_part = shorted[:, :, width : 2 * width]
    value_part = shorted[:, :, 2 * width :]
    valid_mask = (jnp.arange(block_len, dtype=jnp.int32)[None, :] < block_counts).astype(
        jnp.float32
    )
    carried = (key_part * value_part * valid_mask[:, :, None]).astype(jnp.bfloat16)
    piece = lax.all_gather(carried, "seq", axis=1, tiled=True)

    return fused_conv(piece, basis_spec, stacked_out, query_gate, carried, full_skip)


def solution(mesh):
    placed = (
        P(("groups", "fsdp"), "seq", None),
        P(None, "fsdp"),
        P(),
        P(),
        P(),
        P(),
        P(),
        P(None, None, "fsdp"),
        P("fsdp"),
        P(("groups", "fsdp"), "seq"),
    )
    return jax.shard_map(
        shards,
        mesh=mesh,
        in_specs=placed,
        out_specs=P(("groups", "fsdp"), "seq", None),
        check_vma=False,
    )
```

```python
import jax
import ml_dtypes
import numpy as np
import jax.numpy as jnp
from jax import lax
from jax.sharding import PartitionSpec as P
from jax.experimental import pallas as pl
from jax.experimental.pallas import tpu as pltpu


def padded_2(cells, sides, width):
    for axis, dim in sides:
        count = lax.axis_size(axis)
        ends = count - 1
        head = lax.slice_in_dim(cells, 0, width, axis=dim)
        tail = lax.slice_in_dim(cells, cells.shape[dim] - width, cells.shape[dim], axis=dim)
        cells = jnp.concatenate(
            [
                lax.ppermute(tail, axis, [(i, (i + 1) % count) for i in range(ends)]),
                cells,
                lax.ppermute(head, axis, [((i + 1) % count, i) for i in range(ends)]),
            ],
            axis=dim,
        )
    return cells


def gather_by_permutes(values, axis):
    count = lax.axis_size(axis)
    own = lax.axis_index(axis)
    received = [values]
    for shift in range(1, count):
        received.append(
            lax.ppermute(values, axis, [(i, (i + shift) % count) for i in range(count)])
        )
    stacked = jnp.stack(received)
    sources = (own - jnp.arange(count, dtype=jnp.int32)) % count
    order = jnp.argsort(sources)
    return jnp.take(stacked, order, axis=0)


def filter_basis(lag_values, total_len, basis_in, basis_bias, basis_mid, basis_shift):
    band_count = (basis_in.shape[0] - 1) // 2
    distance = jnp.abs(lag_values)
    periods = (2 ** (jnp.arange(band_count, dtype=jnp.int32) + 2) + 1).astype(jnp.int32)
    angles = (
        2.0
        * jnp.pi
        * (distance[:, None] % periods[None, :]).astype(jnp.float32)
        / periods[None, :].astype(jnp.float32)
    )
    linear = distance.astype(jnp.float32)[:, None] / total_len
    encoded = jnp.concatenate([linear, jnp.cos(angles), jnp.sin(angles)], axis=1)
    hidden = jnp.sin(jnp.dot(encoded, basis_in, precision=lax.Precision.HIGHEST) + basis_bias)
    return jnp.sin(jnp.dot(hidden, basis_mid, precision=lax.Precision.HIGHEST) + basis_shift)


def forward_table(block_len):
    period = 2 * block_len
    frequency = jnp.arange(block_len, dtype=jnp.int32)[:, None]
    samples = jnp.arange(period, dtype=jnp.int32)[None, :]
    phases = 2.0 * jnp.pi / period * (frequency * samples % period).astype(jnp.float32)
    alternate = (1 - 2 * (samples % 2)).astype(jnp.float32)
    real_rows = jnp.cos(phases)
    imag_rows = jnp.where(frequency == 0, alternate, -jnp.sin(phases))
    return jnp.concatenate([real_rows, imag_rows], axis=0)


def inverse_table(block_len):
    period = 2 * block_len
    places = jnp.arange(block_len, dtype=jnp.int32)[:, None]
    frequency = jnp.arange(block_len, dtype=jnp.int32)[None, :]
    phases = 2.0 * jnp.pi / period * (places * frequency % period).astype(jnp.float32)
    alternate = (1 - 2 * (places % 2)).astype(jnp.float32)
    real_cols = jnp.where(frequency == 0, 1.0, 2.0 * jnp.cos(phases)) / period
    imag_cols = jnp.where(frequency == 0, alternate, -2.0 * jnp.sin(phases)) / period
    return jnp.concatenate([real_cols, imag_cols], axis=1)


def packed_product(response, signal, block_len):
    first_slot = (jnp.arange(block_len) == 0)[:, None]
    resp_real = response[..., :block_len, :]
    resp_imag = response[..., block_len:, :]
    sig_real = signal[..., :block_len, :]
    sig_imag = signal[..., block_len:, :]
    cross_term = resp_imag * sig_imag
    prod_real = resp_real * sig_real - jnp.where(first_slot, 0.0, cross_term)
    prod_imag = jnp.where(first_slot, cross_term, resp_real * sig_imag + resp_imag * sig_real)
    return jnp.concatenate([prod_real, prod_imag], axis=-2)


def split_bf16(values):
    high = values.astype(jnp.bfloat16)
    return high, (values - high.astype(jnp.float32)).astype(jnp.bfloat16)


def split_table(values):
    high = values.astype(ml_dtypes.bfloat16)
    low = (values - high.astype(np.float64)).astype(ml_dtypes.bfloat16)
    return np.stack([high, low])


def dft_tables(block_len):
    period = 2 * block_len
    frequency = np.arange(block_len)[:, None]
    samples = np.arange(block_len)[None, :]
    phases = 2.0 * np.pi / period * (frequency * samples % period)
    alternate = (1 - 2 * (samples % 2)).astype(np.float64)
    real_rows = np.cos(phases)
    imag_rows = np.where(frequency == 0, alternate, -np.sin(phases))
    forward = np.concatenate([real_rows, imag_rows], axis=0)
    places = np.arange(block_len)[:, None]
    freq = np.arange(block_len)[None, :]
    phases = 2.0 * np.pi / period * (places * freq % period)
    alt = (1 - 2 * (places % 2)).astype(np.float64)
    real_cols = np.where(freq == 0, 1.0, 2.0 * np.cos(phases)) / period
    imag_cols = np.where(freq == 0, alt, -2.0 * np.sin(phases)) / period
    inverse = np.concatenate([np.broadcast_to(real_cols, (block_len, block_len)), imag_cols], axis=1)
    return split_table(forward), split_table(inverse)


def conv_kernel(
    piece_ref, basis_ref, out_cols_ref, query_ref, carried_ref, skip_ref, fwd_ref, inv_ref,
    out_ref, resp_ref,
):
    tables, rows, lanes = carried_ref.shape
    block_total = resp_ref.shape[0]
    cols_hi, cols_lo = split_bf16(out_cols_ref[...])
    cols = jnp.concatenate([cols_hi, cols_lo, cols_hi], axis=0)

    def dot(a, b):
        return jnp.dot(a, b, preferred_element_type=jnp.float32)

    def fill(block, carry):
        resp_ref[block] = dot(basis_ref[block], cols)
        return carry

    lax.fori_loop(0, block_total, fill, 0)
    first = lax.broadcasted_iota(jnp.int32, (rows, lanes), 0) == 0
    fwd = fwd_ref[...]
    inv = inv_ref[...]

    for table in range(tables):

        def one_block(block, acc):
            acc_real, acc_imag, edge = acc
            block_rows = piece_ref[table, pl.ds(pl.multiple_of(block * rows, rows), rows), :]
            signal = dot(fwd, jnp.concatenate([block_rows, block_rows], axis=0))
            response = resp_ref[block]
            resp_real = response[:rows]
            resp_imag = response[rows:]
            sig_real = signal[:rows]
            sig_imag = signal[rows:]
            acc_real = acc_real + (resp_real * sig_real - resp_imag * sig_imag)
            acc_imag = acc_imag + (resp_real * sig_imag + resp_imag * sig_real)
            edge = edge + resp_imag[0:1] * sig_imag[0:1]
            return acc_real, acc_imag, edge

        zeros = jnp.zeros((rows, lanes), jnp.float32)
        acc_real, acc_imag, edge = lax.fori_loop(
            0, block_total, one_block, (zeros, zeros, jnp.zeros((1, lanes), jnp.float32))
        )
        acc_real = acc_real + jnp.where(first, edge, 0.0)
        acc_imag = jnp.where(first, edge, acc_imag)
        spectrum = jnp.concatenate([acc_real, acc_imag], axis=0)
        spec_hi, spec_lo = split_bf16(spectrum)
        conv = dot(inv, jnp.concatenate([spec_hi, spec_lo, spec_hi], axis=0))
        gated = query_ref[table] * (conv + skip_ref[...] * carried_ref[table].astype(jnp.float32))
        out_ref[table] = gated.astype(out_ref.dtype)


def fused_conv(piece, basis_spec, out_cols, query_gate, carried, skip):
    tables, rows, width = carried.shape
    block_total = basis_spec.shape[0]
    basis_hi, basis_lo = split_bf16(basis_spec)
    basis = jnp.concatenate([basis_hi, basis_hi, basis_lo], axis=2)
    fwd, inv = dft_tables(rows)
    fwd = np.concatenate([fwd[0], fwd[1]], axis=1)
    inv = np.concatenate([inv[0], inv[0], inv[1]], axis=1)
    lanes = 768 if width % 768 == 0 else width
    tile3 = lambda i: (0, 0, i)
    return pl.pallas_call(
        conv_kernel,
        grid=(width // lanes,),
        in_specs=[
            pl.BlockSpec((tables, piece.shape[1], lanes), tile3),
            pl.BlockSpec(basis.shape, lambda i: (0, 0, 0)),
            pl.BlockSpec((out_cols.shape[0], lanes), lambda i: (0, i)),
            pl.BlockSpec((tables, rows, lanes), tile3),
            pl.BlockSpec((tables, rows, lanes), tile3),
            pl.BlockSpec((1, lanes), lambda i: (0, i)),
            pl.BlockSpec(fwd.shape, lambda i: (0, 0)),
            pl.BlockSpec(inv.shape, lambda i: (0, 0)),
        ],
        out_specs=pl.BlockSpec((tables, rows, lanes), tile3),
        out_shape=jax.ShapeDtypeStruct((tables, rows, width), jnp.bfloat16),
        scratch_shapes=[pltpu.VMEM((block_total, 2 * rows, lanes), jnp.float32)],
        compiler_params=pltpu.CompilerParams(vmem_limit_bytes=48 * 1024 * 1024),
    )(piece, basis, out_cols, query_gate, carried, skip.reshape(1, width), jnp.asarray(fwd), jnp.asarray(inv))


def shards(
    tokens,
    in_weight,
    short_weight,
    basis_in,
    basis_bias,
    basis_mid,
    basis_shift,
    response_out,
    skip_gain,
    block_counts,
):
    seq_dev, block_len, width = tokens.shape
    local_ch = skip_gain.shape[0]
    params = jnp.concatenate(
        [response_out.reshape(2 * response_out.shape[1], local_ch), skip_gain[None, :]], axis=0
    )
    gathered = gather_by_permutes(params, "fsdp")
    gathered = jnp.transpose(gathered, (1, 0, 2)).reshape(params.shape[0], width)
    stacked_out = gathered[:-1]
    full_skip = gathered[-1]
    seq_count = lax.axis_size("seq")
    position = lax.axis_index("seq")
    total_len = float(seq_count * block_len)
    forward = forward_table(block_len)
    forward_half = forward[:, :block_len]
    inverse = inverse_table(block_len)
    circular = jnp.arange(2 * block_len, dtype=jnp.int32)
    wrapped = jnp.where(circular < block_len, circular, circular - 2 * block_len)

    block_total = seq_count
    offsets = (position - jnp.arange(block_total, dtype=jnp.int32)) * block_len
    lag_values = (offsets[:, None] + wrapped[None, :]).reshape(-1)
    basis_rows = filter_basis(lag_values, total_len, basis_in, basis_bias, basis_mid, basis_shift)
    ahead_mask = (lag_values >= 0).astype(jnp.float32)[:, None]
    paired = jnp.concatenate([basis_rows * ahead_mask, basis_rows * (1.0 - ahead_mask)], axis=1)
    paired = paired.reshape(block_total, 2 * block_len, paired.shape[-1])
    basis_spec = jnp.einsum("gf,bfk->bgk", forward, paired, precision=lax.Precision.HIGHEST)
    group_tokens = lax.all_gather(tokens, "fsdp", axis=0, tiled=True)
    group_tokens, basis_spec = lax.optimization_barrier((group_tokens, basis_spec))
    group_rows = group_tokens.shape[0]
    local_cols = in_weight.shape[1]
    partial = jnp.dot(
        group_tokens.reshape(group_rows * block_len, width),
        in_weight,
        preferred_element_type=jnp.float32,
    ).astype(jnp.bfloat16)
    partial = partial.reshape(group_rows, block_len, local_cols)
    projected = lax.all_to_all(partial, "fsdp", 0, 2, tiled=True)
    padded = padded_2(projected, (("seq", 1),), 1)
    shorted = (
        short_weight[0] * padded[:, :-2]
        + short_weight[1] * padded[:, 1:-1]
        + short_weight[2] * padded[:, 2:]
    )
    query_gate = shorted[:, :, :width]
    key_part = shorted[:, :, width : 2 * width]
    value_part = shorted[:, :, 2 * width :]
    valid_mask = (jnp.arange(block_len, dtype=jnp.int32)[None, :] < block_counts).astype(
        jnp.float32
    )
    carried = (key_part * value_part * valid_mask[:, :, None]).astype(jnp.bfloat16)
    piece = lax.all_gather(carried, "seq", axis=1, tiled=True)

    return fused_conv(piece, basis_spec, stacked_out, query_gate, carried, full_skip)


def solution(mesh):
    placed = (
        P(("groups", "fsdp"), "seq", None),
        P(None, "fsdp"),
        P(),
        P(),
        P(),
        P(),
        P(),
        P(None, None, "fsdp"),
        P("fsdp"),
        P(("groups", "fsdp"), "seq"),
    )
    return jax.shard_map(
        shards,
        mesh=mesh,
        in_specs=placed,
        out_specs=P(("groups", "fsdp"), "seq", None),
        check_vma=False,
    )
```

```python
import jax
import ml_dtypes
import numpy as np
import jax.numpy as jnp
from jax import lax
from jax.sharding import PartitionSpec as P
from jax.experimental import pallas as pl
from jax.experimental.pallas import tpu as pltpu


def padded_2(cells, sides, width):
    for axis, dim in sides:
        count = lax.axis_size(axis)
        ends = count - 1
        head = lax.slice_in_dim(cells, 0, width, axis=dim)
        tail = lax.slice_in_dim(cells, cells.shape[dim] - width, cells.shape[dim], axis=dim)
        cells = jnp.concatenate(
            [
                lax.ppermute(tail, axis, [(i, (i + 1) % count) for i in range(ends)]),
                cells,
                lax.ppermute(head, axis, [((i + 1) % count, i) for i in range(ends)]),
            ],
            axis=dim,
        )
    return cells


def gather_by_permutes(values, axis):
    count = lax.axis_size(axis)
    own = lax.axis_index(axis)
    received = [values]
    for shift in range(1, count):
        received.append(
            lax.ppermute(values, axis, [(i, (i + shift) % count) for i in range(count)])
        )
    stacked = jnp.stack(received)
    sources = (own - jnp.arange(count, dtype=jnp.int32)) % count
    order = jnp.argsort(sources)
    return jnp.take(stacked, order, axis=0)


def filter_basis(lag_values, total_len, basis_in, basis_bias, basis_mid, basis_shift):
    band_count = (basis_in.shape[0] - 1) // 2
    distance = jnp.abs(lag_values)
    periods = (2 ** (jnp.arange(band_count, dtype=jnp.int32) + 2) + 1).astype(jnp.int32)
    angles = (
        2.0
        * jnp.pi
        * (distance[:, None] % periods[None, :]).astype(jnp.float32)
        / periods[None, :].astype(jnp.float32)
    )
    linear = distance.astype(jnp.float32)[:, None] / total_len
    encoded = jnp.concatenate([linear, jnp.cos(angles), jnp.sin(angles)], axis=1)
    hidden = jnp.sin(jnp.dot(encoded, basis_in, precision=lax.Precision.HIGHEST) + basis_bias)
    return jnp.sin(jnp.dot(hidden, basis_mid, precision=lax.Precision.HIGHEST) + basis_shift)


def forward_table(block_len):
    period = 2 * block_len
    frequency = jnp.arange(block_len, dtype=jnp.int32)[:, None]
    samples = jnp.arange(period, dtype=jnp.int32)[None, :]
    phases = 2.0 * jnp.pi / period * (frequency * samples % period).astype(jnp.float32)
    alternate = (1 - 2 * (samples % 2)).astype(jnp.float32)
    real_rows = jnp.cos(phases)
    imag_rows = jnp.where(frequency == 0, alternate, -jnp.sin(phases))
    return jnp.concatenate([real_rows, imag_rows], axis=0)


def inverse_table(block_len):
    period = 2 * block_len
    places = jnp.arange(block_len, dtype=jnp.int32)[:, None]
    frequency = jnp.arange(block_len, dtype=jnp.int32)[None, :]
    phases = 2.0 * jnp.pi / period * (places * frequency % period).astype(jnp.float32)
    alternate = (1 - 2 * (places % 2)).astype(jnp.float32)
    real_cols = jnp.where(frequency == 0, 1.0, 2.0 * jnp.cos(phases)) / period
    imag_cols = jnp.where(frequency == 0, alternate, -2.0 * jnp.sin(phases)) / period
    return jnp.concatenate([real_cols, imag_cols], axis=1)


def packed_product(response, signal, block_len):
    first_slot = (jnp.arange(block_len) == 0)[:, None]
    resp_real = response[..., :block_len, :]
    resp_imag = response[..., block_len:, :]
    sig_real = signal[..., :block_len, :]
    sig_imag = signal[..., block_len:, :]
    cross_term = resp_imag * sig_imag
    prod_real = resp_real * sig_real - jnp.where(first_slot, 0.0, cross_term)
    prod_imag = jnp.where(first_slot, cross_term, resp_real * sig_imag + resp_imag * sig_real)
    return jnp.concatenate([prod_real, prod_imag], axis=-2)


def split_bf16(values):
    high = values.astype(jnp.bfloat16)
    return high, (values - high.astype(jnp.float32)).astype(jnp.bfloat16)


def split_table(values):
    high = values.astype(ml_dtypes.bfloat16)
    low = (values - high.astype(np.float64)).astype(ml_dtypes.bfloat16)
    return np.stack([high, low])


def dft_tables(block_len):
    period = 2 * block_len
    frequency = np.arange(block_len)[:, None]
    samples = np.arange(block_len)[None, :]
    phases = 2.0 * np.pi / period * (frequency * samples % period)
    alternate = (1 - 2 * (samples % 2)).astype(np.float64)
    real_rows = np.cos(phases)
    imag_rows = np.where(frequency == 0, alternate, -np.sin(phases))
    forward = np.concatenate([real_rows, imag_rows], axis=0)
    places = np.arange(block_len)[:, None]
    freq = np.arange(block_len)[None, :]
    phases = 2.0 * np.pi / period * (places * freq % period)
    alt = (1 - 2 * (places % 2)).astype(np.float64)
    real_cols = np.where(freq == 0, 1.0, 2.0 * np.cos(phases)) / period
    imag_cols = np.where(freq == 0, alt, -2.0 * np.sin(phases)) / period
    inverse = np.concatenate([np.broadcast_to(real_cols, (block_len, block_len)), imag_cols], axis=1)
    return split_table(forward), split_table(inverse)


def conv_kernel(
    piece_ref, basis_ref, out_cols_ref, query_ref, carried_ref, skip_ref, fwd_ref, inv_ref,
    out_ref, resp_ref,
):
    tables, rows, lanes = carried_ref.shape
    block_total = resp_ref.shape[0]
    cols_hi, cols_lo = split_bf16(out_cols_ref[...])
    cols = jnp.concatenate([cols_hi, cols_lo, cols_hi], axis=0)

    def dot(a, b):
        return jnp.dot(a, b, preferred_element_type=jnp.float32)

    def fill(block, carry):
        resp_ref[block] = dot(basis_ref[block], cols)
        return carry

    lax.fori_loop(0, block_total, fill, 0)
    first = lax.broadcasted_iota(jnp.int32, (rows, lanes), 0) == 0
    fwd = fwd_ref[...]
    inv = inv_ref[...]

    for table in range(tables):

        def one_block(block, acc):
            acc_real, acc_imag, edge = acc
            block_rows = piece_ref[table, pl.ds(pl.multiple_of(block * rows, rows), rows), :]
            signal = dot(fwd, jnp.concatenate([block_rows, block_rows], axis=0))
            response = resp_ref[block]
            resp_real = response[:rows]
            resp_imag = response[rows:]
            sig_real = signal[:rows]
            sig_imag = signal[rows:]
            acc_real = acc_real + (resp_real * sig_real - resp_imag * sig_imag)
            acc_imag = acc_imag + (resp_real * sig_imag + resp_imag * sig_real)
            edge = edge + resp_imag[0:1] * sig_imag[0:1]
            return acc_real, acc_imag, edge

        zeros = jnp.zeros((rows, lanes), jnp.float32)
        acc_real, acc_imag, edge = lax.fori_loop(
            0, block_total, one_block, (zeros, zeros, jnp.zeros((1, lanes), jnp.float32))
        )
        acc_real = acc_real + jnp.where(first, edge, 0.0)
        acc_imag = jnp.where(first, edge, acc_imag)
        spectrum = jnp.concatenate([acc_real, acc_imag], axis=0)
        spec_hi, spec_lo = split_bf16(spectrum)
        conv = dot(inv, jnp.concatenate([spec_hi, spec_lo, spec_hi], axis=0))
        gated = query_ref[table] * (conv + skip_ref[...] * carried_ref[table].astype(jnp.float32))
        out_ref[table] = gated.astype(out_ref.dtype)


def fused_conv(piece, basis_spec, out_cols, query_gate, carried, skip):
    tables, rows, width = carried.shape
    block_total = basis_spec.shape[0]
    basis_hi, basis_lo = split_bf16(basis_spec)
    basis = jnp.concatenate([basis_hi, basis_hi, basis_lo], axis=2)
    fwd, inv = dft_tables(rows)
    fwd = np.concatenate([fwd[0], fwd[1]], axis=1)
    inv = np.concatenate([inv[0], inv[0], inv[1]], axis=1)
    lanes = 768 if width % 768 == 0 else width
    tile3 = lambda i: (0, 0, i)
    return pl.pallas_call(
        conv_kernel,
        grid=(width // lanes,),
        in_specs=[
            pl.BlockSpec((tables, piece.shape[1], lanes), tile3),
            pl.BlockSpec(basis.shape, lambda i: (0, 0, 0)),
            pl.BlockSpec((out_cols.shape[0], lanes), lambda i: (0, i)),
            pl.BlockSpec((tables, rows, lanes), tile3),
            pl.BlockSpec((tables, rows, lanes), tile3),
            pl.BlockSpec((1, lanes), lambda i: (0, i)),
            pl.BlockSpec(fwd.shape, lambda i: (0, 0)),
            pl.BlockSpec(inv.shape, lambda i: (0, 0)),
        ],
        out_specs=pl.BlockSpec((tables, rows, lanes), tile3),
        out_shape=jax.ShapeDtypeStruct((tables, rows, width), jnp.bfloat16),
        scratch_shapes=[pltpu.VMEM((block_total, 2 * rows, lanes), jnp.float32)],
        compiler_params=pltpu.CompilerParams(vmem_limit_bytes=48 * 1024 * 1024),
    )(piece, basis, out_cols, query_gate, carried, skip.reshape(1, width), jnp.asarray(fwd), jnp.asarray(inv))


def shards(
    tokens,
    in_weight,
    short_weight,
    basis_in,
    basis_bias,
    basis_mid,
    basis_shift,
    response_out,
    skip_gain,
    block_counts,
):
    seq_dev, block_len, width = tokens.shape
    local_ch = skip_gain.shape[0]
    params = jnp.concatenate(
        [response_out.reshape(2 * response_out.shape[1], local_ch), skip_gain[None, :]], axis=0
    )
    parts = lax.axis_size("groups") * lax.axis_size("seq")
    part = lax.axis_index("groups") * lax.axis_size("seq") + lax.axis_index("seq")
    part_cols = local_ch // parts
    mine = lax.dynamic_slice_in_dim(params, part * part_cols, part_cols, axis=1)
    across = lax.all_gather(mine, "fsdp", axis=0, tiled=False)
    gathered = lax.all_gather(across, ("groups", "seq"), axis=0, tiled=False)
    gathered = jnp.transpose(gathered, (2, 1, 0, 3)).reshape(params.shape[0], width)
    seq_count = lax.axis_size("seq")
    position = lax.axis_index("seq")
    total_len = float(seq_count * block_len)
    forward = forward_table(block_len)
    forward_half = forward[:, :block_len]
    inverse = inverse_table(block_len)
    circular = jnp.arange(2 * block_len, dtype=jnp.int32)
    wrapped = jnp.where(circular < block_len, circular, circular - 2 * block_len)

    block_total = seq_count
    offsets = (position - jnp.arange(block_total, dtype=jnp.int32)) * block_len
    lag_values = (offsets[:, None] + wrapped[None, :]).reshape(-1)
    basis_rows = filter_basis(lag_values, total_len, basis_in, basis_bias, basis_mid, basis_shift)
    ahead_mask = (lag_values >= 0).astype(jnp.float32)[:, None]
    paired = jnp.concatenate([basis_rows * ahead_mask, basis_rows * (1.0 - ahead_mask)], axis=1)
    paired = paired.reshape(block_total, 2 * block_len, paired.shape[-1])
    basis_spec = jnp.einsum("gf,bfk->bgk", forward, paired, precision=lax.Precision.HIGHEST)
    group_tokens = lax.all_gather(tokens, "fsdp", axis=0, tiled=True)
    group_tokens, basis_spec, gathered = lax.optimization_barrier((group_tokens, basis_spec, gathered))
    stacked_out = gathered[:-1]
    full_skip = gathered[-1]
    group_rows = group_tokens.shape[0]
    local_cols = in_weight.shape[1]
    partial = jnp.dot(
        group_tokens.reshape(group_rows * block_len, width),
        in_weight,
        preferred_element_type=jnp.float32,
    ).astype(jnp.bfloat16)
    partial = partial.reshape(group_rows, block_len, local_cols)
    projected = lax.all_to_all(partial, "fsdp", 0, 2, tiled=True)
    padded = padded_2(projected, (("seq", 1),), 1)
    shorted = (
        short_weight[0] * padded[:, :-2]
        + short_weight[1] * padded[:, 1:-1]
        + short_weight[2] * padded[:, 2:]
    )
    query_gate = shorted[:, :, :width]
    key_part = shorted[:, :, width : 2 * width]
    value_part = shorted[:, :, 2 * width :]
    valid_mask = (jnp.arange(block_len, dtype=jnp.int32)[None, :] < block_counts).astype(
        jnp.float32
    )
    carried = (key_part * value_part * valid_mask[:, :, None]).astype(jnp.bfloat16)
    piece = lax.all_gather(carried, "seq", axis=1, tiled=True)

    return fused_conv(piece, basis_spec, stacked_out, query_gate, carried, full_skip)


def solution(mesh):
    placed = (
        P(("groups", "fsdp"), "seq", None),
        P(None, "fsdp"),
        P(),
        P(),
        P(),
        P(),
        P(),
        P(None, None, "fsdp"),
        P("fsdp"),
        P(("groups", "fsdp"), "seq"),
    )
    return jax.shard_map(
        shards,
        mesh=mesh,
        in_specs=placed,
        out_specs=P(("groups", "fsdp"), "seq", None),
        check_vma=False,
    )
```

```python
import jax
import ml_dtypes
import numpy as np
import jax.numpy as jnp
from jax import lax
from jax.sharding import PartitionSpec as P
from jax.experimental import pallas as pl
from jax.experimental.pallas import tpu as pltpu


def padded_2(cells, sides, width):
    for axis, dim in sides:
        count = lax.axis_size(axis)
        ends = count - 1
        head = lax.slice_in_dim(cells, 0, width, axis=dim)
        tail = lax.slice_in_dim(cells, cells.shape[dim] - width, cells.shape[dim], axis=dim)
        cells = jnp.concatenate(
            [
                lax.ppermute(tail, axis, [(i, (i + 1) % count) for i in range(ends)]),
                cells,
                lax.ppermute(head, axis, [((i + 1) % count, i) for i in range(ends)]),
            ],
            axis=dim,
        )
    return cells


def gather_by_permutes(values, axis):
    count = lax.axis_size(axis)
    own = lax.axis_index(axis)
    received = [values]
    for shift in range(1, count):
        received.append(
            lax.ppermute(values, axis, [(i, (i + shift) % count) for i in range(count)])
        )
    stacked = jnp.stack(received)
    sources = (own - jnp.arange(count, dtype=jnp.int32)) % count
    order = jnp.argsort(sources)
    return jnp.take(stacked, order, axis=0)


def filter_basis(lag_values, total_len, basis_in, basis_bias, basis_mid, basis_shift):
    band_count = (basis_in.shape[0] - 1) // 2
    distance = jnp.abs(lag_values)
    periods = (2 ** (jnp.arange(band_count, dtype=jnp.int32) + 2) + 1).astype(jnp.int32)
    angles = (
        2.0
        * jnp.pi
        * (distance[:, None] % periods[None, :]).astype(jnp.float32)
        / periods[None, :].astype(jnp.float32)
    )
    linear = distance.astype(jnp.float32)[:, None] / total_len
    encoded = jnp.concatenate([linear, jnp.cos(angles), jnp.sin(angles)], axis=1)
    hidden = jnp.sin(jnp.dot(encoded, basis_in, precision=lax.Precision.HIGHEST) + basis_bias)
    return jnp.sin(jnp.dot(hidden, basis_mid, precision=lax.Precision.HIGHEST) + basis_shift)


def forward_table(block_len):
    period = 2 * block_len
    frequency = jnp.arange(block_len, dtype=jnp.int32)[:, None]
    samples = jnp.arange(period, dtype=jnp.int32)[None, :]
    phases = 2.0 * jnp.pi / period * (frequency * samples % period).astype(jnp.float32)
    alternate = (1 - 2 * (samples % 2)).astype(jnp.float32)
    real_rows = jnp.cos(phases)
    imag_rows = jnp.where(frequency == 0, alternate, -jnp.sin(phases))
    return jnp.concatenate([real_rows, imag_rows], axis=0)


def inverse_table(block_len):
    period = 2 * block_len
    places = jnp.arange(block_len, dtype=jnp.int32)[:, None]
    frequency = jnp.arange(block_len, dtype=jnp.int32)[None, :]
    phases = 2.0 * jnp.pi / period * (places * frequency % period).astype(jnp.float32)
    alternate = (1 - 2 * (places % 2)).astype(jnp.float32)
    real_cols = jnp.where(frequency == 0, 1.0, 2.0 * jnp.cos(phases)) / period
    imag_cols = jnp.where(frequency == 0, alternate, -2.0 * jnp.sin(phases)) / period
    return jnp.concatenate([real_cols, imag_cols], axis=1)


def packed_product(response, signal, block_len):
    first_slot = (jnp.arange(block_len) == 0)[:, None]
    resp_real = response[..., :block_len, :]
    resp_imag = response[..., block_len:, :]
    sig_real = signal[..., :block_len, :]
    sig_imag = signal[..., block_len:, :]
    cross_term = resp_imag * sig_imag
    prod_real = resp_real * sig_real - jnp.where(first_slot, 0.0, cross_term)
    prod_imag = jnp.where(first_slot, cross_term, resp_real * sig_imag + resp_imag * sig_real)
    return jnp.concatenate([prod_real, prod_imag], axis=-2)


def split_bf16(values):
    high = values.astype(jnp.bfloat16)
    return high, (values - high.astype(jnp.float32)).astype(jnp.bfloat16)


def split_table(values):
    high = values.astype(ml_dtypes.bfloat16)
    low = (values - high.astype(np.float64)).astype(ml_dtypes.bfloat16)
    return np.stack([high, low])


def dft_tables(block_len):
    period = 2 * block_len
    frequency = np.arange(block_len)[:, None]
    samples = np.arange(block_len)[None, :]
    phases = 2.0 * np.pi / period * (frequency * samples % period)
    alternate = (1 - 2 * (samples % 2)).astype(np.float64)
    real_rows = np.cos(phases)
    imag_rows = np.where(frequency == 0, alternate, -np.sin(phases))
    forward = np.concatenate([real_rows, imag_rows], axis=0)
    places = np.arange(block_len)[:, None]
    freq = np.arange(block_len)[None, :]
    phases = 2.0 * np.pi / period * (places * freq % period)
    alt = (1 - 2 * (places % 2)).astype(np.float64)
    real_cols = np.where(freq == 0, 1.0, 2.0 * np.cos(phases)) / period
    imag_cols = np.where(freq == 0, alt, -2.0 * np.sin(phases)) / period
    inverse = np.concatenate([np.broadcast_to(real_cols, (block_len, block_len)), imag_cols], axis=1)
    return split_table(forward), split_table(inverse)


def conv_kernel(
    piece_ref, basis_ref, out_cols_ref, query_ref, carried_ref, skip_ref, fwd_ref, inv_ref,
    out_ref, resp_ref,
):
    tables, rows, lanes = carried_ref.shape
    block_total = resp_ref.shape[0]
    cols_hi, cols_lo = split_bf16(out_cols_ref[...])
    cols = jnp.concatenate([cols_hi, cols_lo, cols_hi], axis=0)

    def dot(a, b):
        return jnp.dot(a, b, preferred_element_type=jnp.float32)

    def fill(block, carry):
        resp_ref[block] = dot(basis_ref[block], cols)
        return carry

    lax.fori_loop(0, block_total, fill, 0)
    first = lax.broadcasted_iota(jnp.int32, (rows, lanes), 0) == 0
    fwd = fwd_ref[...]
    inv = inv_ref[...]

    for table in range(tables):

        def one_block(block, acc):
            acc_real, acc_imag, edge = acc
            block_rows = piece_ref[table, pl.ds(pl.multiple_of(block * rows, rows), rows), :]
            signal = dot(fwd, jnp.concatenate([block_rows, block_rows], axis=0))
            response = resp_ref[block]
            resp_real = response[:rows]
            resp_imag = response[rows:]
            sig_real = signal[:rows]
            sig_imag = signal[rows:]
            acc_real = acc_real + (resp_real * sig_real - resp_imag * sig_imag)
            acc_imag = acc_imag + (resp_real * sig_imag + resp_imag * sig_real)
            edge = edge + resp_imag[0:1] * sig_imag[0:1]
            return acc_real, acc_imag, edge

        zeros = jnp.zeros((rows, lanes), jnp.float32)
        acc_real, acc_imag, edge = lax.fori_loop(
            0, block_total, one_block, (zeros, zeros, jnp.zeros((1, lanes), jnp.float32))
        )
        acc_real = acc_real + jnp.where(first, edge, 0.0)
        acc_imag = jnp.where(first, edge, acc_imag)
        spectrum = jnp.concatenate([acc_real, acc_imag], axis=0)
        spec_hi, spec_lo = split_bf16(spectrum)
        conv = dot(inv, jnp.concatenate([spec_hi, spec_lo, spec_hi], axis=0))
        gated = query_ref[table] * (conv + skip_ref[...] * carried_ref[table].astype(jnp.float32))
        out_ref[table] = gated.astype(out_ref.dtype)


def fused_conv(piece, basis_spec, out_cols, query_gate, carried, skip):
    tables, rows, width = carried.shape
    block_total = basis_spec.shape[0]
    basis_hi, basis_lo = split_bf16(basis_spec)
    basis = jnp.concatenate([basis_hi, basis_hi, basis_lo], axis=2)
    fwd, inv = dft_tables(rows)
    fwd = np.concatenate([fwd[0], fwd[1]], axis=1)
    inv = np.concatenate([inv[0], inv[0], inv[1]], axis=1)
    lanes = 768 if width % 768 == 0 else width
    tile3 = lambda i: (0, 0, i)
    return pl.pallas_call(
        conv_kernel,
        grid=(width // lanes,),
        in_specs=[
            pl.BlockSpec((tables, piece.shape[1], lanes), tile3),
            pl.BlockSpec(basis.shape, lambda i: (0, 0, 0)),
            pl.BlockSpec((out_cols.shape[0], lanes), lambda i: (0, i)),
            pl.BlockSpec((tables, rows, lanes), tile3),
            pl.BlockSpec((tables, rows, lanes), tile3),
            pl.BlockSpec((1, lanes), lambda i: (0, i)),
            pl.BlockSpec(fwd.shape, lambda i: (0, 0)),
            pl.BlockSpec(inv.shape, lambda i: (0, 0)),
        ],
        out_specs=pl.BlockSpec((tables, rows, lanes), tile3),
        out_shape=jax.ShapeDtypeStruct((tables, rows, width), jnp.bfloat16),
        scratch_shapes=[pltpu.VMEM((block_total, 2 * rows, lanes), jnp.float32)],
        compiler_params=pltpu.CompilerParams(vmem_limit_bytes=48 * 1024 * 1024),
    )(piece, basis, out_cols, query_gate, carried, skip.reshape(1, width), jnp.asarray(fwd), jnp.asarray(inv))


def shards(
    tokens,
    in_weight,
    short_weight,
    basis_in,
    basis_bias,
    basis_mid,
    basis_shift,
    response_out,
    skip_gain,
    block_counts,
):
    seq_dev, block_len, width = tokens.shape
    local_ch = skip_gain.shape[0]
    params = jnp.concatenate(
        [response_out.reshape(2 * response_out.shape[1], local_ch), skip_gain[None, :]], axis=0
    )
    parts = lax.axis_size("groups") * lax.axis_size("seq")
    part = lax.axis_index("groups") * lax.axis_size("seq") + lax.axis_index("seq")
    part_cols = local_ch // parts
    mine = lax.dynamic_slice_in_dim(params, part * part_cols, part_cols, axis=1)
    across = lax.all_gather(mine, "fsdp", axis=0, tiled=False)
    gathered = lax.all_gather(across, ("groups", "seq"), axis=0, tiled=False)
    gathered = jnp.transpose(gathered, (2, 1, 0, 3)).reshape(params.shape[0], width)
    seq_count = lax.axis_size("seq")
    position = lax.axis_index("seq")
    total_len = float(seq_count * block_len)
    forward = forward_table(block_len)
    forward_half = forward[:, :block_len]
    inverse = inverse_table(block_len)
    circular = jnp.arange(2 * block_len, dtype=jnp.int32)
    wrapped = jnp.where(circular < block_len, circular, circular - 2 * block_len)

    block_total = seq_count
    offsets = (position - jnp.arange(block_total, dtype=jnp.int32)) * block_len
    lag_values = (offsets[:, None] + wrapped[None, :]).reshape(-1)
    basis_rows = filter_basis(lag_values, total_len, basis_in, basis_bias, basis_mid, basis_shift)
    ahead_mask = (lag_values >= 0).astype(jnp.float32)[:, None]
    paired = jnp.concatenate([basis_rows * ahead_mask, basis_rows * (1.0 - ahead_mask)], axis=1)
    paired = paired.reshape(block_total, 2 * block_len, paired.shape[-1])
    basis_spec = jnp.einsum("gf,bfk->bgk", forward, paired, precision=lax.Precision.HIGHEST)
    group_tokens = lax.all_gather(tokens, "fsdp", axis=0, tiled=True)
    group_tokens, basis_spec, gathered = lax.optimization_barrier((group_tokens, basis_spec, gathered))
    stacked_out = gathered[:-1]
    full_skip = gathered[-1]
    local_cols = in_weight.shape[1]
    fsdp_count = lax.axis_size("fsdp")
    grouped = group_tokens.reshape(fsdp_count, seq_dev, block_len, width)
    partials = []
    for table in range(seq_dev):
        partial = jnp.dot(
            grouped[:, table].reshape(fsdp_count * block_len, width),
            in_weight,
            preferred_element_type=jnp.float32,
        ).astype(jnp.bfloat16)
        partials.append(partial.reshape(fsdp_count, block_len, local_cols))
    outputs = []
    previous = None
    for table in range(seq_dev):
        partial = partials[table]
        if previous is not None:
            partial, previous = lax.optimization_barrier((partial, previous))
        projected = lax.all_to_all(partial, "fsdp", 0, 2, tiled=True)
        if outputs:
            projected, outputs[-1] = lax.optimization_barrier((projected, outputs[-1]))
        padded = padded_2(projected, (("seq", 1),), 1)
        shorted = (
            short_weight[0] * padded[:, :-2]
            + short_weight[1] * padded[:, 1:-1]
            + short_weight[2] * padded[:, 2:]
        )
        query_gate = shorted[:, :, :width]
        key_part = shorted[:, :, width : 2 * width]
        value_part = shorted[:, :, 2 * width :]
        valid_mask = (
            jnp.arange(block_len, dtype=jnp.int32)[None, :] < block_counts[table : table + 1]
        ).astype(jnp.float32)
        carried = (key_part * value_part * valid_mask[:, :, None]).astype(jnp.bfloat16)
        piece = lax.all_gather(carried, "seq", axis=1, tiled=True)
        previous = carried
        outputs.append(fused_conv(piece, basis_spec, stacked_out, query_gate, carried, full_skip))
    return jnp.concatenate(outputs, axis=0)


def solution(mesh):
    placed = (
        P(("groups", "fsdp"), "seq", None),
        P(None, "fsdp"),
        P(),
        P(),
        P(),
        P(),
        P(),
        P(None, None, "fsdp"),
        P("fsdp"),
        P(("groups", "fsdp"), "seq"),
    )
    return jax.shard_map(
        shards,
        mesh=mesh,
        in_specs=placed,
        out_specs=P(("groups", "fsdp"), "seq", None),
        check_vma=False,
    )
```

```python
import jax
import ml_dtypes
import numpy as np
import jax.numpy as jnp
from jax import lax
from jax.sharding import PartitionSpec as P
from jax.experimental import pallas as pl
from jax.experimental.pallas import tpu as pltpu


def padded_2(cells, sides, width):
    for axis, dim in sides:
        count = lax.axis_size(axis)
        ends = count - 1
        head = lax.slice_in_dim(cells, 0, width, axis=dim)
        tail = lax.slice_in_dim(cells, cells.shape[dim] - width, cells.shape[dim], axis=dim)
        cells = jnp.concatenate(
            [
                lax.ppermute(tail, axis, [(i, (i + 1) % count) for i in range(ends)]),
                cells,
                lax.ppermute(head, axis, [((i + 1) % count, i) for i in range(ends)]),
            ],
            axis=dim,
        )
    return cells


def gather_by_permutes(values, axis):
    count = lax.axis_size(axis)
    own = lax.axis_index(axis)
    received = [values]
    for shift in range(1, count):
        received.append(
            lax.ppermute(values, axis, [(i, (i + shift) % count) for i in range(count)])
        )
    stacked = jnp.stack(received)
    sources = (own - jnp.arange(count, dtype=jnp.int32)) % count
    order = jnp.argsort(sources)
    return jnp.take(stacked, order, axis=0)


def filter_basis(lag_values, total_len, basis_in, basis_bias, basis_mid, basis_shift):
    band_count = (basis_in.shape[0] - 1) // 2
    distance = jnp.abs(lag_values)
    periods = (2 ** (jnp.arange(band_count, dtype=jnp.int32) + 2) + 1).astype(jnp.int32)
    angles = (
        2.0
        * jnp.pi
        * (distance[:, None] % periods[None, :]).astype(jnp.float32)
        / periods[None, :].astype(jnp.float32)
    )
    linear = distance.astype(jnp.float32)[:, None] / total_len
    encoded = jnp.concatenate([linear, jnp.cos(angles), jnp.sin(angles)], axis=1)
    hidden = jnp.sin(jnp.dot(encoded, basis_in, precision=lax.Precision.HIGHEST) + basis_bias)
    return jnp.sin(jnp.dot(hidden, basis_mid, precision=lax.Precision.HIGHEST) + basis_shift)


def forward_table(block_len):
    period = 2 * block_len
    frequency = jnp.arange(block_len, dtype=jnp.int32)[:, None]
    samples = jnp.arange(period, dtype=jnp.int32)[None, :]
    phases = 2.0 * jnp.pi / period * (frequency * samples % period).astype(jnp.float32)
    alternate = (1 - 2 * (samples % 2)).astype(jnp.float32)
    real_rows = jnp.cos(phases)
    imag_rows = jnp.where(frequency == 0, alternate, -jnp.sin(phases))
    return jnp.concatenate([real_rows, imag_rows], axis=0)


def inverse_table(block_len):
    period = 2 * block_len
    places = jnp.arange(block_len, dtype=jnp.int32)[:, None]
    frequency = jnp.arange(block_len, dtype=jnp.int32)[None, :]
    phases = 2.0 * jnp.pi / period * (places * frequency % period).astype(jnp.float32)
    alternate = (1 - 2 * (places % 2)).astype(jnp.float32)
    real_cols = jnp.where(frequency == 0, 1.0, 2.0 * jnp.cos(phases)) / period
    imag_cols = jnp.where(frequency == 0, alternate, -2.0 * jnp.sin(phases)) / period
    return jnp.concatenate([real_cols, imag_cols], axis=1)


def packed_product(response, signal, block_len):
    first_slot = (jnp.arange(block_len) == 0)[:, None]
    resp_real = response[..., :block_len, :]
    resp_imag = response[..., block_len:, :]
    sig_real = signal[..., :block_len, :]
    sig_imag = signal[..., block_len:, :]
    cross_term = resp_imag * sig_imag
    prod_real = resp_real * sig_real - jnp.where(first_slot, 0.0, cross_term)
    prod_imag = jnp.where(first_slot, cross_term, resp_real * sig_imag + resp_imag * sig_real)
    return jnp.concatenate([prod_real, prod_imag], axis=-2)


def split_bf16(values):
    high = values.astype(jnp.bfloat16)
    return high, (values - high.astype(jnp.float32)).astype(jnp.bfloat16)


def split_table(values):
    high = values.astype(ml_dtypes.bfloat16)
    low = (values - high.astype(np.float64)).astype(ml_dtypes.bfloat16)
    return np.stack([high, low])


def dft_tables(block_len):
    period = 2 * block_len
    frequency = np.arange(block_len)[:, None]
    samples = np.arange(block_len)[None, :]
    phases = 2.0 * np.pi / period * (frequency * samples % period)
    alternate = (1 - 2 * (samples % 2)).astype(np.float64)
    real_rows = np.cos(phases)
    imag_rows = np.where(frequency == 0, alternate, -np.sin(phases))
    forward = np.concatenate([real_rows, imag_rows], axis=0)
    places = np.arange(block_len)[:, None]
    freq = np.arange(block_len)[None, :]
    phases = 2.0 * np.pi / period * (places * freq % period)
    alt = (1 - 2 * (places % 2)).astype(np.float64)
    real_cols = np.where(freq == 0, 1.0, 2.0 * np.cos(phases)) / period
    imag_cols = np.where(freq == 0, alt, -2.0 * np.sin(phases)) / period
    inverse = np.concatenate([np.broadcast_to(real_cols, (block_len, block_len)), imag_cols], axis=1)
    return split_table(forward), split_table(inverse)


def conv_kernel(
    piece_ref, basis_ref, out_cols_ref, query_ref, carried_ref, fwd_ref, inv_ref,
    out_ref, resp_ref,
):
    tables, rows, lanes = carried_ref.shape
    block_total = resp_ref.shape[0]
    out_cols = out_cols_ref[...]
    cols_hi, cols_lo = split_bf16(out_cols[:-1])
    skip = out_cols[out_cols.shape[0] - 1 :]
    cols = jnp.concatenate([cols_hi, cols_lo, cols_hi], axis=0)

    def dot(a, b):
        return jnp.dot(a, b, preferred_element_type=jnp.float32)

    def fill(block, carry):
        resp_ref[block] = dot(basis_ref[block], cols)
        return carry

    lax.fori_loop(0, block_total, fill, 0)
    first = lax.broadcasted_iota(jnp.int32, (rows, lanes), 0) == 0
    fwd = fwd_ref[...]
    inv = inv_ref[...]

    for table in range(tables):

        def one_block(block, acc):
            acc_real, acc_imag, edge = acc
            block_rows = piece_ref[table, pl.ds(pl.multiple_of(block * rows, rows), rows), :]
            signal = dot(fwd, jnp.concatenate([block_rows, block_rows], axis=0))
            response = resp_ref[block]
            resp_real = response[:rows]
            resp_imag = response[rows:]
            sig_real = signal[:rows]
            sig_imag = signal[rows:]
            acc_real = acc_real + (resp_real * sig_real - resp_imag * sig_imag)
            acc_imag = acc_imag + (resp_real * sig_imag + resp_imag * sig_real)
            edge = edge + resp_imag[0:1] * sig_imag[0:1]
            return acc_real, acc_imag, edge

        zeros = jnp.zeros((rows, lanes), jnp.float32)
        acc_real, acc_imag, edge = lax.fori_loop(
            0, block_total, one_block, (zeros, zeros, jnp.zeros((1, lanes), jnp.float32))
        )
        acc_real = acc_real + jnp.where(first, edge, 0.0)
        acc_imag = jnp.where(first, edge, acc_imag)
        spectrum = jnp.concatenate([acc_real, acc_imag], axis=0)
        spec_hi, spec_lo = split_bf16(spectrum)
        conv = dot(inv, jnp.concatenate([spec_hi, spec_lo, spec_hi], axis=0))
        gated = query_ref[table] * (conv + skip * carried_ref[table].astype(jnp.float32))
        out_ref[table] = gated.astype(out_ref.dtype)


def fused_conv(piece, basis_spec, out_cols, query_gate, carried):
    tables, rows, width = carried.shape
    block_total = basis_spec.shape[0]
    basis_hi, basis_lo = split_bf16(basis_spec)
    basis = jnp.concatenate([basis_hi, basis_hi, basis_lo], axis=2)
    fwd, inv = dft_tables(rows)
    fwd = np.concatenate([fwd[0], fwd[1]], axis=1)
    inv = np.concatenate([inv[0], inv[0], inv[1]], axis=1)
    lanes = 768 if width % 768 == 0 else width
    tile3 = lambda i: (0, 0, i)
    return pl.pallas_call(
        conv_kernel,
        grid=(width // lanes,),
        in_specs=[
            pl.BlockSpec((tables, piece.shape[1], lanes), tile3),
            pl.BlockSpec(basis.shape, lambda i: (0, 0, 0)),
            pl.BlockSpec((out_cols.shape[0], lanes), lambda i: (0, i)),
            pl.BlockSpec((tables, rows, lanes), tile3),
            pl.BlockSpec((tables, rows, lanes), tile3),
            pl.BlockSpec(fwd.shape, lambda i: (0, 0)),
            pl.BlockSpec(inv.shape, lambda i: (0, 0)),
        ],
        out_specs=pl.BlockSpec((tables, rows, lanes), tile3),
        out_shape=jax.ShapeDtypeStruct((tables, rows, width), jnp.bfloat16),
        scratch_shapes=[pltpu.VMEM((block_total, 2 * rows, lanes), jnp.float32)],
        compiler_params=pltpu.CompilerParams(vmem_limit_bytes=48 * 1024 * 1024),
    )(piece, basis, out_cols, query_gate, carried, jnp.asarray(fwd), jnp.asarray(inv))


def shards(
    tokens,
    in_weight,
    short_weight,
    basis_in,
    basis_bias,
    basis_mid,
    basis_shift,
    response_out,
    skip_gain,
    block_counts,
):
    seq_dev, block_len, width = tokens.shape
    local_ch = skip_gain.shape[0]
    params = jnp.concatenate(
        [response_out.reshape(2 * response_out.shape[1], local_ch), skip_gain[None, :]], axis=0
    )
    gathered = gather_by_permutes(params, "fsdp")
    gathered = jnp.transpose(gathered, (1, 0, 2)).reshape(params.shape[0], width)
    seq_count = lax.axis_size("seq")
    position = lax.axis_index("seq")
    total_len = float(seq_count * block_len)
    forward = forward_table(block_len)
    forward_half = forward[:, :block_len]
    inverse = inverse_table(block_len)
    circular = jnp.arange(2 * block_len, dtype=jnp.int32)
    wrapped = jnp.where(circular < block_len, circular, circular - 2 * block_len)

    block_total = seq_count
    offsets = (position - jnp.arange(block_total, dtype=jnp.int32)) * block_len
    lag_values = (offsets[:, None] + wrapped[None, :]).reshape(-1)
    basis_rows = filter_basis(lag_values, total_len, basis_in, basis_bias, basis_mid, basis_shift)
    ahead_mask = (lag_values >= 0).astype(jnp.float32)[:, None]
    paired = jnp.concatenate([basis_rows * ahead_mask, basis_rows * (1.0 - ahead_mask)], axis=1)
    paired = paired.reshape(block_total, 2 * block_len, paired.shape[-1])
    basis_spec = jnp.einsum("gf,bfk->bgk", forward, paired, precision=lax.Precision.HIGHEST)
    group_tokens = lax.all_gather(tokens, "fsdp", axis=0, tiled=True)
    group_tokens, basis_spec = lax.optimization_barrier((group_tokens, basis_spec))
    group_rows = group_tokens.shape[0]
    local_cols = in_weight.shape[1]
    partial = jnp.dot(
        group_tokens.reshape(group_rows * block_len, width),
        in_weight,
        preferred_element_type=jnp.float32,
    ).astype(jnp.bfloat16)
    partial = partial.reshape(group_rows, block_len, local_cols)
    projected = lax.all_to_all(partial, "fsdp", 0, 2, tiled=True)
    padded = padded_2(projected, (("seq", 1),), 1)
    shorted = (
        short_weight[0] * padded[:, :-2]
        + short_weight[1] * padded[:, 1:-1]
        + short_weight[2] * padded[:, 2:]
    )
    query_gate = shorted[:, :, :width]
    key_part = shorted[:, :, width : 2 * width]
    value_part = shorted[:, :, 2 * width :]
    valid_mask = (jnp.arange(block_len, dtype=jnp.int32)[None, :] < block_counts).astype(
        jnp.float32
    )
    carried = (key_part * value_part * valid_mask[:, :, None]).astype(jnp.bfloat16)
    piece = lax.all_gather(carried, "seq", axis=1, tiled=True)

    return fused_conv(piece, basis_spec, gathered, query_gate, carried)


def solution(mesh):
    placed = (
        P(("groups", "fsdp"), "seq", None),
        P(None, "fsdp"),
        P(),
        P(),
        P(),
        P(),
        P(),
        P(None, None, "fsdp"),
        P("fsdp"),
        P(("groups", "fsdp"), "seq"),
    )
    return jax.shard_map(
        shards,
        mesh=mesh,
        in_specs=placed,
        out_specs=P(("groups", "fsdp"), "seq", None),
        check_vma=False,
    )
```

```python
import jax
import ml_dtypes
import numpy as np
import jax.numpy as jnp
from jax import lax
from jax.sharding import PartitionSpec as P
from jax.experimental import pallas as pl
from jax.experimental.pallas import tpu as pltpu


def padded_2(cells, sides, width):
    for axis, dim in sides:
        count = lax.axis_size(axis)
        ends = count - 1
        head = lax.slice_in_dim(cells, 0, width, axis=dim)
        tail = lax.slice_in_dim(cells, cells.shape[dim] - width, cells.shape[dim], axis=dim)
        cells = jnp.concatenate(
            [
                lax.ppermute(tail, axis, [(i, (i + 1) % count) for i in range(ends)]),
                cells,
                lax.ppermute(head, axis, [((i + 1) % count, i) for i in range(ends)]),
            ],
            axis=dim,
        )
    return cells


def gather_by_permutes(values, axis):
    count = lax.axis_size(axis)
    own = lax.axis_index(axis)
    received = [values]
    for shift in range(1, count):
        received.append(
            lax.ppermute(values, axis, [(i, (i + shift) % count) for i in range(count)])
        )
    stacked = jnp.stack(received)
    sources = (own - jnp.arange(count, dtype=jnp.int32)) % count
    order = jnp.argsort(sources)
    return jnp.take(stacked, order, axis=0)


def filter_basis(lag_values, total_len, basis_in, basis_bias, basis_mid, basis_shift):
    band_count = (basis_in.shape[0] - 1) // 2
    distance = jnp.abs(lag_values)
    periods = (2 ** (jnp.arange(band_count, dtype=jnp.int32) + 2) + 1).astype(jnp.int32)
    angles = (
        2.0
        * jnp.pi
        * (distance[:, None] % periods[None, :]).astype(jnp.float32)
        / periods[None, :].astype(jnp.float32)
    )
    linear = distance.astype(jnp.float32)[:, None] / total_len
    encoded = jnp.concatenate([linear, jnp.cos(angles), jnp.sin(angles)], axis=1)
    hidden = jnp.sin(jnp.dot(encoded, basis_in, precision=lax.Precision.HIGHEST) + basis_bias)
    return jnp.sin(jnp.dot(hidden, basis_mid, precision=lax.Precision.HIGHEST) + basis_shift)


def forward_table(block_len):
    period = 2 * block_len
    frequency = jnp.arange(block_len, dtype=jnp.int32)[:, None]
    samples = jnp.arange(period, dtype=jnp.int32)[None, :]
    phases = 2.0 * jnp.pi / period * (frequency * samples % period).astype(jnp.float32)
    alternate = (1 - 2 * (samples % 2)).astype(jnp.float32)
    real_rows = jnp.cos(phases)
    imag_rows = jnp.where(frequency == 0, alternate, -jnp.sin(phases))
    return jnp.concatenate([real_rows, imag_rows], axis=0)


def inverse_table(block_len):
    period = 2 * block_len
    places = jnp.arange(block_len, dtype=jnp.int32)[:, None]
    frequency = jnp.arange(block_len, dtype=jnp.int32)[None, :]
    phases = 2.0 * jnp.pi / period * (places * frequency % period).astype(jnp.float32)
    alternate = (1 - 2 * (places % 2)).astype(jnp.float32)
    real_cols = jnp.where(frequency == 0, 1.0, 2.0 * jnp.cos(phases)) / period
    imag_cols = jnp.where(frequency == 0, alternate, -2.0 * jnp.sin(phases)) / period
    return jnp.concatenate([real_cols, imag_cols], axis=1)


def packed_product(response, signal, block_len):
    first_slot = (jnp.arange(block_len) == 0)[:, None]
    resp_real = response[..., :block_len, :]
    resp_imag = response[..., block_len:, :]
    sig_real = signal[..., :block_len, :]
    sig_imag = signal[..., block_len:, :]
    cross_term = resp_imag * sig_imag
    prod_real = resp_real * sig_real - jnp.where(first_slot, 0.0, cross_term)
    prod_imag = jnp.where(first_slot, cross_term, resp_real * sig_imag + resp_imag * sig_real)
    return jnp.concatenate([prod_real, prod_imag], axis=-2)


def split_bf16(values):
    high = values.astype(jnp.bfloat16)
    return high, (values - high.astype(jnp.float32)).astype(jnp.bfloat16)


def split_table(values):
    high = values.astype(ml_dtypes.bfloat16)
    low = (values - high.astype(np.float64)).astype(ml_dtypes.bfloat16)
    return np.stack([high, low])


def dft_tables(block_len):
    period = 2 * block_len
    frequency = np.arange(block_len)[:, None]
    samples = np.arange(block_len)[None, :]
    phases = 2.0 * np.pi / period * (frequency * samples % period)
    alternate = (1 - 2 * (samples % 2)).astype(np.float64)
    real_rows = np.cos(phases)
    imag_rows = np.where(frequency == 0, alternate, -np.sin(phases))
    forward = np.concatenate([real_rows, imag_rows], axis=0)
    places = np.arange(block_len)[:, None]
    freq = np.arange(block_len)[None, :]
    phases = 2.0 * np.pi / period * (places * freq % period)
    alt = (1 - 2 * (places % 2)).astype(np.float64)
    real_cols = np.where(freq == 0, 1.0, 2.0 * np.cos(phases)) / period
    imag_cols = np.where(freq == 0, alt, -2.0 * np.sin(phases)) / period
    inverse = np.concatenate([np.broadcast_to(real_cols, (block_len, block_len)), imag_cols], axis=1)
    return split_table(forward), split_table(inverse)


def conv_kernel(
    piece_ref, basis_ref, out_cols_ref, query_ref, carried_ref, fwd_ref, inv_ref,
    out_ref, resp_ref,
):
    tables, rows, lanes = carried_ref.shape
    block_total = resp_ref.shape[0]
    out_cols = out_cols_ref[...]
    cols_hi, cols_lo = split_bf16(out_cols[:-1])
    skip = out_cols[out_cols.shape[0] - 1 :]
    cols = jnp.concatenate([cols_hi, cols_lo, cols_hi], axis=0)

    def dot(a, b):
        return jnp.dot(a, b, preferred_element_type=jnp.float32)

    def fill(block, carry):
        resp_ref[block] = dot(basis_ref[block], cols)
        return carry

    lax.fori_loop(0, block_total, fill, 0)
    first = lax.broadcasted_iota(jnp.int32, (rows, lanes), 0) == 0
    fwd = fwd_ref[...]
    inv = inv_ref[...]

    for table in range(tables):

        def one_block(block, acc):
            acc_real, acc_imag, edge = acc
            block_rows = piece_ref[block, table]
            signal = dot(fwd, jnp.concatenate([block_rows, block_rows], axis=0))
            response = resp_ref[block]
            resp_real = response[:rows]
            resp_imag = response[rows:]
            sig_real = signal[:rows]
            sig_imag = signal[rows:]
            acc_real = acc_real + (resp_real * sig_real - resp_imag * sig_imag)
            acc_imag = acc_imag + (resp_real * sig_imag + resp_imag * sig_real)
            edge = edge + resp_imag[0:1] * sig_imag[0:1]
            return acc_real, acc_imag, edge

        zeros = jnp.zeros((rows, lanes), jnp.float32)
        acc_real, acc_imag, edge = lax.fori_loop(
            0, block_total, one_block, (zeros, zeros, jnp.zeros((1, lanes), jnp.float32))
        )
        acc_real = acc_real + jnp.where(first, edge, 0.0)
        acc_imag = jnp.where(first, edge, acc_imag)
        spectrum = jnp.concatenate([acc_real, acc_imag], axis=0)
        spec_hi, spec_lo = split_bf16(spectrum)
        conv = dot(inv, jnp.concatenate([spec_hi, spec_lo, spec_hi], axis=0))
        gated = query_ref[table] * (conv + skip * carried_ref[table].astype(jnp.float32))
        out_ref[table] = gated.astype(out_ref.dtype)


def fused_conv(piece, basis_spec, out_cols, query_gate, carried):
    tables, rows, width = carried.shape
    block_total = basis_spec.shape[0]
    basis_hi, basis_lo = split_bf16(basis_spec)
    basis = jnp.concatenate([basis_hi, basis_hi, basis_lo], axis=2)
    fwd, inv = dft_tables(rows)
    fwd = np.concatenate([fwd[0], fwd[1]], axis=1)
    inv = np.concatenate([inv[0], inv[0], inv[1]], axis=1)
    lanes = 768 if width % 768 == 0 else width
    tile3 = lambda i: (0, 0, i)
    return pl.pallas_call(
        conv_kernel,
        grid=(width // lanes,),
        in_specs=[
            pl.BlockSpec((block_total, tables, rows, lanes), lambda i: (0, 0, 0, i)),
            pl.BlockSpec(basis.shape, lambda i: (0, 0, 0)),
            pl.BlockSpec((out_cols.shape[0], lanes), lambda i: (0, i)),
            pl.BlockSpec((tables, rows, lanes), tile3),
            pl.BlockSpec((tables, rows, lanes), tile3),
            pl.BlockSpec(fwd.shape, lambda i: (0, 0)),
            pl.BlockSpec(inv.shape, lambda i: (0, 0)),
        ],
        out_specs=pl.BlockSpec((tables, rows, lanes), tile3),
        out_shape=jax.ShapeDtypeStruct((tables, rows, width), jnp.bfloat16),
        scratch_shapes=[pltpu.VMEM((block_total, 2 * rows, lanes), jnp.float32)],
        compiler_params=pltpu.CompilerParams(vmem_limit_bytes=48 * 1024 * 1024),
    )(piece, basis, out_cols, query_gate, carried, jnp.asarray(fwd), jnp.asarray(inv))


def shards(
    tokens,
    in_weight,
    short_weight,
    basis_in,
    basis_bias,
    basis_mid,
    basis_shift,
    response_out,
    skip_gain,
    block_counts,
):
    seq_dev, block_len, width = tokens.shape
    local_ch = skip_gain.shape[0]
    params = jnp.concatenate(
        [response_out.reshape(2 * response_out.shape[1], local_ch), skip_gain[None, :]], axis=0
    )
    parts = lax.axis_size("groups") * lax.axis_size("seq")
    part = lax.axis_index("groups") * lax.axis_size("seq") + lax.axis_index("seq")
    part_cols = local_ch // parts
    mine = lax.dynamic_slice_in_dim(params, part * part_cols, part_cols, axis=1)
    across = lax.all_gather(mine, "fsdp", axis=0, tiled=False)
    gathered = lax.all_gather(across, ("groups", "seq"), axis=0, tiled=False)
    gathered = jnp.transpose(gathered, (2, 1, 0, 3)).reshape(params.shape[0], width)
    seq_count = lax.axis_size("seq")
    position = lax.axis_index("seq")
    total_len = float(seq_count * block_len)
    forward = forward_table(block_len)
    forward_half = forward[:, :block_len]
    inverse = inverse_table(block_len)
    circular = jnp.arange(2 * block_len, dtype=jnp.int32)
    wrapped = jnp.where(circular < block_len, circular, circular - 2 * block_len)

    block_total = seq_count
    chips = seq_count // 2
    chip, core = position // 2, position % 2
    ring = (chip - jnp.arange(chips, dtype=jnp.int32)) % chips
    order = jnp.concatenate([2 * ring + core, 2 * ring + 1 - core])
    offsets = (position - order) * block_len
    lag_values = (offsets[:, None] + wrapped[None, :]).reshape(-1)
    basis_rows = filter_basis(lag_values, total_len, basis_in, basis_bias, basis_mid, basis_shift)
    ahead_mask = (lag_values >= 0).astype(jnp.float32)[:, None]
    paired = jnp.concatenate([basis_rows * ahead_mask, basis_rows * (1.0 - ahead_mask)], axis=1)
    paired = paired.reshape(block_total, 2 * block_len, paired.shape[-1])
    basis_spec = jnp.einsum("gf,bfk->bgk", forward, paired, precision=lax.Precision.HIGHEST)
    group_tokens = lax.all_gather(tokens, "fsdp", axis=0, tiled=True)
    group_tokens, basis_spec, gathered = lax.optimization_barrier((group_tokens, basis_spec, gathered))
    group_rows = group_tokens.shape[0]
    local_cols = in_weight.shape[1]
    partial = jnp.dot(
        group_tokens.reshape(group_rows * block_len, width),
        in_weight,
        preferred_element_type=jnp.float32,
    ).astype(jnp.bfloat16)
    partial = partial.reshape(group_rows, block_len, local_cols)
    projected = lax.all_to_all(partial, "fsdp", 0, 2, tiled=True)
    padded = padded_2(projected, (("seq", 1),), 1)
    shorted = (
        short_weight[0] * padded[:, :-2]
        + short_weight[1] * padded[:, 1:-1]
        + short_weight[2] * padded[:, 2:]
    )
    query_gate = shorted[:, :, :width]
    key_part = shorted[:, :, width : 2 * width]
    value_part = shorted[:, :, 2 * width :]
    valid_mask = (jnp.arange(block_len, dtype=jnp.int32)[None, :] < block_counts).astype(
        jnp.float32
    )
    carried = (key_part * value_part * valid_mask[:, :, None]).astype(jnp.bfloat16)
    same_core = [carried]
    for shift in range(1, chips):
        same_core.append(
            lax.ppermute(
                carried, "seq", [(i, (i + 2 * shift) % seq_count) for i in range(seq_count)]
            )
        )
    same_core = jnp.stack(same_core)
    other_core = lax.ppermute(same_core, "seq", [(i, i ^ 1) for i in range(seq_count)])
    piece = jnp.concatenate([same_core, other_core], axis=0)

    return fused_conv(piece, basis_spec, gathered, query_gate, carried)


def solution(mesh):
    placed = (
        P(("groups", "fsdp"), "seq", None),
        P(None, "fsdp"),
        P(),
        P(),
        P(),
        P(),
        P(),
        P(None, None, "fsdp"),
        P("fsdp"),
        P(("groups", "fsdp"), "seq"),
    )
    return jax.shard_map(
        shards,
        mesh=mesh,
        in_specs=placed,
        out_specs=P(("groups", "fsdp"), "seq", None),
        check_vma=False,
    )
```

```python
import jax
import ml_dtypes
import numpy as np
import jax.numpy as jnp
from jax import lax
from jax.sharding import PartitionSpec as P
from jax.experimental import pallas as pl
from jax.experimental.pallas import tpu as pltpu


def padded_2(cells, sides, width):
    for axis, dim in sides:
        count = lax.axis_size(axis)
        ends = count - 1
        head = lax.slice_in_dim(cells, 0, width, axis=dim)
        tail = lax.slice_in_dim(cells, cells.shape[dim] - width, cells.shape[dim], axis=dim)
        cells = jnp.concatenate(
            [
                lax.ppermute(tail, axis, [(i, (i + 1) % count) for i in range(ends)]),
                cells,
                lax.ppermute(head, axis, [((i + 1) % count, i) for i in range(ends)]),
            ],
            axis=dim,
        )
    return cells


def gather_by_permutes(values, axis):
    count = lax.axis_size(axis)
    own = lax.axis_index(axis)
    received = [values]
    for shift in range(1, count):
        received.append(
            lax.ppermute(values, axis, [(i, (i + shift) % count) for i in range(count)])
        )
    stacked = jnp.stack(received)
    sources = (own - jnp.arange(count, dtype=jnp.int32)) % count
    order = jnp.argsort(sources)
    return jnp.take(stacked, order, axis=0)


def filter_basis(lag_values, total_len, basis_in, basis_bias, basis_mid, basis_shift):
    band_count = (basis_in.shape[0] - 1) // 2
    distance = jnp.abs(lag_values)
    periods = (2 ** (jnp.arange(band_count, dtype=jnp.int32) + 2) + 1).astype(jnp.int32)
    angles = (
        2.0
        * jnp.pi
        * (distance[:, None] % periods[None, :]).astype(jnp.float32)
        / periods[None, :].astype(jnp.float32)
    )
    linear = distance.astype(jnp.float32)[:, None] / total_len
    encoded = jnp.concatenate([linear, jnp.cos(angles), jnp.sin(angles)], axis=1)
    hidden = jnp.sin(jnp.dot(encoded, basis_in, precision=lax.Precision.HIGHEST) + basis_bias)
    return jnp.sin(jnp.dot(hidden, basis_mid, precision=lax.Precision.HIGHEST) + basis_shift)


def forward_table(block_len):
    period = 2 * block_len
    frequency = jnp.arange(block_len, dtype=jnp.int32)[:, None]
    samples = jnp.arange(period, dtype=jnp.int32)[None, :]
    phases = 2.0 * jnp.pi / period * (frequency * samples % period).astype(jnp.float32)
    alternate = (1 - 2 * (samples % 2)).astype(jnp.float32)
    real_rows = jnp.cos(phases)
    imag_rows = jnp.where(frequency == 0, alternate, -jnp.sin(phases))
    return jnp.concatenate([real_rows, imag_rows], axis=0)


def inverse_table(block_len):
    period = 2 * block_len
    places = jnp.arange(block_len, dtype=jnp.int32)[:, None]
    frequency = jnp.arange(block_len, dtype=jnp.int32)[None, :]
    phases = 2.0 * jnp.pi / period * (places * frequency % period).astype(jnp.float32)
    alternate = (1 - 2 * (places % 2)).astype(jnp.float32)
    real_cols = jnp.where(frequency == 0, 1.0, 2.0 * jnp.cos(phases)) / period
    imag_cols = jnp.where(frequency == 0, alternate, -2.0 * jnp.sin(phases)) / period
    return jnp.concatenate([real_cols, imag_cols], axis=1)


def packed_product(response, signal, block_len):
    first_slot = (jnp.arange(block_len) == 0)[:, None]
    resp_real = response[..., :block_len, :]
    resp_imag = response[..., block_len:, :]
    sig_real = signal[..., :block_len, :]
    sig_imag = signal[..., block_len:, :]
    cross_term = resp_imag * sig_imag
    prod_real = resp_real * sig_real - jnp.where(first_slot, 0.0, cross_term)
    prod_imag = jnp.where(first_slot, cross_term, resp_real * sig_imag + resp_imag * sig_real)
    return jnp.concatenate([prod_real, prod_imag], axis=-2)


def split_bf16(values):
    high = values.astype(jnp.bfloat16)
    return high, (values - high.astype(jnp.float32)).astype(jnp.bfloat16)


def split_table(values):
    high = values.astype(ml_dtypes.bfloat16)
    low = (values - high.astype(np.float64)).astype(ml_dtypes.bfloat16)
    return np.stack([high, low])


def dft_tables(block_len):
    period = 2 * block_len
    frequency = np.arange(block_len)[:, None]
    samples = np.arange(block_len)[None, :]
    phases = 2.0 * np.pi / period * (frequency * samples % period)
    alternate = (1 - 2 * (samples % 2)).astype(np.float64)
    real_rows = np.cos(phases)
    imag_rows = np.where(frequency == 0, alternate, -np.sin(phases))
    forward = np.concatenate([real_rows, imag_rows], axis=0)
    places = np.arange(block_len)[:, None]
    freq = np.arange(block_len)[None, :]
    phases = 2.0 * np.pi / period * (places * freq % period)
    alt = (1 - 2 * (places % 2)).astype(np.float64)
    real_cols = np.where(freq == 0, 1.0, 2.0 * np.cos(phases)) / period
    imag_cols = np.where(freq == 0, alt, -2.0 * np.sin(phases)) / period
    inverse = np.concatenate([np.broadcast_to(real_cols, (block_len, block_len)), imag_cols], axis=1)
    return split_table(forward), split_table(inverse)


def conv_body(finish):
    def kernel(*refs):
        if finish:
            (piece_ref, basis_ref, out_cols_ref, spec_in_ref, query_ref, carried_ref,
             fwd_ref, inv_ref, out_ref, resp_ref) = refs
        else:
            piece_ref, basis_ref, out_cols_ref, fwd_ref, out_ref, resp_ref = refs
        block_total, tables, rows, lanes = piece_ref.shape
        out_cols = out_cols_ref[...]
        cols_hi, cols_lo = split_bf16(out_cols[:-1])
        skip = out_cols[out_cols.shape[0] - 1 :]
        cols = jnp.concatenate([cols_hi, cols_lo, cols_hi], axis=0)

        def dot(a, b):
            return jnp.dot(a, b, preferred_element_type=jnp.float32)

        def fill(block, carry):
            resp_ref[block] = dot(basis_ref[block], cols)
            return carry

        lax.fori_loop(0, block_total, fill, 0)
        first = lax.broadcasted_iota(jnp.int32, (rows, lanes), 0) == 0
        fwd = fwd_ref[...]

        for table in range(tables):

            def one_block(block, acc):
                acc_real, acc_imag, edge = acc
                block_rows = piece_ref[block, table]
                signal = dot(fwd, jnp.concatenate([block_rows, block_rows], axis=0))
                response = resp_ref[block]
                resp_real = response[:rows]
                resp_imag = response[rows:]
                sig_real = signal[:rows]
                sig_imag = signal[rows:]
                acc_real = acc_real + (resp_real * sig_real - resp_imag * sig_imag)
                acc_imag = acc_imag + (resp_real * sig_imag + resp_imag * sig_real)
                edge = edge + resp_imag[0:1] * sig_imag[0:1]
                return acc_real, acc_imag, edge

            zeros = jnp.zeros((rows, lanes), jnp.float32)
            acc_real, acc_imag, edge = lax.fori_loop(
                0, block_total, one_block, (zeros, zeros, jnp.zeros((1, lanes), jnp.float32))
            )
            acc_real = acc_real + jnp.where(first, edge, 0.0)
            acc_imag = jnp.where(first, edge, acc_imag)
            spectrum = jnp.concatenate([acc_real, acc_imag], axis=0)
            if not finish:
                out_ref[table] = spectrum
                continue
            spectrum = spectrum + spec_in_ref[table]
            spec_hi, spec_lo = split_bf16(spectrum)
            conv = dot(inv_ref[...], jnp.concatenate([spec_hi, spec_lo, spec_hi], axis=0))
            gated = query_ref[table] * (conv + skip * carried_ref[table].astype(jnp.float32))
            out_ref[table] = gated.astype(out_ref.dtype)

    return kernel


def fused_conv(piece, basis_spec, out_cols, query_gate=None, carried=None, spec_in=None):
    block_total, tables, rows, width = piece.shape
    finish = spec_in is not None
    basis_hi, basis_lo = split_bf16(basis_spec)
    basis = jnp.concatenate([basis_hi, basis_hi, basis_lo], axis=2)
    fwd, inv = dft_tables(rows)
    fwd = np.concatenate([fwd[0], fwd[1]], axis=1)
    inv = np.concatenate([inv[0], inv[0], inv[1]], axis=1)
    lanes = 768 if width % 768 == 0 else width
    tile3 = lambda i: (0, 0, i)
    specs = [
        pl.BlockSpec((block_total, tables, rows, lanes), lambda i: (0, 0, 0, i)),
        pl.BlockSpec(basis.shape, lambda i: (0, 0, 0)),
        pl.BlockSpec((out_cols.shape[0], lanes), lambda i: (0, i)),
    ]
    operands = [piece, basis, out_cols]
    if finish:
        specs += [
            pl.BlockSpec((tables, 2 * rows, lanes), tile3),
            pl.BlockSpec((tables, rows, lanes), tile3),
            pl.BlockSpec((tables, rows, lanes), tile3),
        ]
        operands += [spec_in, query_gate, carried]
    specs.append(pl.BlockSpec(fwd.shape, lambda i: (0, 0)))
    operands.append(jnp.asarray(fwd))
    if finish:
        specs.append(pl.BlockSpec(inv.shape, lambda i: (0, 0)))
        operands.append(jnp.asarray(inv))
        out_block = (tables, rows, lanes)
        out_shape = jax.ShapeDtypeStruct((tables, rows, width), jnp.bfloat16)
    else:
        out_block = (tables, 2 * rows, lanes)
        out_shape = jax.ShapeDtypeStruct((tables, 2 * rows, width), jnp.float32)
    return pl.pallas_call(
        conv_body(finish),
        grid=(width // lanes,),
        in_specs=specs,
        out_specs=pl.BlockSpec(out_block, tile3),
        out_shape=out_shape,
        scratch_shapes=[pltpu.VMEM((block_total, 2 * rows, lanes), jnp.float32)],
        compiler_params=pltpu.CompilerParams(vmem_limit_bytes=48 * 1024 * 1024),
    )(*operands)


def shards(
    tokens,
    in_weight,
    short_weight,
    basis_in,
    basis_bias,
    basis_mid,
    basis_shift,
    response_out,
    skip_gain,
    block_counts,
):
    seq_dev, block_len, width = tokens.shape
    local_ch = skip_gain.shape[0]
    params = jnp.concatenate(
        [response_out.reshape(2 * response_out.shape[1], local_ch), skip_gain[None, :]], axis=0
    )
    parts = lax.axis_size("groups") * lax.axis_size("seq")
    part = lax.axis_index("groups") * lax.axis_size("seq") + lax.axis_index("seq")
    part_cols = local_ch // parts
    mine = lax.dynamic_slice_in_dim(params, part * part_cols, part_cols, axis=1)
    across = lax.all_gather(mine, "fsdp", axis=0, tiled=False)
    gathered = lax.all_gather(across, ("groups", "seq"), axis=0, tiled=False)
    gathered = jnp.transpose(gathered, (2, 1, 0, 3)).reshape(params.shape[0], width)
    seq_count = lax.axis_size("seq")
    position = lax.axis_index("seq")
    total_len = float(seq_count * block_len)
    forward = forward_table(block_len)
    forward_half = forward[:, :block_len]
    inverse = inverse_table(block_len)
    circular = jnp.arange(2 * block_len, dtype=jnp.int32)
    wrapped = jnp.where(circular < block_len, circular, circular - 2 * block_len)

    block_total = seq_count
    chips = seq_count // 2
    chip, core = position // 2, position % 2
    ring = (chip - jnp.arange(chips, dtype=jnp.int32)) % chips
    order = jnp.concatenate(
        [2 * ring[:1] + core, 2 * ring[:1] + 1 - core, 2 * ring[1:] + core, 2 * ring[1:] + 1 - core]
    )
    offsets = (position - order) * block_len
    lag_values = (offsets[:, None] + wrapped[None, :]).reshape(-1)
    basis_rows = filter_basis(lag_values, total_len, basis_in, basis_bias, basis_mid, basis_shift)
    ahead_mask = (lag_values >= 0).astype(jnp.float32)[:, None]
    paired = jnp.concatenate([basis_rows * ahead_mask, basis_rows * (1.0 - ahead_mask)], axis=1)
    paired = paired.reshape(block_total, 2 * block_len, paired.shape[-1])
    basis_spec = jnp.einsum("gf,bfk->bgk", forward, paired, precision=lax.Precision.HIGHEST)
    group_tokens = lax.all_gather(tokens, "fsdp", axis=0, tiled=True)
    group_tokens, basis_spec, gathered = lax.optimization_barrier((group_tokens, basis_spec, gathered))
    group_rows = group_tokens.shape[0]
    local_cols = in_weight.shape[1]
    partial = jnp.dot(
        group_tokens.reshape(group_rows * block_len, width),
        in_weight,
        preferred_element_type=jnp.float32,
    ).astype(jnp.bfloat16)
    partial = partial.reshape(group_rows, block_len, local_cols)
    projected = lax.all_to_all(partial, "fsdp", 0, 2, tiled=True)
    padded = padded_2(projected, (("seq", 1),), 1)
    shorted = (
        short_weight[0] * padded[:, :-2]
        + short_weight[1] * padded[:, 1:-1]
        + short_weight[2] * padded[:, 2:]
    )
    query_gate = shorted[:, :, :width]
    key_part = shorted[:, :, width : 2 * width]
    value_part = shorted[:, :, 2 * width :]
    valid_mask = (jnp.arange(block_len, dtype=jnp.int32)[None, :] < block_counts).astype(
        jnp.float32
    )
    carried = (key_part * value_part * valid_mask[:, :, None]).astype(jnp.bfloat16)
    partner = [(i, i ^ 1) for i in range(seq_count)]
    near = jnp.stack([carried, lax.ppermute(carried, "seq", partner)])
    far = []
    for shift in range(1, chips):
        far.append(
            lax.ppermute(
                carried, "seq", [(i, (i + 2 * shift) % seq_count) for i in range(seq_count)]
            )
        )
    far = jnp.stack(far)
    near_count = near.shape[0]
    spectrum = fused_conv(near, basis_spec[:near_count], gathered)
    far, spectrum = lax.optimization_barrier((far, spectrum))
    far = jnp.concatenate([far, lax.ppermute(far, "seq", partner)], axis=0)
    return fused_conv(far, basis_spec[near_count:], gathered, query_gate, carried, spectrum)


def solution(mesh):
    placed = (
        P(("groups", "fsdp"), "seq", None),
        P(None, "fsdp"),
        P(),
        P(),
        P(),
        P(),
        P(),
        P(None, None, "fsdp"),
        P("fsdp"),
        P(("groups", "fsdp"), "seq"),
    )
    return jax.shard_map(
        shards,
        mesh=mesh,
        in_specs=placed,
        out_specs=P(("groups", "fsdp"), "seq", None),
        check_vma=False,
    )
```

```python
import jax
import ml_dtypes
import numpy as np
import jax.numpy as jnp
from jax import lax
from jax.sharding import PartitionSpec as P
from jax.experimental import pallas as pl
from jax.experimental.pallas import tpu as pltpu


def padded_2(cells, sides, width):
    for axis, dim in sides:
        count = lax.axis_size(axis)
        ends = count - 1
        head = lax.slice_in_dim(cells, 0, width, axis=dim)
        tail = lax.slice_in_dim(cells, cells.shape[dim] - width, cells.shape[dim], axis=dim)
        cells = jnp.concatenate(
            [
                lax.ppermute(tail, axis, [(i, (i + 1) % count) for i in range(ends)]),
                cells,
                lax.ppermute(head, axis, [((i + 1) % count, i) for i in range(ends)]),
            ],
            axis=dim,
        )
    return cells


def gather_by_permutes(values, axis):
    count = lax.axis_size(axis)
    own = lax.axis_index(axis)
    received = [values]
    for shift in range(1, count):
        received.append(
            lax.ppermute(values, axis, [(i, (i + shift) % count) for i in range(count)])
        )
    stacked = jnp.stack(received)
    sources = (own - jnp.arange(count, dtype=jnp.int32)) % count
    order = jnp.argsort(sources)
    return jnp.take(stacked, order, axis=0)


def relay_gather(values, axis):
    count = lax.axis_size(axis)
    own = lax.axis_index(axis)
    from_left, from_right = [], []
    rightward, leftward = values, values
    for step in range(1, count):
        rightward = lax.ppermute(rightward, axis, [(j, j + 1) for j in range(step - 1, count - 1)])
        leftward = lax.ppermute(leftward, axis, [(j, j - 1) for j in range(1, count - step + 1)])
        from_left.append(rightward)
        from_right.append(leftward)
    chunks = []
    for target in range(count):
        chunk = values
        for step in range(1, count):
            chunk = jnp.where(own - step == target, from_left[step - 1], chunk)
            chunk = jnp.where(own + step == target, from_right[step - 1], chunk)
        chunks.append(chunk)
    return jnp.concatenate(chunks, axis=0)


def filter_basis(lag_values, total_len, basis_in, basis_bias, basis_mid, basis_shift):
    band_count = (basis_in.shape[0] - 1) // 2
    distance = jnp.abs(lag_values)
    periods = (2 ** (jnp.arange(band_count, dtype=jnp.int32) + 2) + 1).astype(jnp.int32)
    angles = (
        2.0
        * jnp.pi
        * (distance[:, None] % periods[None, :]).astype(jnp.float32)
        / periods[None, :].astype(jnp.float32)
    )
    linear = distance.astype(jnp.float32)[:, None] / total_len
    encoded = jnp.concatenate([linear, jnp.cos(angles), jnp.sin(angles)], axis=1)
    hidden = jnp.sin(jnp.dot(encoded, basis_in, precision=lax.Precision.HIGHEST) + basis_bias)
    return jnp.sin(jnp.dot(hidden, basis_mid, precision=lax.Precision.HIGHEST) + basis_shift)


def forward_table(block_len):
    period = 2 * block_len
    frequency = jnp.arange(block_len, dtype=jnp.int32)[:, None]
    samples = jnp.arange(period, dtype=jnp.int32)[None, :]
    phases = 2.0 * jnp.pi / period * (frequency * samples % period).astype(jnp.float32)
    alternate = (1 - 2 * (samples % 2)).astype(jnp.float32)
    real_rows = jnp.cos(phases)
    imag_rows = jnp.where(frequency == 0, alternate, -jnp.sin(phases))
    return jnp.concatenate([real_rows, imag_rows], axis=0)


def inverse_table(block_len):
    period = 2 * block_len
    places = jnp.arange(block_len, dtype=jnp.int32)[:, None]
    frequency = jnp.arange(block_len, dtype=jnp.int32)[None, :]
    phases = 2.0 * jnp.pi / period * (places * frequency % period).astype(jnp.float32)
    alternate = (1 - 2 * (places % 2)).astype(jnp.float32)
    real_cols = jnp.where(frequency == 0, 1.0, 2.0 * jnp.cos(phases)) / period
    imag_cols = jnp.where(frequency == 0, alternate, -2.0 * jnp.sin(phases)) / period
    return jnp.concatenate([real_cols, imag_cols], axis=1)


def packed_product(response, signal, block_len):
    first_slot = (jnp.arange(block_len) == 0)[:, None]
    resp_real = response[..., :block_len, :]
    resp_imag = response[..., block_len:, :]
    sig_real = signal[..., :block_len, :]
    sig_imag = signal[..., block_len:, :]
    cross_term = resp_imag * sig_imag
    prod_real = resp_real * sig_real - jnp.where(first_slot, 0.0, cross_term)
    prod_imag = jnp.where(first_slot, cross_term, resp_real * sig_imag + resp_imag * sig_real)
    return jnp.concatenate([prod_real, prod_imag], axis=-2)


def split_bf16(values):
    high = values.astype(jnp.bfloat16)
    return high, (values - high.astype(jnp.float32)).astype(jnp.bfloat16)


def split_table(values):
    high = values.astype(ml_dtypes.bfloat16)
    low = (values - high.astype(np.float64)).astype(ml_dtypes.bfloat16)
    return np.stack([high, low])


def dft_tables(block_len):
    period = 2 * block_len
    frequency = np.arange(block_len)[:, None]
    samples = np.arange(block_len)[None, :]
    phases = 2.0 * np.pi / period * (frequency * samples % period)
    alternate = (1 - 2 * (samples % 2)).astype(np.float64)
    real_rows = np.cos(phases)
    imag_rows = np.where(frequency == 0, alternate, -np.sin(phases))
    forward = np.concatenate([real_rows, imag_rows], axis=0)
    places = np.arange(block_len)[:, None]
    freq = np.arange(block_len)[None, :]
    phases = 2.0 * np.pi / period * (places * freq % period)
    alt = (1 - 2 * (places % 2)).astype(np.float64)
    real_cols = np.where(freq == 0, 1.0, 2.0 * np.cos(phases)) / period
    imag_cols = np.where(freq == 0, alt, -2.0 * np.sin(phases)) / period
    inverse = np.concatenate([np.broadcast_to(real_cols, (block_len, block_len)), imag_cols], axis=1)
    return split_table(forward), split_table(inverse)


def conv_body(finish):
    def kernel(*refs):
        if finish:
            (piece_ref, basis_ref, out_cols_ref, spec_in_ref, query_ref, carried_ref,
             fwd_ref, inv_ref, out_ref, resp_ref) = refs
        else:
            piece_ref, basis_ref, out_cols_ref, fwd_ref, out_ref, resp_ref = refs
        block_total, tables, rows, lanes = piece_ref.shape
        out_cols = out_cols_ref[...]
        cols_hi, cols_lo = split_bf16(out_cols[:-1])
        skip = out_cols[out_cols.shape[0] - 1 :]
        cols = jnp.concatenate([cols_hi, cols_lo, cols_hi], axis=0)

        def dot(a, b):
            return jnp.dot(a, b, preferred_element_type=jnp.float32)

        def fill(block, carry):
            resp_ref[block] = dot(basis_ref[block], cols)
            return carry

        lax.fori_loop(0, block_total, fill, 0)
        first = lax.broadcasted_iota(jnp.int32, (rows, lanes), 0) == 0
        fwd = fwd_ref[...]

        for table in range(tables):

            def one_block(block, acc):
                acc_real, acc_imag, edge = acc
                block_rows = piece_ref[block, table]
                signal = dot(fwd, jnp.concatenate([block_rows, block_rows], axis=0))
                response = resp_ref[block]
                resp_real = response[:rows]
                resp_imag = response[rows:]
                sig_real = signal[:rows]
                sig_imag = signal[rows:]
                acc_real = acc_real + (resp_real * sig_real - resp_imag * sig_imag)
                acc_imag = acc_imag + (resp_real * sig_imag + resp_imag * sig_real)
                edge = edge + resp_imag[0:1] * sig_imag[0:1]
                return acc_real, acc_imag, edge

            zeros = jnp.zeros((rows, lanes), jnp.float32)
            acc_real, acc_imag, edge = lax.fori_loop(
                0, block_total, one_block, (zeros, zeros, jnp.zeros((1, lanes), jnp.float32))
            )
            acc_real = acc_real + jnp.where(first, edge, 0.0)
            acc_imag = jnp.where(first, edge, acc_imag)
            spectrum = jnp.concatenate([acc_real, acc_imag], axis=0)
            if not finish:
                out_ref[table] = spectrum
                continue
            spectrum = spectrum + spec_in_ref[table]
            spec_hi, spec_lo = split_bf16(spectrum)
            conv = dot(inv_ref[...], jnp.concatenate([spec_hi, spec_lo, spec_hi], axis=0))
            gated = query_ref[table] * (conv + skip * carried_ref[table].astype(jnp.float32))
            out_ref[table] = gated.astype(out_ref.dtype)

    return kernel


def fused_conv(piece, basis_spec, out_cols, query_gate=None, carried=None, spec_in=None):
    block_total, tables, rows, width = piece.shape
    finish = spec_in is not None
    basis_hi, basis_lo = split_bf16(basis_spec)
    basis = jnp.concatenate([basis_hi, basis_hi, basis_lo], axis=2)
    fwd, inv = dft_tables(rows)
    fwd = np.concatenate([fwd[0], fwd[1]], axis=1)
    inv = np.concatenate([inv[0], inv[0], inv[1]], axis=1)
    lanes = 768 if width % 768 == 0 else width
    tile3 = lambda i: (0, 0, i)
    specs = [
        pl.BlockSpec((block_total, tables, rows, lanes), lambda i: (0, 0, 0, i)),
        pl.BlockSpec(basis.shape, lambda i: (0, 0, 0)),
        pl.BlockSpec((out_cols.shape[0], lanes), lambda i: (0, i)),
    ]
    operands = [piece, basis, out_cols]
    if finish:
        specs += [
            pl.BlockSpec((tables, 2 * rows, lanes), tile3),
            pl.BlockSpec((tables, rows, lanes), tile3),
            pl.BlockSpec((tables, rows, lanes), tile3),
        ]
        operands += [spec_in, query_gate, carried]
    specs.append(pl.BlockSpec(fwd.shape, lambda i: (0, 0)))
    operands.append(jnp.asarray(fwd))
    if finish:
        specs.append(pl.BlockSpec(inv.shape, lambda i: (0, 0)))
        operands.append(jnp.asarray(inv))
        out_block = (tables, rows, lanes)
        out_shape = jax.ShapeDtypeStruct((tables, rows, width), jnp.bfloat16)
    else:
        out_block = (tables, 2 * rows, lanes)
        out_shape = jax.ShapeDtypeStruct((tables, 2 * rows, width), jnp.float32)
    return pl.pallas_call(
        conv_body(finish),
        grid=(width // lanes,),
        in_specs=specs,
        out_specs=pl.BlockSpec(out_block, tile3),
        out_shape=out_shape,
        scratch_shapes=[pltpu.VMEM((block_total, 2 * rows, lanes), jnp.float32)],
        compiler_params=pltpu.CompilerParams(vmem_limit_bytes=48 * 1024 * 1024),
    )(*operands)


def shards(
    tokens,
    in_weight,
    short_weight,
    basis_in,
    basis_bias,
    basis_mid,
    basis_shift,
    response_out,
    skip_gain,
    block_counts,
):
    seq_dev, block_len, width = tokens.shape
    local_ch = skip_gain.shape[0]
    params = jnp.concatenate(
        [response_out.reshape(2 * response_out.shape[1], local_ch), skip_gain[None, :]], axis=0
    )
    parts = lax.axis_size("groups") * lax.axis_size("seq")
    part = lax.axis_index("groups") * lax.axis_size("seq") + lax.axis_index("seq")
    part_cols = local_ch // parts
    mine = lax.dynamic_slice_in_dim(params, part * part_cols, part_cols, axis=1)
    across = lax.all_gather(mine, "fsdp", axis=0, tiled=False)
    gathered = lax.all_gather(across, ("groups", "seq"), axis=0, tiled=False)
    gathered = jnp.transpose(gathered, (2, 1, 0, 3)).reshape(params.shape[0], width)
    seq_count = lax.axis_size("seq")
    position = lax.axis_index("seq")
    total_len = float(seq_count * block_len)
    forward = forward_table(block_len)
    forward_half = forward[:, :block_len]
    inverse = inverse_table(block_len)
    circular = jnp.arange(2 * block_len, dtype=jnp.int32)
    wrapped = jnp.where(circular < block_len, circular, circular - 2 * block_len)

    block_total = seq_count
    chips = seq_count // 2
    chip, core = position // 2, position % 2
    ring = (chip - jnp.arange(chips, dtype=jnp.int32)) % chips
    order = jnp.concatenate(
        [2 * ring[:1] + core, 2 * ring[:1] + 1 - core, 2 * ring[1:] + core, 2 * ring[1:] + 1 - core]
    )
    offsets = (position - order) * block_len
    lag_values = (offsets[:, None] + wrapped[None, :]).reshape(-1)
    basis_rows = filter_basis(lag_values, total_len, basis_in, basis_bias, basis_mid, basis_shift)
    ahead_mask = (lag_values >= 0).astype(jnp.float32)[:, None]
    paired = jnp.concatenate([basis_rows * ahead_mask, basis_rows * (1.0 - ahead_mask)], axis=1)
    paired = paired.reshape(block_total, 2 * block_len, paired.shape[-1])
    basis_spec = jnp.einsum("gf,bfk->bgk", forward, paired, precision=lax.Precision.HIGHEST)
    group_tokens = relay_gather(tokens, "fsdp")
    group_tokens, basis_spec, gathered = lax.optimization_barrier((group_tokens, basis_spec, gathered))
    group_rows = group_tokens.shape[0]
    local_cols = in_weight.shape[1]
    partial = jnp.dot(
        group_tokens.reshape(group_rows * block_len, width),
        in_weight,
        preferred_element_type=jnp.float32,
    ).astype(jnp.bfloat16)
    partial = partial.reshape(group_rows, block_len, local_cols)
    projected = lax.all_to_all(partial, "fsdp", 0, 2, tiled=True)
    padded = padded_2(projected, (("seq", 1),), 1)
    shorted = (
        short_weight[0] * padded[:, :-2]
        + short_weight[1] * padded[:, 1:-1]
        + short_weight[2] * padded[:, 2:]
    )
    query_gate = shorted[:, :, :width]
    key_part = shorted[:, :, width : 2 * width]
    value_part = shorted[:, :, 2 * width :]
    valid_mask = (jnp.arange(block_len, dtype=jnp.int32)[None, :] < block_counts).astype(
        jnp.float32
    )
    carried = (key_part * value_part * valid_mask[:, :, None]).astype(jnp.bfloat16)
    partner = [(i, i ^ 1) for i in range(seq_count)]
    near = jnp.stack([carried, lax.ppermute(carried, "seq", partner)])
    far = []
    for shift in range(1, chips):
        far.append(
            lax.ppermute(
                carried, "seq", [(i, (i + 2 * shift) % seq_count) for i in range(seq_count)]
            )
        )
    far = jnp.stack(far)
    near_count = near.shape[0]
    spectrum = fused_conv(near, basis_spec[:near_count], gathered)
    far, spectrum = lax.optimization_barrier((far, spectrum))
    far = jnp.concatenate([far, lax.ppermute(far, "seq", partner)], axis=0)
    return fused_conv(far, basis_spec[near_count:], gathered, query_gate, carried, spectrum)


def solution(mesh):
    placed = (
        P(("groups", "fsdp"), "seq", None),
        P(None, "fsdp"),
        P(),
        P(),
        P(),
        P(),
        P(),
        P(None, None, "fsdp"),
        P("fsdp"),
        P(("groups", "fsdp"), "seq"),
    )
    return jax.shard_map(
        shards,
        mesh=mesh,
        in_specs=placed,
        out_specs=P(("groups", "fsdp"), "seq", None),
        check_vma=False,
    )
```

```python
import jax
import ml_dtypes
import numpy as np
import jax.numpy as jnp
from jax import lax
from jax.sharding import PartitionSpec as P
from jax.experimental import pallas as pl
from jax.experimental.pallas import tpu as pltpu


def padded_2(cells, sides, width):
    for axis, dim in sides:
        count = lax.axis_size(axis)
        ends = count - 1
        head = lax.slice_in_dim(cells, 0, width, axis=dim)
        tail = lax.slice_in_dim(cells, cells.shape[dim] - width, cells.shape[dim], axis=dim)
        cells = jnp.concatenate(
            [
                lax.ppermute(tail, axis, [(i, (i + 1) % count) for i in range(ends)]),
                cells,
                lax.ppermute(head, axis, [((i + 1) % count, i) for i in range(ends)]),
            ],
            axis=dim,
        )
    return cells


def gather_by_permutes(values, axis):
    count = lax.axis_size(axis)
    own = lax.axis_index(axis)
    received = [values]
    for shift in range(1, count):
        received.append(
            lax.ppermute(values, axis, [(i, (i + shift) % count) for i in range(count)])
        )
    stacked = jnp.stack(received)
    sources = (own - jnp.arange(count, dtype=jnp.int32)) % count
    order = jnp.argsort(sources)
    return jnp.take(stacked, order, axis=0)


def relay_gather(values, axis):
    count = lax.axis_size(axis)
    own = lax.axis_index(axis)
    from_left, from_right = [], []
    rightward, leftward = values, values
    for step in range(1, count):
        rightward = lax.ppermute(rightward, axis, [(j, j + 1) for j in range(step - 1, count - 1)])
        leftward = lax.ppermute(leftward, axis, [(j, j - 1) for j in range(1, count - step + 1)])
        from_left.append(rightward)
        from_right.append(leftward)
    chunks = []
    for target in range(count):
        chunk = values
        for step in range(1, count):
            chunk = jnp.where(own - step == target, from_left[step - 1], chunk)
            chunk = jnp.where(own + step == target, from_right[step - 1], chunk)
        chunks.append(chunk)
    return jnp.concatenate(chunks, axis=0)


def filter_basis(lag_values, total_len, basis_in, basis_bias, basis_mid, basis_shift):
    band_count = (basis_in.shape[0] - 1) // 2
    distance = jnp.abs(lag_values)
    periods = (2 ** (jnp.arange(band_count, dtype=jnp.int32) + 2) + 1).astype(jnp.int32)
    angles = (
        2.0
        * jnp.pi
        * (distance[:, None] % periods[None, :]).astype(jnp.float32)
        / periods[None, :].astype(jnp.float32)
    )
    linear = distance.astype(jnp.float32)[:, None] / total_len
    encoded = jnp.concatenate([linear, jnp.cos(angles), jnp.sin(angles)], axis=1)
    hidden = jnp.sin(jnp.dot(encoded, basis_in, precision=lax.Precision.HIGHEST) + basis_bias)
    return jnp.sin(jnp.dot(hidden, basis_mid, precision=lax.Precision.HIGHEST) + basis_shift)


def forward_table(block_len):
    period = 2 * block_len
    frequency = jnp.arange(block_len, dtype=jnp.int32)[:, None]
    samples = jnp.arange(period, dtype=jnp.int32)[None, :]
    phases = 2.0 * jnp.pi / period * (frequency * samples % period).astype(jnp.float32)
    alternate = (1 - 2 * (samples % 2)).astype(jnp.float32)
    real_rows = jnp.cos(phases)
    imag_rows = jnp.where(frequency == 0, alternate, -jnp.sin(phases))
    return jnp.concatenate([real_rows, imag_rows], axis=0)


def inverse_table(block_len):
    period = 2 * block_len
    places = jnp.arange(block_len, dtype=jnp.int32)[:, None]
    frequency = jnp.arange(block_len, dtype=jnp.int32)[None, :]
    phases = 2.0 * jnp.pi / period * (places * frequency % period).astype(jnp.float32)
    alternate = (1 - 2 * (places % 2)).astype(jnp.float32)
    real_cols = jnp.where(frequency == 0, 1.0, 2.0 * jnp.cos(phases)) / period
    imag_cols = jnp.where(frequency == 0, alternate, -2.0 * jnp.sin(phases)) / period
    return jnp.concatenate([real_cols, imag_cols], axis=1)


def packed_product(response, signal, block_len):
    first_slot = (jnp.arange(block_len) == 0)[:, None]
    resp_real = response[..., :block_len, :]
    resp_imag = response[..., block_len:, :]
    sig_real = signal[..., :block_len, :]
    sig_imag = signal[..., block_len:, :]
    cross_term = resp_imag * sig_imag
    prod_real = resp_real * sig_real - jnp.where(first_slot, 0.0, cross_term)
    prod_imag = jnp.where(first_slot, cross_term, resp_real * sig_imag + resp_imag * sig_real)
    return jnp.concatenate([prod_real, prod_imag], axis=-2)


def split_bf16(values):
    high = values.astype(jnp.bfloat16)
    return high, (values - high.astype(jnp.float32)).astype(jnp.bfloat16)


def split_table(values):
    high = values.astype(ml_dtypes.bfloat16)
    low = (values - high.astype(np.float64)).astype(ml_dtypes.bfloat16)
    return np.stack([high, low])


def dft_tables(block_len):
    period = 2 * block_len
    frequency = np.arange(block_len)[:, None]
    samples = np.arange(block_len)[None, :]
    phases = 2.0 * np.pi / period * (frequency * samples % period)
    alternate = (1 - 2 * (samples % 2)).astype(np.float64)
    real_rows = np.cos(phases)
    imag_rows = np.where(frequency == 0, alternate, -np.sin(phases))
    forward = np.concatenate([real_rows, imag_rows], axis=0)
    places = np.arange(block_len)[:, None]
    freq = np.arange(block_len)[None, :]
    phases = 2.0 * np.pi / period * (places * freq % period)
    alt = (1 - 2 * (places % 2)).astype(np.float64)
    real_cols = np.where(freq == 0, 1.0, 2.0 * np.cos(phases)) / period
    imag_cols = np.where(freq == 0, alt, -2.0 * np.sin(phases)) / period
    inverse = np.concatenate([np.broadcast_to(real_cols, (block_len, block_len)), imag_cols], axis=1)
    return split_table(forward), split_table(inverse)


def conv_body(finish):
    def kernel(*refs):
        if finish:
            (piece_ref, basis_ref, out_cols_ref, spec_in_ref, query_ref, carried_ref,
             fwd_ref, inv_ref, out_ref, resp_ref) = refs
        else:
            piece_ref, basis_ref, out_cols_ref, fwd_ref, out_ref, resp_ref = refs
        block_total, tables, rows, lanes = piece_ref.shape
        out_cols = out_cols_ref[...]
        cols_hi, cols_lo = split_bf16(out_cols[:-1])
        skip = out_cols[out_cols.shape[0] - 1 :]
        cols = jnp.concatenate([cols_hi, cols_lo, cols_hi], axis=0)

        def dot(a, b):
            return jnp.dot(a, b, preferred_element_type=jnp.float32)

        def fill(block, carry):
            resp_ref[block] = dot(basis_ref[block], cols)
            return carry

        lax.fori_loop(0, block_total, fill, 0)
        first = lax.broadcasted_iota(jnp.int32, (rows, lanes), 0) == 0
        fwd = fwd_ref[...]

        for table in range(tables):

            def one_block(block, acc):
                acc_real, acc_imag, edge = acc
                block_rows = piece_ref[block, table]
                signal = dot(fwd, jnp.concatenate([block_rows, block_rows], axis=0))
                response = resp_ref[block]
                resp_real = response[:rows]
                resp_imag = response[rows:]
                sig_real = signal[:rows]
                sig_imag = signal[rows:]
                acc_real = acc_real + (resp_real * sig_real - resp_imag * sig_imag)
                acc_imag = acc_imag + (resp_real * sig_imag + resp_imag * sig_real)
                edge = edge + resp_imag[0:1] * sig_imag[0:1]
                return acc_real, acc_imag, edge

            zeros = jnp.zeros((rows, lanes), jnp.float32)
            acc_real, acc_imag, edge = lax.fori_loop(
                0, block_total, one_block, (zeros, zeros, jnp.zeros((1, lanes), jnp.float32))
            )
            acc_real = acc_real + jnp.where(first, edge, 0.0)
            acc_imag = jnp.where(first, edge, acc_imag)
            spectrum = jnp.concatenate([acc_real, acc_imag], axis=0)
            if not finish:
                out_ref[table] = spectrum
                continue
            spectrum = spectrum + spec_in_ref[table]
            spec_hi, spec_lo = split_bf16(spectrum)
            conv = dot(inv_ref[...], jnp.concatenate([spec_hi, spec_lo, spec_hi], axis=0))
            gated = query_ref[table] * (conv + skip * carried_ref[table].astype(jnp.float32))
            out_ref[table] = gated.astype(out_ref.dtype)

    return kernel


def fused_conv(piece, basis_spec, out_cols, query_gate=None, carried=None, spec_in=None):
    block_total, tables, rows, width = piece.shape
    finish = spec_in is not None
    basis_hi, basis_lo = split_bf16(basis_spec)
    basis = jnp.concatenate([basis_hi, basis_hi, basis_lo], axis=2)
    fwd, inv = dft_tables(rows)
    fwd = np.concatenate([fwd[0], fwd[1]], axis=1)
    inv = np.concatenate([inv[0], inv[0], inv[1]], axis=1)
    lanes = 768 if width % 768 == 0 else width
    tile3 = lambda i: (0, 0, i)
    specs = [
        pl.BlockSpec((block_total, tables, rows, lanes), lambda i: (0, 0, 0, i)),
        pl.BlockSpec(basis.shape, lambda i: (0, 0, 0)),
        pl.BlockSpec((out_cols.shape[0], lanes), lambda i: (0, i)),
    ]
    operands = [piece, basis, out_cols]
    if finish:
        specs += [
            pl.BlockSpec((tables, 2 * rows, lanes), tile3),
            pl.BlockSpec((tables, rows, lanes), tile3),
            pl.BlockSpec((tables, rows, lanes), tile3),
        ]
        operands += [spec_in, query_gate, carried]
    specs.append(pl.BlockSpec(fwd.shape, lambda i: (0, 0)))
    operands.append(jnp.asarray(fwd))
    if finish:
        specs.append(pl.BlockSpec(inv.shape, lambda i: (0, 0)))
        operands.append(jnp.asarray(inv))
        out_block = (tables, rows, lanes)
        out_shape = jax.ShapeDtypeStruct((tables, rows, width), jnp.bfloat16)
    else:
        out_block = (tables, 2 * rows, lanes)
        out_shape = jax.ShapeDtypeStruct((tables, 2 * rows, width), jnp.float32)
    return pl.pallas_call(
        conv_body(finish),
        grid=(width // lanes,),
        in_specs=specs,
        out_specs=pl.BlockSpec(out_block, tile3),
        out_shape=out_shape,
        scratch_shapes=[pltpu.VMEM((block_total, 2 * rows, lanes), jnp.float32)],
        compiler_params=pltpu.CompilerParams(vmem_limit_bytes=48 * 1024 * 1024),
    )(*operands)


def shards(
    tokens,
    in_weight,
    short_weight,
    basis_in,
    basis_bias,
    basis_mid,
    basis_shift,
    response_out,
    skip_gain,
    block_counts,
):
    seq_dev, block_len, width = tokens.shape
    local_ch = skip_gain.shape[0]
    params = jnp.concatenate(
        [response_out.reshape(2 * response_out.shape[1], local_ch), skip_gain[None, :]], axis=0
    )
    parts = lax.axis_size("groups") * lax.axis_size("seq")
    part = lax.axis_index("groups") * lax.axis_size("seq") + lax.axis_index("seq")
    part_cols = local_ch // parts
    mine = lax.dynamic_slice_in_dim(params, part * part_cols, part_cols, axis=1)
    across = lax.all_gather(mine, "fsdp", axis=0, tiled=False)
    gathered = lax.all_gather(across, ("groups", "seq"), axis=0, tiled=False)
    gathered = jnp.transpose(gathered, (2, 1, 0, 3)).reshape(params.shape[0], width)
    seq_count = lax.axis_size("seq")
    position = lax.axis_index("seq")
    total_len = float(seq_count * block_len)
    forward = forward_table(block_len)
    forward_half = forward[:, :block_len]
    inverse = inverse_table(block_len)
    circular = jnp.arange(2 * block_len, dtype=jnp.int32)
    wrapped = jnp.where(circular < block_len, circular, circular - 2 * block_len)

    block_total = seq_count
    chips = seq_count // 2
    chip, core = position // 2, position % 2
    ring = (chip - jnp.arange(chips, dtype=jnp.int32)) % chips
    order = jnp.concatenate(
        [2 * ring[:1] + core, 2 * ring[:1] + 1 - core, 2 * ring[1:] + core, 2 * ring[1:] + 1 - core]
    )
    offsets = (position - order) * block_len
    lag_values = (offsets[:, None] + wrapped[None, :]).reshape(-1)
    basis_rows = filter_basis(lag_values, total_len, basis_in, basis_bias, basis_mid, basis_shift)
    ahead_mask = (lag_values >= 0).astype(jnp.float32)[:, None]
    paired = jnp.concatenate([basis_rows * ahead_mask, basis_rows * (1.0 - ahead_mask)], axis=1)
    paired = paired.reshape(block_total, 2 * block_len, paired.shape[-1])
    basis_spec = jnp.einsum("gf,bfk->bgk", forward, paired, precision=lax.Precision.HIGHEST)
    group_tokens = relay_gather(tokens, "fsdp")
    group_tokens, basis_spec = lax.optimization_barrier((group_tokens, basis_spec))
    group_rows = group_tokens.shape[0]
    local_cols = in_weight.shape[1]
    partial = jnp.dot(
        group_tokens.reshape(group_rows * block_len, width),
        in_weight,
        preferred_element_type=jnp.float32,
    ).astype(jnp.bfloat16)
    partial = partial.reshape(group_rows, block_len, local_cols)
    projected = lax.all_to_all(partial, "fsdp", 0, 2, tiled=True)
    projected, gathered = lax.optimization_barrier((projected, gathered))
    padded = padded_2(projected, (("seq", 1),), 1)
    shorted = (
        short_weight[0] * padded[:, :-2]
        + short_weight[1] * padded[:, 1:-1]
        + short_weight[2] * padded[:, 2:]
    )
    query_gate = shorted[:, :, :width]
    key_part = shorted[:, :, width : 2 * width]
    value_part = shorted[:, :, 2 * width :]
    valid_mask = (jnp.arange(block_len, dtype=jnp.int32)[None, :] < block_counts).astype(
        jnp.float32
    )
    carried = (key_part * value_part * valid_mask[:, :, None]).astype(jnp.bfloat16)
    partner = [(i, i ^ 1) for i in range(seq_count)]
    near = jnp.stack([carried, lax.ppermute(carried, "seq", partner)])
    far = []
    for shift in range(1, chips):
        far.append(
            lax.ppermute(
                carried, "seq", [(i, (i + 2 * shift) % seq_count) for i in range(seq_count)]
            )
        )
    far = jnp.stack(far)
    near_count = near.shape[0]
    spectrum = fused_conv(near, basis_spec[:near_count], gathered)
    far, spectrum = lax.optimization_barrier((far, spectrum))
    far = jnp.concatenate([far, lax.ppermute(far, "seq", partner)], axis=0)
    return fused_conv(far, basis_spec[near_count:], gathered, query_gate, carried, spectrum)


def solution(mesh):
    placed = (
        P(("groups", "fsdp"), "seq", None),
        P(None, "fsdp"),
        P(),
        P(),
        P(),
        P(),
        P(),
        P(None, None, "fsdp"),
        P("fsdp"),
        P(("groups", "fsdp"), "seq"),
    )
    return jax.shard_map(
        shards,
        mesh=mesh,
        in_specs=placed,
        out_specs=P(("groups", "fsdp"), "seq", None),
        check_vma=False,
    )
```

```python
import jax
import ml_dtypes
import numpy as np
import jax.numpy as jnp
from jax import lax
from jax.sharding import PartitionSpec as P
from jax.experimental import pallas as pl
from jax.experimental.pallas import tpu as pltpu


def padded_2(cells, sides, width):
    for axis, dim in sides:
        count = lax.axis_size(axis)
        ends = count - 1
        head = lax.slice_in_dim(cells, 0, width, axis=dim)
        tail = lax.slice_in_dim(cells, cells.shape[dim] - width, cells.shape[dim], axis=dim)
        cells = jnp.concatenate(
            [
                lax.ppermute(tail, axis, [(i, (i + 1) % count) for i in range(ends)]),
                cells,
                lax.ppermute(head, axis, [((i + 1) % count, i) for i in range(ends)]),
            ],
            axis=dim,
        )
    return cells


def gather_by_permutes(values, axis):
    count = lax.axis_size(axis)
    own = lax.axis_index(axis)
    received = [values]
    for shift in range(1, count):
        received.append(
            lax.ppermute(values, axis, [(i, (i + shift) % count) for i in range(count)])
        )
    stacked = jnp.stack(received)
    sources = (own - jnp.arange(count, dtype=jnp.int32)) % count
    order = jnp.argsort(sources)
    return jnp.take(stacked, order, axis=0)


def relay_gather(values, axis):
    count = lax.axis_size(axis)
    own = lax.axis_index(axis)
    from_left, from_right = [], []
    rightward, leftward = values, values
    for step in range(1, count):
        rightward = lax.ppermute(rightward, axis, [(j, j + 1) for j in range(step - 1, count - 1)])
        leftward = lax.ppermute(leftward, axis, [(j, j - 1) for j in range(1, count - step + 1)])
        from_left.append(rightward)
        from_right.append(leftward)
    chunks = []
    for target in range(count):
        chunk = values
        for step in range(1, count):
            chunk = jnp.where(own - step == target, from_left[step - 1], chunk)
            chunk = jnp.where(own + step == target, from_right[step - 1], chunk)
        chunks.append(chunk)
    return jnp.concatenate(chunks, axis=0)


def permute_gather(values, axis, count, own):
    received = [values]
    for shift in range(1, count):
        received.append(
            lax.ppermute(values, axis, [(i, (i + shift) % count) for i in range(count)])
        )
    chunks = []
    for target in range(count):
        chunk = received[0]
        for shift in range(1, count):
            chunk = jnp.where((own - shift) % count == target, received[shift], chunk)
        chunks.append(chunk)
    return jnp.stack(chunks)


def filter_basis(lag_values, total_len, basis_in, basis_bias, basis_mid, basis_shift):
    band_count = (basis_in.shape[0] - 1) // 2
    distance = jnp.abs(lag_values)
    periods = (2 ** (jnp.arange(band_count, dtype=jnp.int32) + 2) + 1).astype(jnp.int32)
    angles = (
        2.0
        * jnp.pi
        * (distance[:, None] % periods[None, :]).astype(jnp.float32)
        / periods[None, :].astype(jnp.float32)
    )
    linear = distance.astype(jnp.float32)[:, None] / total_len
    encoded = jnp.concatenate([linear, jnp.cos(angles), jnp.sin(angles)], axis=1)
    hidden = jnp.sin(jnp.dot(encoded, basis_in, precision=lax.Precision.HIGHEST) + basis_bias)
    return jnp.sin(jnp.dot(hidden, basis_mid, precision=lax.Precision.HIGHEST) + basis_shift)


def forward_table(block_len):
    period = 2 * block_len
    frequency = jnp.arange(block_len, dtype=jnp.int32)[:, None]
    samples = jnp.arange(period, dtype=jnp.int32)[None, :]
    phases = 2.0 * jnp.pi / period * (frequency * samples % period).astype(jnp.float32)
    alternate = (1 - 2 * (samples % 2)).astype(jnp.float32)
    real_rows = jnp.cos(phases)
    imag_rows = jnp.where(frequency == 0, alternate, -jnp.sin(phases))
    return jnp.concatenate([real_rows, imag_rows], axis=0)


def inverse_table(block_len):
    period = 2 * block_len
    places = jnp.arange(block_len, dtype=jnp.int32)[:, None]
    frequency = jnp.arange(block_len, dtype=jnp.int32)[None, :]
    phases = 2.0 * jnp.pi / period * (places * frequency % period).astype(jnp.float32)
    alternate = (1 - 2 * (places % 2)).astype(jnp.float32)
    real_cols = jnp.where(frequency == 0, 1.0, 2.0 * jnp.cos(phases)) / period
    imag_cols = jnp.where(frequency == 0, alternate, -2.0 * jnp.sin(phases)) / period
    return jnp.concatenate([real_cols, imag_cols], axis=1)


def packed_product(response, signal, block_len):
    first_slot = (jnp.arange(block_len) == 0)[:, None]
    resp_real = response[..., :block_len, :]
    resp_imag = response[..., block_len:, :]
    sig_real = signal[..., :block_len, :]
    sig_imag = signal[..., block_len:, :]
    cross_term = resp_imag * sig_imag
    prod_real = resp_real * sig_real - jnp.where(first_slot, 0.0, cross_term)
    prod_imag = jnp.where(first_slot, cross_term, resp_real * sig_imag + resp_imag * sig_real)
    return jnp.concatenate([prod_real, prod_imag], axis=-2)


def split_bf16(values):
    high = values.astype(jnp.bfloat16)
    return high, (values - high.astype(jnp.float32)).astype(jnp.bfloat16)


def split_table(values):
    high = values.astype(ml_dtypes.bfloat16)
    low = (values - high.astype(np.float64)).astype(ml_dtypes.bfloat16)
    return np.stack([high, low])


def dft_tables(block_len):
    period = 2 * block_len
    frequency = np.arange(block_len)[:, None]
    samples = np.arange(block_len)[None, :]
    phases = 2.0 * np.pi / period * (frequency * samples % period)
    alternate = (1 - 2 * (samples % 2)).astype(np.float64)
    real_rows = np.cos(phases)
    imag_rows = np.where(frequency == 0, alternate, -np.sin(phases))
    forward = np.concatenate([real_rows, imag_rows], axis=0)
    places = np.arange(block_len)[:, None]
    freq = np.arange(block_len)[None, :]
    phases = 2.0 * np.pi / period * (places * freq % period)
    alt = (1 - 2 * (places % 2)).astype(np.float64)
    real_cols = np.where(freq == 0, 1.0, 2.0 * np.cos(phases)) / period
    imag_cols = np.where(freq == 0, alt, -2.0 * np.sin(phases)) / period
    inverse = np.concatenate([np.broadcast_to(real_cols, (block_len, block_len)), imag_cols], axis=1)
    return split_table(forward), split_table(inverse)


def conv_body(finish):
    def kernel(*refs):
        if finish:
            (piece_ref, basis_ref, out_cols_ref, spec_in_ref, query_ref, carried_ref,
             fwd_ref, inv_ref, out_ref, resp_ref) = refs
        else:
            piece_ref, basis_ref, out_cols_ref, fwd_ref, out_ref, resp_ref = refs
        block_total, tables, rows, lanes = piece_ref.shape
        out_cols = out_cols_ref[...]
        cols_hi, cols_lo = split_bf16(out_cols[:-1])
        skip = out_cols[out_cols.shape[0] - 1 :]
        cols = jnp.concatenate([cols_hi, cols_lo, cols_hi], axis=0)

        def dot(a, b):
            return jnp.dot(a, b, preferred_element_type=jnp.float32)

        def fill(block, carry):
            resp_ref[block] = dot(basis_ref[block], cols)
            return carry

        lax.fori_loop(0, block_total, fill, 0)
        first = lax.broadcasted_iota(jnp.int32, (rows, lanes), 0) == 0
        fwd = fwd_ref[...]

        for table in range(tables):

            def one_block(block, acc):
                acc_real, acc_imag, edge = acc
                block_rows = piece_ref[block, table]
                signal = dot(fwd, jnp.concatenate([block_rows, block_rows], axis=0))
                response = resp_ref[block]
                resp_real = response[:rows]
                resp_imag = response[rows:]
                sig_real = signal[:rows]
                sig_imag = signal[rows:]
                acc_real = acc_real + (resp_real * sig_real - resp_imag * sig_imag)
                acc_imag = acc_imag + (resp_real * sig_imag + resp_imag * sig_real)
                edge = edge + resp_imag[0:1] * sig_imag[0:1]
                return acc_real, acc_imag, edge

            zeros = jnp.zeros((rows, lanes), jnp.float32)
            acc_real, acc_imag, edge = lax.fori_loop(
                0, block_total, one_block, (zeros, zeros, jnp.zeros((1, lanes), jnp.float32))
            )
            acc_real = acc_real + jnp.where(first, edge, 0.0)
            acc_imag = jnp.where(first, edge, acc_imag)
            spectrum = jnp.concatenate([acc_real, acc_imag], axis=0)
            if not finish:
                out_ref[table] = spectrum
                continue
            spectrum = spectrum + spec_in_ref[table]
            spec_hi, spec_lo = split_bf16(spectrum)
            conv = dot(inv_ref[...], jnp.concatenate([spec_hi, spec_lo, spec_hi], axis=0))
            gated = query_ref[table] * (conv + skip * carried_ref[table].astype(jnp.float32))
            out_ref[table] = gated.astype(out_ref.dtype)

    return kernel


def fused_conv(piece, basis_spec, out_cols, query_gate=None, carried=None, spec_in=None):
    block_total, tables, rows, width = piece.shape
    finish = spec_in is not None
    basis_hi, basis_lo = split_bf16(basis_spec)
    basis = jnp.concatenate([basis_hi, basis_hi, basis_lo], axis=2)
    fwd, inv = dft_tables(rows)
    fwd = np.concatenate([fwd[0], fwd[1]], axis=1)
    inv = np.concatenate([inv[0], inv[0], inv[1]], axis=1)
    lanes = 768 if width % 768 == 0 else width
    tile3 = lambda i: (0, 0, i)
    specs = [
        pl.BlockSpec((block_total, tables, rows, lanes), lambda i: (0, 0, 0, i)),
        pl.BlockSpec(basis.shape, lambda i: (0, 0, 0)),
        pl.BlockSpec((out_cols.shape[0], lanes), lambda i: (0, i)),
    ]
    operands = [piece, basis, out_cols]
    if finish:
        specs += [
            pl.BlockSpec((tables, 2 * rows, lanes), tile3),
            pl.BlockSpec((tables, rows, lanes), tile3),
            pl.BlockSpec((tables, rows, lanes), tile3),
        ]
        operands += [spec_in, query_gate, carried]
    specs.append(pl.BlockSpec(fwd.shape, lambda i: (0, 0)))
    operands.append(jnp.asarray(fwd))
    if finish:
        specs.append(pl.BlockSpec(inv.shape, lambda i: (0, 0)))
        operands.append(jnp.asarray(inv))
        out_block = (tables, rows, lanes)
        out_shape = jax.ShapeDtypeStruct((tables, rows, width), jnp.bfloat16)
    else:
        out_block = (tables, 2 * rows, lanes)
        out_shape = jax.ShapeDtypeStruct((tables, 2 * rows, width), jnp.float32)
    return pl.pallas_call(
        conv_body(finish),
        grid=(width // lanes,),
        in_specs=specs,
        out_specs=pl.BlockSpec(out_block, tile3),
        out_shape=out_shape,
        scratch_shapes=[pltpu.VMEM((block_total, 2 * rows, lanes), jnp.float32)],
        compiler_params=pltpu.CompilerParams(vmem_limit_bytes=48 * 1024 * 1024),
    )(*operands)


def shards(
    tokens,
    in_weight,
    short_weight,
    basis_in,
    basis_bias,
    basis_mid,
    basis_shift,
    response_out,
    skip_gain,
    block_counts,
):
    seq_dev, block_len, width = tokens.shape
    local_ch = skip_gain.shape[0]
    params = jnp.concatenate(
        [response_out.reshape(2 * response_out.shape[1], local_ch), skip_gain[None, :]], axis=0
    )
    parts = lax.axis_size("groups") * lax.axis_size("seq")
    part = lax.axis_index("groups") * lax.axis_size("seq") + lax.axis_index("seq")
    part_cols = local_ch // parts
    mine = lax.dynamic_slice_in_dim(params, part * part_cols, part_cols, axis=1)
    across = permute_gather(mine, "fsdp", lax.axis_size("fsdp"), lax.axis_index("fsdp"))
    gathered = permute_gather(across, ("groups", "seq"), parts, part)
    gathered = jnp.transpose(gathered, (2, 1, 0, 3)).reshape(params.shape[0], width)
    seq_count = lax.axis_size("seq")
    position = lax.axis_index("seq")
    total_len = float(seq_count * block_len)
    forward = forward_table(block_len)
    forward_half = forward[:, :block_len]
    inverse = inverse_table(block_len)
    circular = jnp.arange(2 * block_len, dtype=jnp.int32)
    wrapped = jnp.where(circular < block_len, circular, circular - 2 * block_len)

    block_total = seq_count
    chips = seq_count // 2
    chip, core = position // 2, position % 2
    ring = (chip - jnp.arange(chips, dtype=jnp.int32)) % chips
    order = jnp.concatenate(
        [2 * ring[:1] + core, 2 * ring[:1] + 1 - core, 2 * ring[1:] + core, 2 * ring[1:] + 1 - core]
    )
    offsets = (position - order) * block_len
    lag_values = (offsets[:, None] + wrapped[None, :]).reshape(-1)
    basis_rows = filter_basis(lag_values, total_len, basis_in, basis_bias, basis_mid, basis_shift)
    ahead_mask = (lag_values >= 0).astype(jnp.float32)[:, None]
    paired = jnp.concatenate([basis_rows * ahead_mask, basis_rows * (1.0 - ahead_mask)], axis=1)
    paired = paired.reshape(block_total, 2 * block_len, paired.shape[-1])
    basis_spec = jnp.einsum("gf,bfk->bgk", forward, paired, precision=lax.Precision.HIGHEST)
    group_tokens = relay_gather(tokens, "fsdp")
    group_tokens, basis_spec, gathered = lax.optimization_barrier((group_tokens, basis_spec, gathered))
    group_rows = group_tokens.shape[0]
    local_cols = in_weight.shape[1]
    partial = jnp.dot(
        group_tokens.reshape(group_rows * block_len, width),
        in_weight,
        preferred_element_type=jnp.float32,
    ).astype(jnp.bfloat16)
    partial = partial.reshape(group_rows, block_len, local_cols)
    projected = lax.all_to_all(partial, "fsdp", 0, 2, tiled=True)
    padded = padded_2(projected, (("seq", 1),), 1)
    shorted = (
        short_weight[0] * padded[:, :-2]
        + short_weight[1] * padded[:, 1:-1]
        + short_weight[2] * padded[:, 2:]
    )
    query_gate = shorted[:, :, :width]
    key_part = shorted[:, :, width : 2 * width]
    value_part = shorted[:, :, 2 * width :]
    valid_mask = (jnp.arange(block_len, dtype=jnp.int32)[None, :] < block_counts).astype(
        jnp.float32
    )
    carried = (key_part * value_part * valid_mask[:, :, None]).astype(jnp.bfloat16)
    partner = [(i, i ^ 1) for i in range(seq_count)]
    near = jnp.stack([carried, lax.ppermute(carried, "seq", partner)])
    far = []
    for shift in range(1, chips):
        far.append(
            lax.ppermute(
                carried, "seq", [(i, (i + 2 * shift) % seq_count) for i in range(seq_count)]
            )
        )
    far = jnp.stack(far)
    near_count = near.shape[0]
    spectrum = fused_conv(near, basis_spec[:near_count], gathered)
    far, spectrum = lax.optimization_barrier((far, spectrum))
    far = jnp.concatenate([far, lax.ppermute(far, "seq", partner)], axis=0)
    return fused_conv(far, basis_spec[near_count:], gathered, query_gate, carried, spectrum)


def solution(mesh):
    placed = (
        P(("groups", "fsdp"), "seq", None),
        P(None, "fsdp"),
        P(),
        P(),
        P(),
        P(),
        P(),
        P(None, None, "fsdp"),
        P("fsdp"),
        P(("groups", "fsdp"), "seq"),
    )
    return jax.shard_map(
        shards,
        mesh=mesh,
        in_specs=placed,
        out_specs=P(("groups", "fsdp"), "seq", None),
        check_vma=False,
    )
```

```python
import jax
import ml_dtypes
import numpy as np
import jax.numpy as jnp
from jax import lax
from jax.sharding import PartitionSpec as P
from jax.experimental import pallas as pl
from jax.experimental.pallas import tpu as pltpu


def padded_2(cells, sides, width):
    for axis, dim in sides:
        count = lax.axis_size(axis)
        ends = count - 1
        head = lax.slice_in_dim(cells, 0, width, axis=dim)
        tail = lax.slice_in_dim(cells, cells.shape[dim] - width, cells.shape[dim], axis=dim)
        cells = jnp.concatenate(
            [
                lax.ppermute(tail, axis, [(i, (i + 1) % count) for i in range(ends)]),
                cells,
                lax.ppermute(head, axis, [((i + 1) % count, i) for i in range(ends)]),
            ],
            axis=dim,
        )
    return cells


def gather_by_permutes(values, axis):
    count = lax.axis_size(axis)
    own = lax.axis_index(axis)
    received = [values]
    for shift in range(1, count):
        received.append(
            lax.ppermute(values, axis, [(i, (i + shift) % count) for i in range(count)])
        )
    stacked = jnp.stack(received)
    sources = (own - jnp.arange(count, dtype=jnp.int32)) % count
    order = jnp.argsort(sources)
    return jnp.take(stacked, order, axis=0)


def relay_gather(values, axis):
    count = lax.axis_size(axis)
    own = lax.axis_index(axis)
    from_left, from_right = [], []
    rightward, leftward = values, values
    for step in range(1, count):
        rightward = lax.ppermute(rightward, axis, [(j, j + 1) for j in range(step - 1, count - 1)])
        leftward = lax.ppermute(leftward, axis, [(j, j - 1) for j in range(1, count - step + 1)])
        from_left.append(rightward)
        from_right.append(leftward)
    chunks = []
    for target in range(count):
        chunk = values
        for step in range(1, count):
            chunk = jnp.where(own - step == target, from_left[step - 1], chunk)
            chunk = jnp.where(own + step == target, from_right[step - 1], chunk)
        chunks.append(chunk)
    return jnp.concatenate(chunks, axis=0)


def permute_gather(values, axis, count, own):
    received = [values]
    for shift in range(1, count):
        received.append(
            lax.ppermute(values, axis, [(i, (i + shift) % count) for i in range(count)])
        )
    chunks = []
    for target in range(count):
        chunk = received[0]
        for shift in range(1, count):
            chunk = jnp.where((own - shift) % count == target, received[shift], chunk)
        chunks.append(chunk)
    return jnp.stack(chunks)


def filter_basis(lag_values, total_len, basis_in, basis_bias, basis_mid, basis_shift):
    band_count = (basis_in.shape[0] - 1) // 2
    distance = jnp.abs(lag_values)
    periods = (2 ** (jnp.arange(band_count, dtype=jnp.int32) + 2) + 1).astype(jnp.int32)
    angles = (
        2.0
        * jnp.pi
        * (distance[:, None] % periods[None, :]).astype(jnp.float32)
        / periods[None, :].astype(jnp.float32)
    )
    linear = distance.astype(jnp.float32)[:, None] / total_len
    encoded = jnp.concatenate([linear, jnp.cos(angles), jnp.sin(angles)], axis=1)
    hidden = jnp.sin(jnp.dot(encoded, basis_in, precision=lax.Precision.HIGHEST) + basis_bias)
    return jnp.sin(jnp.dot(hidden, basis_mid, precision=lax.Precision.HIGHEST) + basis_shift)


def forward_table(block_len):
    period = 2 * block_len
    frequency = jnp.arange(block_len, dtype=jnp.int32)[:, None]
    samples = jnp.arange(period, dtype=jnp.int32)[None, :]
    phases = 2.0 * jnp.pi / period * (frequency * samples % period).astype(jnp.float32)
    alternate = (1 - 2 * (samples % 2)).astype(jnp.float32)
    real_rows = jnp.cos(phases)
    imag_rows = jnp.where(frequency == 0, alternate, -jnp.sin(phases))
    return jnp.concatenate([real_rows, imag_rows], axis=0)


def inverse_table(block_len):
    period = 2 * block_len
    places = jnp.arange(block_len, dtype=jnp.int32)[:, None]
    frequency = jnp.arange(block_len, dtype=jnp.int32)[None, :]
    phases = 2.0 * jnp.pi / period * (places * frequency % period).astype(jnp.float32)
    alternate = (1 - 2 * (places % 2)).astype(jnp.float32)
    real_cols = jnp.where(frequency == 0, 1.0, 2.0 * jnp.cos(phases)) / period
    imag_cols = jnp.where(frequency == 0, alternate, -2.0 * jnp.sin(phases)) / period
    return jnp.concatenate([real_cols, imag_cols], axis=1)


def packed_product(response, signal, block_len):
    first_slot = (jnp.arange(block_len) == 0)[:, None]
    resp_real = response[..., :block_len, :]
    resp_imag = response[..., block_len:, :]
    sig_real = signal[..., :block_len, :]
    sig_imag = signal[..., block_len:, :]
    cross_term = resp_imag * sig_imag
    prod_real = resp_real * sig_real - jnp.where(first_slot, 0.0, cross_term)
    prod_imag = jnp.where(first_slot, cross_term, resp_real * sig_imag + resp_imag * sig_real)
    return jnp.concatenate([prod_real, prod_imag], axis=-2)


def split_bf16(values):
    high = values.astype(jnp.bfloat16)
    return high, (values - high.astype(jnp.float32)).astype(jnp.bfloat16)


def split_table(values):
    high = values.astype(ml_dtypes.bfloat16)
    low = (values - high.astype(np.float64)).astype(ml_dtypes.bfloat16)
    return np.stack([high, low])


def dft_tables(block_len):
    period = 2 * block_len
    frequency = np.arange(block_len)[:, None]
    samples = np.arange(block_len)[None, :]
    phases = 2.0 * np.pi / period * (frequency * samples % period)
    alternate = (1 - 2 * (samples % 2)).astype(np.float64)
    real_rows = np.cos(phases)
    imag_rows = np.where(frequency == 0, alternate, -np.sin(phases))
    forward = np.concatenate([real_rows, imag_rows], axis=0)
    places = np.arange(block_len)[:, None]
    freq = np.arange(block_len)[None, :]
    phases = 2.0 * np.pi / period * (places * freq % period)
    alt = (1 - 2 * (places % 2)).astype(np.float64)
    real_cols = np.where(freq == 0, 1.0, 2.0 * np.cos(phases)) / period
    imag_cols = np.where(freq == 0, alt, -2.0 * np.sin(phases)) / period
    inverse = np.concatenate([np.broadcast_to(real_cols, (block_len, block_len)), imag_cols], axis=1)
    return split_table(forward), split_table(inverse)


def conv_body(finish):
    def kernel(*refs):
        if finish:
            (piece_ref, basis_ref, out_cols_ref, spec_in_ref, query_ref, carried_ref,
             fwd_ref, inv_ref, out_ref, resp_ref) = refs
        else:
            piece_ref, basis_ref, out_cols_ref, fwd_ref, out_ref, resp_ref = refs
        block_total, tables, rows, lanes = piece_ref.shape
        out_cols = out_cols_ref[...]
        cols_hi, cols_lo = split_bf16(out_cols[:-1])
        skip = out_cols[out_cols.shape[0] - 1 :]
        cols = jnp.concatenate([cols_hi, cols_lo, cols_hi], axis=0)

        def dot(a, b):
            return jnp.dot(a, b, preferred_element_type=jnp.float32)

        def fill(block, carry):
            resp_ref[block] = dot(basis_ref[block], cols)
            return carry

        lax.fori_loop(0, block_total, fill, 0)
        first = lax.broadcasted_iota(jnp.int32, (rows, lanes), 0) == 0
        fwd = fwd_ref[...]

        for table in range(tables):

            def one_block(block, acc):
                acc_real, acc_imag, edge = acc
                block_rows = piece_ref[block, table]
                signal = dot(fwd, jnp.concatenate([block_rows, block_rows], axis=0))
                response = resp_ref[block]
                resp_real = response[:rows]
                resp_imag = response[rows:]
                sig_real = signal[:rows]
                sig_imag = signal[rows:]
                acc_real = acc_real + (resp_real * sig_real - resp_imag * sig_imag)
                acc_imag = acc_imag + (resp_real * sig_imag + resp_imag * sig_real)
                edge = edge + resp_imag[0:1] * sig_imag[0:1]
                return acc_real, acc_imag, edge

            zeros = jnp.zeros((rows, lanes), jnp.float32)
            acc_real, acc_imag, edge = lax.fori_loop(
                0, block_total, one_block, (zeros, zeros, jnp.zeros((1, lanes), jnp.float32))
            )
            acc_real = acc_real + jnp.where(first, edge, 0.0)
            acc_imag = jnp.where(first, edge, acc_imag)
            spectrum = jnp.concatenate([acc_real, acc_imag], axis=0)
            if not finish:
                out_ref[table] = spectrum
                continue
            spectrum = spectrum + spec_in_ref[table]
            spec_hi, spec_lo = split_bf16(spectrum)
            conv = dot(inv_ref[...], jnp.concatenate([spec_hi, spec_lo, spec_hi], axis=0))
            gated = query_ref[table] * (conv + skip * carried_ref[table].astype(jnp.float32))
            out_ref[table] = gated.astype(out_ref.dtype)

    return kernel


def fused_conv(piece, basis_spec, out_cols, query_gate=None, carried=None, spec_in=None):
    block_total, tables, rows, width = piece.shape
    finish = spec_in is not None
    basis_hi, basis_lo = split_bf16(basis_spec)
    basis = jnp.concatenate([basis_hi, basis_hi, basis_lo], axis=2)
    fwd, inv = dft_tables(rows)
    fwd = np.concatenate([fwd[0], fwd[1]], axis=1)
    inv = np.concatenate([inv[0], inv[0], inv[1]], axis=1)
    lanes = 768 if width % 768 == 0 else width
    tile3 = lambda i: (0, 0, i)
    specs = [
        pl.BlockSpec((block_total, tables, rows, lanes), lambda i: (0, 0, 0, i)),
        pl.BlockSpec(basis.shape, lambda i: (0, 0, 0)),
        pl.BlockSpec((out_cols.shape[0], lanes), lambda i: (0, i)),
    ]
    operands = [piece, basis, out_cols]
    if finish:
        specs += [
            pl.BlockSpec((tables, 2 * rows, lanes), tile3),
            pl.BlockSpec((tables, rows, lanes), tile3),
            pl.BlockSpec((tables, rows, lanes), tile3),
        ]
        operands += [spec_in, query_gate, carried]
    specs.append(pl.BlockSpec(fwd.shape, lambda i: (0, 0)))
    operands.append(jnp.asarray(fwd))
    if finish:
        specs.append(pl.BlockSpec(inv.shape, lambda i: (0, 0)))
        operands.append(jnp.asarray(inv))
        out_block = (tables, rows, lanes)
        out_shape = jax.ShapeDtypeStruct((tables, rows, width), jnp.bfloat16)
    else:
        out_block = (tables, 2 * rows, lanes)
        out_shape = jax.ShapeDtypeStruct((tables, 2 * rows, width), jnp.float32)
    return pl.pallas_call(
        conv_body(finish),
        grid=(width // lanes,),
        in_specs=specs,
        out_specs=pl.BlockSpec(out_block, tile3),
        out_shape=out_shape,
        scratch_shapes=[pltpu.VMEM((block_total, 2 * rows, lanes), jnp.float32)],
        compiler_params=pltpu.CompilerParams(vmem_limit_bytes=48 * 1024 * 1024),
    )(*operands)


def shards(
    tokens,
    in_weight,
    short_weight,
    basis_in,
    basis_bias,
    basis_mid,
    basis_shift,
    response_out,
    skip_gain,
    block_counts,
):
    seq_dev, block_len, width = tokens.shape
    local_ch = skip_gain.shape[0]
    params = jnp.concatenate(
        [response_out.reshape(2 * response_out.shape[1], local_ch), skip_gain[None, :]], axis=0
    )
    parts = lax.axis_size("groups") * lax.axis_size("seq")
    part = lax.axis_index("groups") * lax.axis_size("seq") + lax.axis_index("seq")
    part_cols = local_ch // parts
    mine = lax.dynamic_slice_in_dim(params, part * part_cols, part_cols, axis=1)
    across = permute_gather(mine, "fsdp", lax.axis_size("fsdp"), lax.axis_index("fsdp"))
    seq_count = lax.axis_size("seq")
    position = lax.axis_index("seq")
    total_len = float(seq_count * block_len)
    forward = forward_table(block_len)
    forward_half = forward[:, :block_len]
    inverse = inverse_table(block_len)
    circular = jnp.arange(2 * block_len, dtype=jnp.int32)
    wrapped = jnp.where(circular < block_len, circular, circular - 2 * block_len)

    block_total = seq_count
    chips = seq_count // 2
    chip, core = position // 2, position % 2
    ring = (chip - jnp.arange(chips, dtype=jnp.int32)) % chips
    order = jnp.concatenate(
        [2 * ring[:1] + core, 2 * ring[:1] + 1 - core, 2 * ring[1:] + core, 2 * ring[1:] + 1 - core]
    )
    offsets = (position - order) * block_len
    lag_values = (offsets[:, None] + wrapped[None, :]).reshape(-1)
    basis_rows = filter_basis(lag_values, total_len, basis_in, basis_bias, basis_mid, basis_shift)
    ahead_mask = (lag_values >= 0).astype(jnp.float32)[:, None]
    paired = jnp.concatenate([basis_rows * ahead_mask, basis_rows * (1.0 - ahead_mask)], axis=1)
    paired = paired.reshape(block_total, 2 * block_len, paired.shape[-1])
    basis_spec = jnp.einsum("gf,bfk->bgk", forward, paired, precision=lax.Precision.HIGHEST)
    group_tokens = relay_gather(tokens, "fsdp")
    group_tokens, basis_spec, across = lax.optimization_barrier((group_tokens, basis_spec, across))
    gathered = lax.all_gather(across, ("groups", "seq"), axis=0, tiled=False)
    gathered = jnp.transpose(gathered, (2, 1, 0, 3)).reshape(params.shape[0], width)
    group_rows = group_tokens.shape[0]
    local_cols = in_weight.shape[1]
    partial = jnp.dot(
        group_tokens.reshape(group_rows * block_len, width),
        in_weight,
        preferred_element_type=jnp.float32,
    ).astype(jnp.bfloat16)
    partial = partial.reshape(group_rows, block_len, local_cols)
    projected = lax.all_to_all(partial, "fsdp", 0, 2, tiled=True)
    projected, gathered = lax.optimization_barrier((projected, gathered))
    padded = padded_2(projected, (("seq", 1),), 1)
    shorted = (
        short_weight[0] * padded[:, :-2]
        + short_weight[1] * padded[:, 1:-1]
        + short_weight[2] * padded[:, 2:]
    )
    query_gate = shorted[:, :, :width]
    key_part = shorted[:, :, width : 2 * width]
    value_part = shorted[:, :, 2 * width :]
    valid_mask = (jnp.arange(block_len, dtype=jnp.int32)[None, :] < block_counts).astype(
        jnp.float32
    )
    carried = (key_part * value_part * valid_mask[:, :, None]).astype(jnp.bfloat16)
    partner = [(i, i ^ 1) for i in range(seq_count)]
    near = jnp.stack([carried, lax.ppermute(carried, "seq", partner)])
    far = []
    for shift in range(1, chips):
        far.append(
            lax.ppermute(
                carried, "seq", [(i, (i + 2 * shift) % seq_count) for i in range(seq_count)]
            )
        )
    far = jnp.stack(far)
    near_count = near.shape[0]
    spectrum = fused_conv(near, basis_spec[:near_count], gathered)
    far, spectrum = lax.optimization_barrier((far, spectrum))
    far = jnp.concatenate([far, lax.ppermute(far, "seq", partner)], axis=0)
    return fused_conv(far, basis_spec[near_count:], gathered, query_gate, carried, spectrum)


def solution(mesh):
    placed = (
        P(("groups", "fsdp"), "seq", None),
        P(None, "fsdp"),
        P(),
        P(),
        P(),
        P(),
        P(),
        P(None, None, "fsdp"),
        P("fsdp"),
        P(("groups", "fsdp"), "seq"),
    )
    return jax.shard_map(
        shards,
        mesh=mesh,
        in_specs=placed,
        out_specs=P(("groups", "fsdp"), "seq", None),
        check_vma=False,
    )
```

```python
import jax
import ml_dtypes
import numpy as np
import jax.numpy as jnp
from jax import lax
from jax.sharding import PartitionSpec as P
from jax.experimental import pallas as pl
from jax.experimental.pallas import tpu as pltpu


def padded_2(cells, sides, width):
    for axis, dim in sides:
        count = lax.axis_size(axis)
        ends = count - 1
        head = lax.slice_in_dim(cells, 0, width, axis=dim)
        tail = lax.slice_in_dim(cells, cells.shape[dim] - width, cells.shape[dim], axis=dim)
        cells = jnp.concatenate(
            [
                lax.ppermute(tail, axis, [(i, (i + 1) % count) for i in range(ends)]),
                cells,
                lax.ppermute(head, axis, [((i + 1) % count, i) for i in range(ends)]),
            ],
            axis=dim,
        )
    return cells


def gather_by_permutes(values, axis):
    count = lax.axis_size(axis)
    own = lax.axis_index(axis)
    received = [values]
    for shift in range(1, count):
        received.append(
            lax.ppermute(values, axis, [(i, (i + shift) % count) for i in range(count)])
        )
    stacked = jnp.stack(received)
    sources = (own - jnp.arange(count, dtype=jnp.int32)) % count
    order = jnp.argsort(sources)
    return jnp.take(stacked, order, axis=0)


def relay_gather(values, axis, apply=lambda block: block):
    count = lax.axis_size(axis)
    own = lax.axis_index(axis)
    from_left, from_right = [], []
    rightward, leftward = values, values
    for step in range(1, count):
        rightward = lax.ppermute(rightward, axis, [(j, j + 1) for j in range(step - 1, count - 1)])
        leftward = lax.ppermute(leftward, axis, [(j, j - 1) for j in range(1, count - step + 1)])
        from_left.append(rightward)
        from_right.append(leftward)
    values = apply(values)
    from_left = [apply(block) for block in from_left]
    from_right = [apply(block) for block in from_right]
    chunks = []
    for target in range(count):
        chunk = values
        for step in range(1, count):
            chunk = jnp.where(own - step == target, from_left[step - 1], chunk)
            chunk = jnp.where(own + step == target, from_right[step - 1], chunk)
        chunks.append(chunk)
    return jnp.concatenate(chunks, axis=0)


def permute_gather(values, axis, count, own):
    received = [values]
    for shift in range(1, count):
        received.append(
            lax.ppermute(values, axis, [(i, (i + shift) % count) for i in range(count)])
        )
    chunks = []
    for target in range(count):
        chunk = received[0]
        for shift in range(1, count):
            chunk = jnp.where((own - shift) % count == target, received[shift], chunk)
        chunks.append(chunk)
    return jnp.stack(chunks)


def filter_basis(lag_values, total_len, basis_in, basis_bias, basis_mid, basis_shift):
    band_count = (basis_in.shape[0] - 1) // 2
    distance = jnp.abs(lag_values)
    periods = (2 ** (jnp.arange(band_count, dtype=jnp.int32) + 2) + 1).astype(jnp.int32)
    angles = (
        2.0
        * jnp.pi
        * (distance[:, None] % periods[None, :]).astype(jnp.float32)
        / periods[None, :].astype(jnp.float32)
    )
    linear = distance.astype(jnp.float32)[:, None] / total_len
    encoded = jnp.concatenate([linear, jnp.cos(angles), jnp.sin(angles)], axis=1)
    hidden = jnp.sin(jnp.dot(encoded, basis_in, precision=lax.Precision.HIGHEST) + basis_bias)
    return jnp.sin(jnp.dot(hidden, basis_mid, precision=lax.Precision.HIGHEST) + basis_shift)


def forward_table(block_len):
    period = 2 * block_len
    frequency = jnp.arange(block_len, dtype=jnp.int32)[:, None]
    samples = jnp.arange(period, dtype=jnp.int32)[None, :]
    phases = 2.0 * jnp.pi / period * (frequency * samples % period).astype(jnp.float32)
    alternate = (1 - 2 * (samples % 2)).astype(jnp.float32)
    real_rows = jnp.cos(phases)
    imag_rows = jnp.where(frequency == 0, alternate, -jnp.sin(phases))
    return jnp.concatenate([real_rows, imag_rows], axis=0)


def inverse_table(block_len):
    period = 2 * block_len
    places = jnp.arange(block_len, dtype=jnp.int32)[:, None]
    frequency = jnp.arange(block_len, dtype=jnp.int32)[None, :]
    phases = 2.0 * jnp.pi / period * (places * frequency % period).astype(jnp.float32)
    alternate = (1 - 2 * (places % 2)).astype(jnp.float32)
    real_cols = jnp.where(frequency == 0, 1.0, 2.0 * jnp.cos(phases)) / period
    imag_cols = jnp.where(frequency == 0, alternate, -2.0 * jnp.sin(phases)) / period
    return jnp.concatenate([real_cols, imag_cols], axis=1)


def packed_product(response, signal, block_len):
    first_slot = (jnp.arange(block_len) == 0)[:, None]
    resp_real = response[..., :block_len, :]
    resp_imag = response[..., block_len:, :]
    sig_real = signal[..., :block_len, :]
    sig_imag = signal[..., block_len:, :]
    cross_term = resp_imag * sig_imag
    prod_real = resp_real * sig_real - jnp.where(first_slot, 0.0, cross_term)
    prod_imag = jnp.where(first_slot, cross_term, resp_real * sig_imag + resp_imag * sig_real)
    return jnp.concatenate([prod_real, prod_imag], axis=-2)


def split_bf16(values):
    high = values.astype(jnp.bfloat16)
    return high, (values - high.astype(jnp.float32)).astype(jnp.bfloat16)


def split_table(values):
    high = values.astype(ml_dtypes.bfloat16)
    low = (values - high.astype(np.float64)).astype(ml_dtypes.bfloat16)
    return np.stack([high, low])


def dft_tables(block_len):
    period = 2 * block_len
    frequency = np.arange(block_len)[:, None]
    samples = np.arange(block_len)[None, :]
    phases = 2.0 * np.pi / period * (frequency * samples % period)
    alternate = (1 - 2 * (samples % 2)).astype(np.float64)
    real_rows = np.cos(phases)
    imag_rows = np.where(frequency == 0, alternate, -np.sin(phases))
    forward = np.concatenate([real_rows, imag_rows], axis=0)
    places = np.arange(block_len)[:, None]
    freq = np.arange(block_len)[None, :]
    phases = 2.0 * np.pi / period * (places * freq % period)
    alt = (1 - 2 * (places % 2)).astype(np.float64)
    real_cols = np.where(freq == 0, 1.0, 2.0 * np.cos(phases)) / period
    imag_cols = np.where(freq == 0, alt, -2.0 * np.sin(phases)) / period
    inverse = np.concatenate([np.broadcast_to(real_cols, (block_len, block_len)), imag_cols], axis=1)
    return split_table(forward), split_table(inverse)


def conv_body(finish):
    def kernel(*refs):
        if finish:
            (piece_ref, basis_ref, out_cols_ref, spec_in_ref, query_ref, carried_ref,
             fwd_ref, inv_ref, out_ref, resp_ref) = refs
        else:
            piece_ref, basis_ref, out_cols_ref, fwd_ref, out_ref, resp_ref = refs
        block_total, tables, rows, lanes = piece_ref.shape
        out_cols = out_cols_ref[...]
        cols_hi, cols_lo = split_bf16(out_cols[:-1])
        skip = out_cols[out_cols.shape[0] - 1 :]
        cols = jnp.concatenate([cols_hi, cols_lo, cols_hi], axis=0)

        def dot(a, b):
            return jnp.dot(a, b, preferred_element_type=jnp.float32)

        def fill(block, carry):
            resp_ref[block] = dot(basis_ref[block], cols)
            return carry

        lax.fori_loop(0, block_total, fill, 0)
        first = lax.broadcasted_iota(jnp.int32, (rows, lanes), 0) == 0
        fwd = fwd_ref[...]

        for table in range(tables):

            def one_block(block, acc):
                acc_real, acc_imag, edge = acc
                block_rows = piece_ref[block, table]
                signal = dot(fwd, jnp.concatenate([block_rows, block_rows], axis=0))
                response = resp_ref[block]
                resp_real = response[:rows]
                resp_imag = response[rows:]
                sig_real = signal[:rows]
                sig_imag = signal[rows:]
                acc_real = acc_real + (resp_real * sig_real - resp_imag * sig_imag)
                acc_imag = acc_imag + (resp_real * sig_imag + resp_imag * sig_real)
                edge = edge + resp_imag[0:1] * sig_imag[0:1]
                return acc_real, acc_imag, edge

            zeros = jnp.zeros((rows, lanes), jnp.float32)
            acc_real, acc_imag, edge = lax.fori_loop(
                0, block_total, one_block, (zeros, zeros, jnp.zeros((1, lanes), jnp.float32))
            )
            acc_real = acc_real + jnp.where(first, edge, 0.0)
            acc_imag = jnp.where(first, edge, acc_imag)
            spectrum = jnp.concatenate([acc_real, acc_imag], axis=0)
            if not finish:
                out_ref[table] = spectrum
                continue
            spectrum = spectrum + spec_in_ref[table]
            spec_hi, spec_lo = split_bf16(spectrum)
            conv = dot(inv_ref[...], jnp.concatenate([spec_hi, spec_lo, spec_hi], axis=0))
            gated = query_ref[table] * (conv + skip * carried_ref[table].astype(jnp.float32))
            out_ref[table] = gated.astype(out_ref.dtype)

    return kernel


def fused_conv(piece, basis_spec, out_cols, query_gate=None, carried=None, spec_in=None):
    block_total, tables, rows, width = piece.shape
    finish = spec_in is not None
    basis_hi, basis_lo = split_bf16(basis_spec)
    basis = jnp.concatenate([basis_hi, basis_hi, basis_lo], axis=2)
    fwd, inv = dft_tables(rows)
    fwd = np.concatenate([fwd[0], fwd[1]], axis=1)
    inv = np.concatenate([inv[0], inv[0], inv[1]], axis=1)
    lanes = 768 if width % 768 == 0 else width
    tile3 = lambda i: (0, 0, i)
    specs = [
        pl.BlockSpec((block_total, tables, rows, lanes), lambda i: (0, 0, 0, i)),
        pl.BlockSpec(basis.shape, lambda i: (0, 0, 0)),
        pl.BlockSpec((out_cols.shape[0], lanes), lambda i: (0, i)),
    ]
    operands = [piece, basis, out_cols]
    if finish:
        specs += [
            pl.BlockSpec((tables, 2 * rows, lanes), tile3),
            pl.BlockSpec((tables, rows, lanes), tile3),
            pl.BlockSpec((tables, rows, lanes), tile3),
        ]
        operands += [spec_in, query_gate, carried]
    specs.append(pl.BlockSpec(fwd.shape, lambda i: (0, 0)))
    operands.append(jnp.asarray(fwd))
    if finish:
        specs.append(pl.BlockSpec(inv.shape, lambda i: (0, 0)))
        operands.append(jnp.asarray(inv))
        out_block = (tables, rows, lanes)
        out_shape = jax.ShapeDtypeStruct((tables, rows, width), jnp.bfloat16)
    else:
        out_block = (tables, 2 * rows, lanes)
        out_shape = jax.ShapeDtypeStruct((tables, 2 * rows, width), jnp.float32)
    return pl.pallas_call(
        conv_body(finish),
        grid=(width // lanes,),
        in_specs=specs,
        out_specs=pl.BlockSpec(out_block, tile3),
        out_shape=out_shape,
        scratch_shapes=[pltpu.VMEM((block_total, 2 * rows, lanes), jnp.float32)],
        compiler_params=pltpu.CompilerParams(vmem_limit_bytes=48 * 1024 * 1024),
    )(*operands)


def shards(
    tokens,
    in_weight,
    short_weight,
    basis_in,
    basis_bias,
    basis_mid,
    basis_shift,
    response_out,
    skip_gain,
    block_counts,
):
    seq_dev, block_len, width = tokens.shape
    local_ch = skip_gain.shape[0]
    params = jnp.concatenate(
        [response_out.reshape(2 * response_out.shape[1], local_ch), skip_gain[None, :]], axis=0
    )
    parts = lax.axis_size("groups") * lax.axis_size("seq")
    part = lax.axis_index("groups") * lax.axis_size("seq") + lax.axis_index("seq")
    part_cols = local_ch // parts
    mine = lax.dynamic_slice_in_dim(params, part * part_cols, part_cols, axis=1)
    across = permute_gather(mine, "fsdp", lax.axis_size("fsdp"), lax.axis_index("fsdp"))
    seq_count = lax.axis_size("seq")
    position = lax.axis_index("seq")
    total_len = float(seq_count * block_len)
    forward = forward_table(block_len)
    forward_half = forward[:, :block_len]
    inverse = inverse_table(block_len)
    circular = jnp.arange(2 * block_len, dtype=jnp.int32)
    wrapped = jnp.where(circular < block_len, circular, circular - 2 * block_len)

    block_total = seq_count
    chips = seq_count // 2
    chip, core = position // 2, position % 2
    ring = (chip - jnp.arange(chips, dtype=jnp.int32)) % chips
    order = jnp.concatenate(
        [2 * ring[:1] + core, 2 * ring[:1] + 1 - core, 2 * ring[1:] + core, 2 * ring[1:] + 1 - core]
    )
    offsets = (position - order) * block_len
    lag_values = (offsets[:, None] + wrapped[None, :]).reshape(-1)
    basis_rows = filter_basis(lag_values, total_len, basis_in, basis_bias, basis_mid, basis_shift)
    ahead_mask = (lag_values >= 0).astype(jnp.float32)[:, None]
    paired = jnp.concatenate([basis_rows * ahead_mask, basis_rows * (1.0 - ahead_mask)], axis=1)
    paired = paired.reshape(block_total, 2 * block_len, paired.shape[-1])
    basis_spec = jnp.einsum("gf,bfk->bgk", forward, paired, precision=lax.Precision.HIGHEST)
    local_cols = in_weight.shape[1]

    def project(block):
        rows = jnp.dot(
            block.reshape(seq_dev * block_len, width),
            in_weight,
            preferred_element_type=jnp.float32,
        ).astype(jnp.bfloat16)
        return rows.reshape(seq_dev, block_len, local_cols)

    partial = relay_gather(tokens, "fsdp", project)
    partial, basis_spec, across = lax.optimization_barrier((partial, basis_spec, across))
    gathered = lax.all_gather(across, ("groups", "seq"), axis=0, tiled=False)
    gathered = jnp.transpose(gathered, (2, 1, 0, 3)).reshape(params.shape[0], width)
    projected = lax.all_to_all(partial, "fsdp", 0, 2, tiled=True)
    projected, gathered = lax.optimization_barrier((projected, gathered))
    padded = padded_2(projected, (("seq", 1),), 1)
    shorted = (
        short_weight[0] * padded[:, :-2]
        + short_weight[1] * padded[:, 1:-1]
        + short_weight[2] * padded[:, 2:]
    )
    query_gate = shorted[:, :, :width]
    key_part = shorted[:, :, width : 2 * width]
    value_part = shorted[:, :, 2 * width :]
    valid_mask = (jnp.arange(block_len, dtype=jnp.int32)[None, :] < block_counts).astype(
        jnp.float32
    )
    carried = (key_part * value_part * valid_mask[:, :, None]).astype(jnp.bfloat16)
    partner = [(i, i ^ 1) for i in range(seq_count)]
    near = jnp.stack([carried, lax.ppermute(carried, "seq", partner)])
    far = []
    for shift in range(1, chips):
        far.append(
            lax.ppermute(
                carried, "seq", [(i, (i + 2 * shift) % seq_count) for i in range(seq_count)]
            )
        )
    far = jnp.stack(far)
    near_count = near.shape[0]
    spectrum = fused_conv(near, basis_spec[:near_count], gathered)
    far, spectrum = lax.optimization_barrier((far, spectrum))
    far = jnp.concatenate([far, lax.ppermute(far, "seq", partner)], axis=0)
    return fused_conv(far, basis_spec[near_count:], gathered, query_gate, carried, spectrum)


def solution(mesh):
    placed = (
        P(("groups", "fsdp"), "seq", None),
        P(None, "fsdp"),
        P(),
        P(),
        P(),
        P(),
        P(),
        P(None, None, "fsdp"),
        P("fsdp"),
        P(("groups", "fsdp"), "seq"),
    )
    return jax.shard_map(
        shards,
        mesh=mesh,
        in_specs=placed,
        out_specs=P(("groups", "fsdp"), "seq", None),
        check_vma=False,
    )
```

```python
import jax
import ml_dtypes
import numpy as np
import jax.numpy as jnp
from jax import lax
from jax.sharding import PartitionSpec as P
from jax.experimental import pallas as pl
from jax.experimental.pallas import tpu as pltpu


def padded_2(cells, sides, width):
    for axis, dim in sides:
        count = lax.axis_size(axis)
        ends = count - 1
        head = lax.slice_in_dim(cells, 0, width, axis=dim)
        tail = lax.slice_in_dim(cells, cells.shape[dim] - width, cells.shape[dim], axis=dim)
        cells = jnp.concatenate(
            [
                lax.ppermute(tail, axis, [(i, (i + 1) % count) for i in range(ends)]),
                cells,
                lax.ppermute(head, axis, [((i + 1) % count, i) for i in range(ends)]),
            ],
            axis=dim,
        )
    return cells


def gather_by_permutes(values, axis):
    count = lax.axis_size(axis)
    own = lax.axis_index(axis)
    received = [values]
    for shift in range(1, count):
        received.append(
            lax.ppermute(values, axis, [(i, (i + shift) % count) for i in range(count)])
        )
    stacked = jnp.stack(received)
    sources = (own - jnp.arange(count, dtype=jnp.int32)) % count
    order = jnp.argsort(sources)
    return jnp.take(stacked, order, axis=0)


def relay_gather(values, axis, apply=lambda block: block):
    count = lax.axis_size(axis)
    own = lax.axis_index(axis)
    from_left, from_right = [], []
    rightward, leftward = values, values
    for step in range(1, count):
        rightward = lax.ppermute(rightward, axis, [(j, j + 1) for j in range(step - 1, count - 1)])
        leftward = lax.ppermute(leftward, axis, [(j, j - 1) for j in range(1, count - step + 1)])
        from_left.append(rightward)
        from_right.append(leftward)
    values = apply(values)
    from_left = [apply(block) for block in from_left]
    from_right = [apply(block) for block in from_right]
    chunks = []
    for target in range(count):
        chunk = values
        for step in range(1, count):
            chunk = jnp.where(own - step == target, from_left[step - 1], chunk)
            chunk = jnp.where(own + step == target, from_right[step - 1], chunk)
        chunks.append(chunk)
    return jnp.concatenate(chunks, axis=0)


def permute_gather(values, axis, count, own):
    received = [values]
    for shift in range(1, count):
        received.append(
            lax.ppermute(values, axis, [(i, (i + shift) % count) for i in range(count)])
        )
    chunks = []
    for target in range(count):
        chunk = received[0]
        for shift in range(1, count):
            chunk = jnp.where((own - shift) % count == target, received[shift], chunk)
        chunks.append(chunk)
    return jnp.stack(chunks)


def filter_basis(lag_values, total_len, basis_in, basis_bias, basis_mid, basis_shift):
    band_count = (basis_in.shape[0] - 1) // 2
    distance = jnp.abs(lag_values)
    periods = (2 ** (jnp.arange(band_count, dtype=jnp.int32) + 2) + 1).astype(jnp.int32)
    angles = (
        2.0
        * jnp.pi
        * (distance[:, None] % periods[None, :]).astype(jnp.float32)
        / periods[None, :].astype(jnp.float32)
    )
    linear = distance.astype(jnp.float32)[:, None] / total_len
    encoded = jnp.concatenate([linear, jnp.cos(angles), jnp.sin(angles)], axis=1)
    hidden = jnp.sin(jnp.dot(encoded, basis_in, precision=lax.Precision.HIGHEST) + basis_bias)
    return jnp.sin(jnp.dot(hidden, basis_mid, precision=lax.Precision.HIGHEST) + basis_shift)


def forward_table(block_len):
    period = 2 * block_len
    frequency = jnp.arange(block_len, dtype=jnp.int32)[:, None]
    samples = jnp.arange(period, dtype=jnp.int32)[None, :]
    phases = 2.0 * jnp.pi / period * (frequency * samples % period).astype(jnp.float32)
    alternate = (1 - 2 * (samples % 2)).astype(jnp.float32)
    real_rows = jnp.cos(phases)
    imag_rows = jnp.where(frequency == 0, alternate, -jnp.sin(phases))
    return jnp.concatenate([real_rows, imag_rows], axis=0)


def inverse_table(block_len):
    period = 2 * block_len
    places = jnp.arange(block_len, dtype=jnp.int32)[:, None]
    frequency = jnp.arange(block_len, dtype=jnp.int32)[None, :]
    phases = 2.0 * jnp.pi / period * (places * frequency % period).astype(jnp.float32)
    alternate = (1 - 2 * (places % 2)).astype(jnp.float32)
    real_cols = jnp.where(frequency == 0, 1.0, 2.0 * jnp.cos(phases)) / period
    imag_cols = jnp.where(frequency == 0, alternate, -2.0 * jnp.sin(phases)) / period
    return jnp.concatenate([real_cols, imag_cols], axis=1)


def packed_product(response, signal, block_len):
    first_slot = (jnp.arange(block_len) == 0)[:, None]
    resp_real = response[..., :block_len, :]
    resp_imag = response[..., block_len:, :]
    sig_real = signal[..., :block_len, :]
    sig_imag = signal[..., block_len:, :]
    cross_term = resp_imag * sig_imag
    prod_real = resp_real * sig_real - jnp.where(first_slot, 0.0, cross_term)
    prod_imag = jnp.where(first_slot, cross_term, resp_real * sig_imag + resp_imag * sig_real)
    return jnp.concatenate([prod_real, prod_imag], axis=-2)


def split_bf16(values):
    high = values.astype(jnp.bfloat16)
    return high, (values - high.astype(jnp.float32)).astype(jnp.bfloat16)


def split_table(values):
    high = values.astype(ml_dtypes.bfloat16)
    low = (values - high.astype(np.float64)).astype(ml_dtypes.bfloat16)
    return np.stack([high, low])


def dft_tables(block_len):
    period = 2 * block_len
    frequency = np.arange(block_len)[:, None]
    samples = np.arange(block_len)[None, :]
    phases = 2.0 * np.pi / period * (frequency * samples % period)
    alternate = (1 - 2 * (samples % 2)).astype(np.float64)
    real_rows = np.cos(phases)
    imag_rows = np.where(frequency == 0, alternate, -np.sin(phases))
    forward = np.concatenate([real_rows, imag_rows], axis=0)
    places = np.arange(block_len)[:, None]
    freq = np.arange(block_len)[None, :]
    phases = 2.0 * np.pi / period * (places * freq % period)
    alt = (1 - 2 * (places % 2)).astype(np.float64)
    real_cols = np.where(freq == 0, 1.0, 2.0 * np.cos(phases)) / period
    imag_cols = np.where(freq == 0, alt, -2.0 * np.sin(phases)) / period
    inverse = np.concatenate([np.broadcast_to(real_cols, (block_len, block_len)), imag_cols], axis=1)
    return split_table(forward), split_table(inverse)


def conv_body(finish):
    def kernel(*refs):
        if finish:
            (piece_ref, basis_ref, out_cols_ref, spec_in_ref, query_ref, carried_ref,
             fwd_ref, inv_ref, out_ref, resp_ref) = refs
        else:
            piece_ref, basis_ref, out_cols_ref, fwd_ref, out_ref, resp_ref = refs
        block_total, tables, rows, lanes = piece_ref.shape
        out_cols = out_cols_ref[...]
        cols_hi, cols_lo = split_bf16(out_cols[:-1])
        skip = out_cols[out_cols.shape[0] - 1 :]
        cols = jnp.concatenate([cols_hi, cols_lo, cols_hi], axis=0)

        def dot(a, b):
            return jnp.dot(a, b, preferred_element_type=jnp.float32)

        def fill(block, carry):
            resp_ref[block] = dot(basis_ref[block], cols)
            return carry

        lax.fori_loop(0, block_total, fill, 0)
        first = lax.broadcasted_iota(jnp.int32, (rows, lanes), 0) == 0
        fwd = fwd_ref[...]

        for table in range(tables):

            def one_block(block, acc):
                acc_real, acc_imag, edge = acc
                block_rows = piece_ref[block, table]
                signal = dot(fwd, jnp.concatenate([block_rows, block_rows], axis=0))
                response = resp_ref[block]
                resp_real = response[:rows]
                resp_imag = response[rows:]
                sig_real = signal[:rows]
                sig_imag = signal[rows:]
                acc_real = acc_real + (resp_real * sig_real - resp_imag * sig_imag)
                acc_imag = acc_imag + (resp_real * sig_imag + resp_imag * sig_real)
                edge = edge + resp_imag[0:1] * sig_imag[0:1]
                return acc_real, acc_imag, edge

            zeros = jnp.zeros((rows, lanes), jnp.float32)
            acc_real, acc_imag, edge = lax.fori_loop(
                0, block_total, one_block, (zeros, zeros, jnp.zeros((1, lanes), jnp.float32))
            )
            acc_real = acc_real + jnp.where(first, edge, 0.0)
            acc_imag = jnp.where(first, edge, acc_imag)
            spectrum = jnp.concatenate([acc_real, acc_imag], axis=0)
            if not finish:
                out_ref[table] = spectrum
                continue
            spectrum = spectrum + spec_in_ref[table]
            spec_hi, spec_lo = split_bf16(spectrum)
            conv = dot(inv_ref[...], jnp.concatenate([spec_hi, spec_lo, spec_hi], axis=0))
            gated = query_ref[table] * (conv + skip * carried_ref[table].astype(jnp.float32))
            out_ref[table] = gated.astype(out_ref.dtype)

    return kernel


def fused_conv(piece, basis_spec, out_cols, query_gate=None, carried=None, spec_in=None):
    block_total, tables, rows, width = piece.shape
    finish = spec_in is not None
    basis_hi, basis_lo = split_bf16(basis_spec)
    basis = jnp.concatenate([basis_hi, basis_hi, basis_lo], axis=2)
    fwd, inv = dft_tables(rows)
    fwd = np.concatenate([fwd[0], fwd[1]], axis=1)
    inv = np.concatenate([inv[0], inv[0], inv[1]], axis=1)
    lanes = width if block_total <= 4 or width % 768 else 768
    tile3 = lambda i: (0, 0, i)
    specs = [
        pl.BlockSpec((block_total, tables, rows, lanes), lambda i: (0, 0, 0, i)),
        pl.BlockSpec(basis.shape, lambda i: (0, 0, 0)),
        pl.BlockSpec((out_cols.shape[0], lanes), lambda i: (0, i)),
    ]
    operands = [piece, basis, out_cols]
    if finish:
        specs += [
            pl.BlockSpec((tables, 2 * rows, lanes), tile3),
            pl.BlockSpec((tables, rows, lanes), tile3),
            pl.BlockSpec((tables, rows, lanes), tile3),
        ]
        operands += [spec_in, query_gate, carried]
    specs.append(pl.BlockSpec(fwd.shape, lambda i: (0, 0)))
    operands.append(jnp.asarray(fwd))
    if finish:
        specs.append(pl.BlockSpec(inv.shape, lambda i: (0, 0)))
        operands.append(jnp.asarray(inv))
        out_block = (tables, rows, lanes)
        out_shape = jax.ShapeDtypeStruct((tables, rows, width), jnp.bfloat16)
    else:
        out_block = (tables, 2 * rows, lanes)
        out_shape = jax.ShapeDtypeStruct((tables, 2 * rows, width), jnp.float32)
    return pl.pallas_call(
        conv_body(finish),
        grid=(width // lanes,),
        in_specs=specs,
        out_specs=pl.BlockSpec(out_block, tile3),
        out_shape=out_shape,
        scratch_shapes=[pltpu.VMEM((block_total, 2 * rows, lanes), jnp.float32)],
        compiler_params=pltpu.CompilerParams(vmem_limit_bytes=48 * 1024 * 1024),
    )(*operands)


def shards(
    tokens,
    in_weight,
    short_weight,
    basis_in,
    basis_bias,
    basis_mid,
    basis_shift,
    response_out,
    skip_gain,
    block_counts,
):
    seq_dev, block_len, width = tokens.shape
    local_ch = skip_gain.shape[0]
    params = jnp.concatenate(
        [response_out.reshape(2 * response_out.shape[1], local_ch), skip_gain[None, :]], axis=0
    )
    parts = lax.axis_size("groups") * lax.axis_size("seq")
    part = lax.axis_index("groups") * lax.axis_size("seq") + lax.axis_index("seq")
    part_cols = local_ch // parts
    mine = lax.dynamic_slice_in_dim(params, part * part_cols, part_cols, axis=1)
    across = permute_gather(mine, "fsdp", lax.axis_size("fsdp"), lax.axis_index("fsdp"))
    seq_count = lax.axis_size("seq")
    position = lax.axis_index("seq")
    total_len = float(seq_count * block_len)
    forward = forward_table(block_len)
    forward_half = forward[:, :block_len]
    inverse = inverse_table(block_len)
    circular = jnp.arange(2 * block_len, dtype=jnp.int32)
    wrapped = jnp.where(circular < block_len, circular, circular - 2 * block_len)

    block_total = seq_count
    chips = seq_count // 2
    chip, core = position // 2, position % 2
    ring = (chip - jnp.arange(chips, dtype=jnp.int32)) % chips
    order = jnp.concatenate(
        [2 * ring[:1] + core, 2 * ring[:1] + 1 - core, 2 * ring[1:] + core, 2 * ring[1:] + 1 - core]
    )
    offsets = (position - order) * block_len
    lag_values = (offsets[:, None] + wrapped[None, :]).reshape(-1)
    basis_rows = filter_basis(lag_values, total_len, basis_in, basis_bias, basis_mid, basis_shift)
    ahead_mask = (lag_values >= 0).astype(jnp.float32)[:, None]
    paired = jnp.concatenate([basis_rows * ahead_mask, basis_rows * (1.0 - ahead_mask)], axis=1)
    paired = paired.reshape(block_total, 2 * block_len, paired.shape[-1])
    basis_spec = jnp.einsum("gf,bfk->bgk", forward, paired, precision=lax.Precision.HIGHEST)
    local_cols = in_weight.shape[1]

    def project(block):
        rows = jnp.dot(
            block.reshape(seq_dev * block_len, width),
            in_weight,
            preferred_element_type=jnp.float32,
        ).astype(jnp.bfloat16)
        return rows.reshape(seq_dev, block_len, local_cols)

    partial = relay_gather(tokens, "fsdp", project)
    partial, basis_spec, across = lax.optimization_barrier((partial, basis_spec, across))
    gathered = lax.all_gather(across, ("groups", "seq"), axis=0, tiled=False)
    gathered = jnp.transpose(gathered, (2, 1, 0, 3)).reshape(params.shape[0], width)
    projected = lax.all_to_all(partial, "fsdp", 0, 2, tiled=True)
    projected, gathered = lax.optimization_barrier((projected, gathered))
    padded = padded_2(projected, (("seq", 1),), 1)
    shorted = (
        short_weight[0] * padded[:, :-2]
        + short_weight[1] * padded[:, 1:-1]
        + short_weight[2] * padded[:, 2:]
    )
    query_gate = shorted[:, :, :width]
    key_part = shorted[:, :, width : 2 * width]
    value_part = shorted[:, :, 2 * width :]
    valid_mask = (jnp.arange(block_len, dtype=jnp.int32)[None, :] < block_counts).astype(
        jnp.float32
    )
    carried = (key_part * value_part * valid_mask[:, :, None]).astype(jnp.bfloat16)
    partner = [(i, i ^ 1) for i in range(seq_count)]
    near = jnp.stack([carried, lax.ppermute(carried, "seq", partner)])
    far = []
    for shift in range(1, chips):
        far.append(
            lax.ppermute(
                carried, "seq", [(i, (i + 2 * shift) % seq_count) for i in range(seq_count)]
            )
        )
    far = jnp.stack(far)
    near_count = near.shape[0]
    spectrum = fused_conv(near, basis_spec[:near_count], gathered)
    far, spectrum = lax.optimization_barrier((far, spectrum))
    far = jnp.concatenate([far, lax.ppermute(far, "seq", partner)], axis=0)
    return fused_conv(far, basis_spec[near_count:], gathered, query_gate, carried, spectrum)


def solution(mesh):
    placed = (
        P(("groups", "fsdp"), "seq", None),
        P(None, "fsdp"),
        P(),
        P(),
        P(),
        P(),
        P(),
        P(None, None, "fsdp"),
        P("fsdp"),
        P(("groups", "fsdp"), "seq"),
    )
    return jax.shard_map(
        shards,
        mesh=mesh,
        in_specs=placed,
        out_specs=P(("groups", "fsdp"), "seq", None),
        check_vma=False,
    )
```

```python
import jax
import ml_dtypes
import numpy as np
import jax.numpy as jnp
from jax import lax
from jax.sharding import PartitionSpec as P
from jax.experimental import pallas as pl
from jax.experimental.pallas import tpu as pltpu


def padded_2(cells, sides, width):
    for axis, dim in sides:
        count = lax.axis_size(axis)
        ends = count - 1
        head = lax.slice_in_dim(cells, 0, width, axis=dim)
        tail = lax.slice_in_dim(cells, cells.shape[dim] - width, cells.shape[dim], axis=dim)
        cells = jnp.concatenate(
            [
                lax.ppermute(tail, axis, [(i, (i + 1) % count) for i in range(ends)]),
                cells,
                lax.ppermute(head, axis, [((i + 1) % count, i) for i in range(ends)]),
            ],
            axis=dim,
        )
    return cells


def gather_by_permutes(values, axis):
    count = lax.axis_size(axis)
    own = lax.axis_index(axis)
    received = [values]
    for shift in range(1, count):
        received.append(
            lax.ppermute(values, axis, [(i, (i + shift) % count) for i in range(count)])
        )
    stacked = jnp.stack(received)
    sources = (own - jnp.arange(count, dtype=jnp.int32)) % count
    order = jnp.argsort(sources)
    return jnp.take(stacked, order, axis=0)


def relay_gather(values, axis, apply=lambda block: block):
    count = lax.axis_size(axis)
    own = lax.axis_index(axis)
    from_left, from_right = [], []
    rightward, leftward = values, values
    for step in range(1, count):
        rightward = lax.ppermute(rightward, axis, [(j, j + 1) for j in range(step - 1, count - 1)])
        leftward = lax.ppermute(leftward, axis, [(j, j - 1) for j in range(1, count - step + 1)])
        from_left.append(rightward)
        from_right.append(leftward)
    values = apply(values)
    from_left = [apply(block) for block in from_left]
    from_right = [apply(block) for block in from_right]
    chunks = []
    for target in range(count):
        chunk = values
        for step in range(1, count):
            chunk = jnp.where(own - step == target, from_left[step - 1], chunk)
            chunk = jnp.where(own + step == target, from_right[step - 1], chunk)
        chunks.append(chunk)
    return jnp.concatenate(chunks, axis=0)


def permute_gather(values, axis, count, own):
    received = [values]
    for shift in range(1, count):
        received.append(
            lax.ppermute(values, axis, [(i, (i + shift) % count) for i in range(count)])
        )
    chunks = []
    for target in range(count):
        chunk = received[0]
        for shift in range(1, count):
            chunk = jnp.where((own - shift) % count == target, received[shift], chunk)
        chunks.append(chunk)
    return jnp.stack(chunks)


def filter_basis(lag_values, total_len, basis_in, basis_bias, basis_mid, basis_shift):
    band_count = (basis_in.shape[0] - 1) // 2
    distance = jnp.abs(lag_values)
    periods = (2 ** (jnp.arange(band_count, dtype=jnp.int32) + 2) + 1).astype(jnp.int32)
    angles = (
        2.0
        * jnp.pi
        * (distance[:, None] % periods[None, :]).astype(jnp.float32)
        / periods[None, :].astype(jnp.float32)
    )
    linear = distance.astype(jnp.float32)[:, None] / total_len
    encoded = jnp.concatenate([linear, jnp.cos(angles), jnp.sin(angles)], axis=1)
    hidden = jnp.sin(jnp.dot(encoded, basis_in, precision=lax.Precision.HIGHEST) + basis_bias)
    return jnp.sin(jnp.dot(hidden, basis_mid, precision=lax.Precision.HIGHEST) + basis_shift)


def forward_table(block_len):
    period = 2 * block_len
    frequency = jnp.arange(block_len, dtype=jnp.int32)[:, None]
    samples = jnp.arange(period, dtype=jnp.int32)[None, :]
    phases = 2.0 * jnp.pi / period * (frequency * samples % period).astype(jnp.float32)
    alternate = (1 - 2 * (samples % 2)).astype(jnp.float32)
    real_rows = jnp.cos(phases)
    imag_rows = jnp.where(frequency == 0, alternate, -jnp.sin(phases))
    return jnp.concatenate([real_rows, imag_rows], axis=0)


def inverse_table(block_len):
    period = 2 * block_len
    places = jnp.arange(block_len, dtype=jnp.int32)[:, None]
    frequency = jnp.arange(block_len, dtype=jnp.int32)[None, :]
    phases = 2.0 * jnp.pi / period * (places * frequency % period).astype(jnp.float32)
    alternate = (1 - 2 * (places % 2)).astype(jnp.float32)
    real_cols = jnp.where(frequency == 0, 1.0, 2.0 * jnp.cos(phases)) / period
    imag_cols = jnp.where(frequency == 0, alternate, -2.0 * jnp.sin(phases)) / period
    return jnp.concatenate([real_cols, imag_cols], axis=1)


def packed_product(response, signal, block_len):
    first_slot = (jnp.arange(block_len) == 0)[:, None]
    resp_real = response[..., :block_len, :]
    resp_imag = response[..., block_len:, :]
    sig_real = signal[..., :block_len, :]
    sig_imag = signal[..., block_len:, :]
    cross_term = resp_imag * sig_imag
    prod_real = resp_real * sig_real - jnp.where(first_slot, 0.0, cross_term)
    prod_imag = jnp.where(first_slot, cross_term, resp_real * sig_imag + resp_imag * sig_real)
    return jnp.concatenate([prod_real, prod_imag], axis=-2)


def split_bf16(values):
    high = values.astype(jnp.bfloat16)
    return high, (values - high.astype(jnp.float32)).astype(jnp.bfloat16)


def split_table(values):
    high = values.astype(ml_dtypes.bfloat16)
    low = (values - high.astype(np.float64)).astype(ml_dtypes.bfloat16)
    return np.stack([high, low])


def dft_tables(block_len):
    period = 2 * block_len
    frequency = np.arange(block_len)[:, None]
    samples = np.arange(block_len)[None, :]
    phases = 2.0 * np.pi / period * (frequency * samples % period)
    alternate = (1 - 2 * (samples % 2)).astype(np.float64)
    real_rows = np.cos(phases)
    imag_rows = np.where(frequency == 0, alternate, -np.sin(phases))
    forward = np.concatenate([real_rows, imag_rows], axis=0)
    places = np.arange(block_len)[:, None]
    freq = np.arange(block_len)[None, :]
    phases = 2.0 * np.pi / period * (places * freq % period)
    alt = (1 - 2 * (places % 2)).astype(np.float64)
    real_cols = np.where(freq == 0, 1.0, 2.0 * np.cos(phases)) / period
    imag_cols = np.where(freq == 0, alt, -2.0 * np.sin(phases)) / period
    inverse = np.concatenate([np.broadcast_to(real_cols, (block_len, block_len)), imag_cols], axis=1)
    return split_table(forward), split_table(inverse)


def conv_body(finish):
    def kernel(*refs):
        if finish:
            (piece_ref, resp_ref, out_cols_ref, spec_in_ref, query_ref, carried_ref,
             fwd_ref, inv_ref, out_ref) = refs
        else:
            piece_ref, basis_ref, out_cols_ref, fwd_ref, out_ref, resp_ref = refs
        block_total, tables, rows, lanes = piece_ref.shape
        out_cols = out_cols_ref[...]
        cols_hi, cols_lo = split_bf16(out_cols[:-1])
        skip = out_cols[out_cols.shape[0] - 1 :]
        cols = jnp.concatenate([cols_hi, cols_lo, cols_hi], axis=0)

        def dot(a, b):
            return jnp.dot(a, b, preferred_element_type=jnp.float32)

        def fill(block, carry):
            resp_ref[block] = dot(basis_ref[block], cols)
            return carry

        if not finish:
            lax.fori_loop(0, block_total, fill, 0)
        first = lax.broadcasted_iota(jnp.int32, (rows, lanes), 0) == 0
        fwd = fwd_ref[...]

        for table in range(tables):

            def one_block(block, acc):
                acc_real, acc_imag, edge = acc
                block_rows = piece_ref[block, table]
                signal = dot(fwd, jnp.concatenate([block_rows, block_rows], axis=0))
                response = resp_ref[block]
                resp_real = response[:rows]
                resp_imag = response[rows:]
                sig_real = signal[:rows]
                sig_imag = signal[rows:]
                acc_real = acc_real + (resp_real * sig_real - resp_imag * sig_imag)
                acc_imag = acc_imag + (resp_real * sig_imag + resp_imag * sig_real)
                edge = edge + resp_imag[0:1] * sig_imag[0:1]
                return acc_real, acc_imag, edge

            zeros = jnp.zeros((rows, lanes), jnp.float32)
            acc_real, acc_imag, edge = lax.fori_loop(
                0, block_total, one_block, (zeros, zeros, jnp.zeros((1, lanes), jnp.float32))
            )
            acc_real = acc_real + jnp.where(first, edge, 0.0)
            acc_imag = jnp.where(first, edge, acc_imag)
            spectrum = jnp.concatenate([acc_real, acc_imag], axis=0)
            if not finish:
                out_ref[table] = spectrum
                continue
            spectrum = spectrum + spec_in_ref[table]
            spec_hi, spec_lo = split_bf16(spectrum)
            conv = dot(inv_ref[...], jnp.concatenate([spec_hi, spec_lo, spec_hi], axis=0))
            gated = query_ref[table] * (conv + skip * carried_ref[table].astype(jnp.float32))
            out_ref[table] = gated.astype(out_ref.dtype)

    return kernel


def fused_conv(piece, basis_spec, out_cols, query_gate=None, carried=None, spec_in=None):
    block_total, tables, rows, width = piece.shape
    finish = spec_in is not None
    basis_hi, basis_lo = split_bf16(basis_spec)
    basis = jnp.concatenate([basis_hi, basis_hi, basis_lo], axis=2)
    fwd, inv = dft_tables(rows)
    fwd = np.concatenate([fwd[0], fwd[1]], axis=1)
    inv = np.concatenate([inv[0], inv[0], inv[1]], axis=1)
    lanes = width if block_total <= 4 or width % 768 else 768
    tile3 = lambda i: (0, 0, i)
    if finish:
        cols_hi, cols_lo = split_bf16(out_cols[:-1])
        cols = jnp.concatenate([cols_hi, cols_lo, cols_hi], axis=0)
        response = jnp.einsum("bgk,kd->bgd", basis, cols, preferred_element_type=jnp.float32)
        second = pl.BlockSpec((block_total, 2 * rows, lanes), lambda i: (0, 0, i))
    else:
        response = basis
        second = pl.BlockSpec(basis.shape, lambda i: (0, 0, 0))
    specs = [
        pl.BlockSpec((block_total, tables, rows, lanes), lambda i: (0, 0, 0, i)),
        second,
        pl.BlockSpec((out_cols.shape[0], lanes), lambda i: (0, i)),
    ]
    operands = [piece, response, out_cols]
    if finish:
        specs += [
            pl.BlockSpec((tables, 2 * rows, lanes), tile3),
            pl.BlockSpec((tables, rows, lanes), tile3),
            pl.BlockSpec((tables, rows, lanes), tile3),
        ]
        operands += [spec_in, query_gate, carried]
    specs.append(pl.BlockSpec(fwd.shape, lambda i: (0, 0)))
    operands.append(jnp.asarray(fwd))
    if finish:
        specs.append(pl.BlockSpec(inv.shape, lambda i: (0, 0)))
        operands.append(jnp.asarray(inv))
        out_block = (tables, rows, lanes)
        out_shape = jax.ShapeDtypeStruct((tables, rows, width), jnp.bfloat16)
    else:
        out_block = (tables, 2 * rows, lanes)
        out_shape = jax.ShapeDtypeStruct((tables, 2 * rows, width), jnp.float32)
    return pl.pallas_call(
        conv_body(finish),
        grid=(width // lanes,),
        in_specs=specs,
        out_specs=pl.BlockSpec(out_block, tile3),
        out_shape=out_shape,
        scratch_shapes=[] if finish else [pltpu.VMEM((block_total, 2 * rows, lanes), jnp.float32)],
        compiler_params=pltpu.CompilerParams(vmem_limit_bytes=48 * 1024 * 1024),
    )(*operands)


def shards(
    tokens,
    in_weight,
    short_weight,
    basis_in,
    basis_bias,
    basis_mid,
    basis_shift,
    response_out,
    skip_gain,
    block_counts,
):
    seq_dev, block_len, width = tokens.shape
    local_ch = skip_gain.shape[0]
    params = jnp.concatenate(
        [response_out.reshape(2 * response_out.shape[1], local_ch), skip_gain[None, :]], axis=0
    )
    parts = lax.axis_size("groups") * lax.axis_size("seq")
    part = lax.axis_index("groups") * lax.axis_size("seq") + lax.axis_index("seq")
    part_cols = local_ch // parts
    mine = lax.dynamic_slice_in_dim(params, part * part_cols, part_cols, axis=1)
    across = permute_gather(mine, "fsdp", lax.axis_size("fsdp"), lax.axis_index("fsdp"))
    seq_count = lax.axis_size("seq")
    position = lax.axis_index("seq")
    total_len = float(seq_count * block_len)
    forward = forward_table(block_len)
    forward_half = forward[:, :block_len]
    inverse = inverse_table(block_len)
    circular = jnp.arange(2 * block_len, dtype=jnp.int32)
    wrapped = jnp.where(circular < block_len, circular, circular - 2 * block_len)

    block_total = seq_count
    chips = seq_count // 2
    chip, core = position // 2, position % 2
    ring = (chip - jnp.arange(chips, dtype=jnp.int32)) % chips
    order = jnp.concatenate(
        [2 * ring[:1] + core, 2 * ring[:1] + 1 - core, 2 * ring[1:] + core, 2 * ring[1:] + 1 - core]
    )
    offsets = (position - order) * block_len
    lag_values = (offsets[:, None] + wrapped[None, :]).reshape(-1)
    basis_rows = filter_basis(lag_values, total_len, basis_in, basis_bias, basis_mid, basis_shift)
    ahead_mask = (lag_values >= 0).astype(jnp.float32)[:, None]
    paired = jnp.concatenate([basis_rows * ahead_mask, basis_rows * (1.0 - ahead_mask)], axis=1)
    paired = paired.reshape(block_total, 2 * block_len, paired.shape[-1])
    basis_spec = jnp.einsum("gf,bfk->bgk", forward, paired, precision=lax.Precision.HIGHEST)
    local_cols = in_weight.shape[1]

    def project(block):
        rows = jnp.dot(
            block.reshape(seq_dev * block_len, width),
            in_weight,
            preferred_element_type=jnp.float32,
        ).astype(jnp.bfloat16)
        return rows.reshape(seq_dev, block_len, local_cols)

    partial = relay_gather(tokens, "fsdp", project)
    partial, basis_spec, across = lax.optimization_barrier((partial, basis_spec, across))
    gathered = lax.all_gather(across, ("groups", "seq"), axis=0, tiled=False)
    gathered = jnp.transpose(gathered, (2, 1, 0, 3)).reshape(params.shape[0], width)
    projected = lax.all_to_all(partial, "fsdp", 0, 2, tiled=True)
    projected, gathered = lax.optimization_barrier((projected, gathered))
    padded = padded_2(projected, (("seq", 1),), 1)
    shorted = (
        short_weight[0] * padded[:, :-2]
        + short_weight[1] * padded[:, 1:-1]
        + short_weight[2] * padded[:, 2:]
    )
    query_gate = shorted[:, :, :width]
    key_part = shorted[:, :, width : 2 * width]
    value_part = shorted[:, :, 2 * width :]
    valid_mask = (jnp.arange(block_len, dtype=jnp.int32)[None, :] < block_counts).astype(
        jnp.float32
    )
    carried = (key_part * value_part * valid_mask[:, :, None]).astype(jnp.bfloat16)
    partner = [(i, i ^ 1) for i in range(seq_count)]
    near = jnp.stack([carried, lax.ppermute(carried, "seq", partner)])
    far = []
    for shift in range(1, chips):
        far.append(
            lax.ppermute(
                carried, "seq", [(i, (i + 2 * shift) % seq_count) for i in range(seq_count)]
            )
        )
    far = jnp.stack(far)
    near_count = near.shape[0]
    spectrum = fused_conv(near, basis_spec[:near_count], gathered)
    far, spectrum = lax.optimization_barrier((far, spectrum))
    far = jnp.concatenate([far, lax.ppermute(far, "seq", partner)], axis=0)
    return fused_conv(far, basis_spec[near_count:], gathered, query_gate, carried, spectrum)


def solution(mesh):
    placed = (
        P(("groups", "fsdp"), "seq", None),
        P(None, "fsdp"),
        P(),
        P(),
        P(),
        P(),
        P(),
        P(None, None, "fsdp"),
        P("fsdp"),
        P(("groups", "fsdp"), "seq"),
    )
    return jax.shard_map(
        shards,
        mesh=mesh,
        in_specs=placed,
        out_specs=P(("groups", "fsdp"), "seq", None),
        check_vma=False,
    )
```

```python
import jax
import ml_dtypes
import numpy as np
import jax.numpy as jnp
from jax import lax
from jax.sharding import PartitionSpec as P
from jax.experimental import pallas as pl
from jax.experimental.pallas import tpu as pltpu


def padded_2(cells, sides, width):
    for axis, dim in sides:
        count = lax.axis_size(axis)
        ends = count - 1
        head = lax.slice_in_dim(cells, 0, width, axis=dim)
        tail = lax.slice_in_dim(cells, cells.shape[dim] - width, cells.shape[dim], axis=dim)
        cells = jnp.concatenate(
            [
                lax.ppermute(tail, axis, [(i, (i + 1) % count) for i in range(ends)]),
                cells,
                lax.ppermute(head, axis, [((i + 1) % count, i) for i in range(ends)]),
            ],
            axis=dim,
        )
    return cells


def gather_by_permutes(values, axis):
    count = lax.axis_size(axis)
    own = lax.axis_index(axis)
    received = [values]
    for shift in range(1, count):
        received.append(
            lax.ppermute(values, axis, [(i, (i + shift) % count) for i in range(count)])
        )
    stacked = jnp.stack(received)
    sources = (own - jnp.arange(count, dtype=jnp.int32)) % count
    order = jnp.argsort(sources)
    return jnp.take(stacked, order, axis=0)


def relay_gather(values, axis, apply=lambda block: block):
    count = lax.axis_size(axis)
    own = lax.axis_index(axis)
    from_left, from_right = [], []
    rightward, leftward = values, values
    for step in range(1, count):
        rightward = lax.ppermute(rightward, axis, [(j, j + 1) for j in range(step - 1, count - 1)])
        leftward = lax.ppermute(leftward, axis, [(j, j - 1) for j in range(1, count - step + 1)])
        from_left.append(rightward)
        from_right.append(leftward)
    values = apply(values)
    from_left = [apply(block) for block in from_left]
    from_right = [apply(block) for block in from_right]
    chunks = []
    for target in range(count):
        chunk = values
        for step in range(1, count):
            chunk = jnp.where(own - step == target, from_left[step - 1], chunk)
            chunk = jnp.where(own + step == target, from_right[step - 1], chunk)
        chunks.append(chunk)
    return jnp.stack(chunks)


def permute_gather(values, axis, count, own):
    received = [values]
    for shift in range(1, count):
        received.append(
            lax.ppermute(values, axis, [(i, (i + shift) % count) for i in range(count)])
        )
    chunks = []
    for target in range(count):
        chunk = received[0]
        for shift in range(1, count):
            chunk = jnp.where((own - shift) % count == target, received[shift], chunk)
        chunks.append(chunk)
    return jnp.stack(chunks)


def filter_basis(lag_values, total_len, basis_in, basis_bias, basis_mid, basis_shift):
    band_count = (basis_in.shape[0] - 1) // 2
    distance = jnp.abs(lag_values)
    periods = (2 ** (jnp.arange(band_count, dtype=jnp.int32) + 2) + 1).astype(jnp.int32)
    angles = (
        2.0
        * jnp.pi
        * (distance[:, None] % periods[None, :]).astype(jnp.float32)
        / periods[None, :].astype(jnp.float32)
    )
    linear = distance.astype(jnp.float32)[:, None] / total_len
    encoded = jnp.concatenate([linear, jnp.cos(angles), jnp.sin(angles)], axis=1)
    hidden = jnp.sin(jnp.dot(encoded, basis_in, precision=lax.Precision.HIGHEST) + basis_bias)
    return jnp.sin(jnp.dot(hidden, basis_mid, precision=lax.Precision.HIGHEST) + basis_shift)


def forward_table(block_len):
    period = 2 * block_len
    frequency = jnp.arange(block_len, dtype=jnp.int32)[:, None]
    samples = jnp.arange(period, dtype=jnp.int32)[None, :]
    phases = 2.0 * jnp.pi / period * (frequency * samples % period).astype(jnp.float32)
    alternate = (1 - 2 * (samples % 2)).astype(jnp.float32)
    real_rows = jnp.cos(phases)
    imag_rows = jnp.where(frequency == 0, alternate, -jnp.sin(phases))
    return jnp.concatenate([real_rows, imag_rows], axis=0)


def inverse_table(block_len):
    period = 2 * block_len
    places = jnp.arange(block_len, dtype=jnp.int32)[:, None]
    frequency = jnp.arange(block_len, dtype=jnp.int32)[None, :]
    phases = 2.0 * jnp.pi / period * (places * frequency % period).astype(jnp.float32)
    alternate = (1 - 2 * (places % 2)).astype(jnp.float32)
    real_cols = jnp.where(frequency == 0, 1.0, 2.0 * jnp.cos(phases)) / period
    imag_cols = jnp.where(frequency == 0, alternate, -2.0 * jnp.sin(phases)) / period
    return jnp.concatenate([real_cols, imag_cols], axis=1)


def packed_product(response, signal, block_len):
    first_slot = (jnp.arange(block_len) == 0)[:, None]
    resp_real = response[..., :block_len, :]
    resp_imag = response[..., block_len:, :]
    sig_real = signal[..., :block_len, :]
    sig_imag = signal[..., block_len:, :]
    cross_term = resp_imag * sig_imag
    prod_real = resp_real * sig_real - jnp.where(first_slot, 0.0, cross_term)
    prod_imag = jnp.where(first_slot, cross_term, resp_real * sig_imag + resp_imag * sig_real)
    return jnp.concatenate([prod_real, prod_imag], axis=-2)


def split_bf16(values):
    high = values.astype(jnp.bfloat16)
    return high, (values - high.astype(jnp.float32)).astype(jnp.bfloat16)


def split_table(values):
    high = values.astype(ml_dtypes.bfloat16)
    low = (values - high.astype(np.float64)).astype(ml_dtypes.bfloat16)
    return np.stack([high, low])


def dft_tables(block_len):
    period = 2 * block_len
    frequency = np.arange(block_len)[:, None]
    samples = np.arange(block_len)[None, :]
    phases = 2.0 * np.pi / period * (frequency * samples % period)
    alternate = (1 - 2 * (samples % 2)).astype(np.float64)
    real_rows = np.cos(phases)
    imag_rows = np.where(frequency == 0, alternate, -np.sin(phases))
    forward = np.concatenate([real_rows, imag_rows], axis=0)
    places = np.arange(block_len)[:, None]
    freq = np.arange(block_len)[None, :]
    phases = 2.0 * np.pi / period * (places * freq % period)
    alt = (1 - 2 * (places % 2)).astype(np.float64)
    real_cols = np.where(freq == 0, 1.0, 2.0 * np.cos(phases)) / period
    imag_cols = np.where(freq == 0, alt, -2.0 * np.sin(phases)) / period
    inverse = np.concatenate([np.broadcast_to(real_cols, (block_len, block_len)), imag_cols], axis=1)
    return split_table(forward), split_table(inverse)


def conv_body(finish):
    def kernel(*refs):
        if finish:
            (piece_ref, basis_ref, out_cols_ref, spec_in_ref, query_ref, carried_ref,
             fwd_ref, inv_ref, out_ref, resp_ref) = refs
        else:
            piece_ref, basis_ref, out_cols_ref, fwd_ref, out_ref, resp_ref = refs
        block_total, tables, rows, lanes = piece_ref.shape
        out_cols = out_cols_ref[...]
        cols_hi, cols_lo = split_bf16(out_cols[:-1])
        skip = out_cols[out_cols.shape[0] - 1 :]
        cols = jnp.concatenate([cols_hi, cols_lo, cols_hi], axis=0)

        def dot(a, b):
            return jnp.dot(a, b, preferred_element_type=jnp.float32)

        def fill(block, carry):
            resp_ref[block] = dot(basis_ref[block], cols)
            return carry

        lax.fori_loop(0, block_total, fill, 0)
        first = lax.broadcasted_iota(jnp.int32, (rows, lanes), 0) == 0
        fwd = fwd_ref[...]

        for table in range(tables):

            def one_block(block, acc):
                acc_real, acc_imag, edge = acc
                block_rows = piece_ref[block, table]
                signal = dot(fwd, jnp.concatenate([block_rows, block_rows], axis=0))
                response = resp_ref[block]
                resp_real = response[:rows]
                resp_imag = response[rows:]
                sig_real = signal[:rows]
                sig_imag = signal[rows:]
                acc_real = acc_real + (resp_real * sig_real - resp_imag * sig_imag)
                acc_imag = acc_imag + (resp_real * sig_imag + resp_imag * sig_real)
                edge = edge + resp_imag[0:1] * sig_imag[0:1]
                return acc_real, acc_imag, edge

            zeros = jnp.zeros((rows, lanes), jnp.float32)
            acc_real, acc_imag, edge = lax.fori_loop(
                0, block_total, one_block, (zeros, zeros, jnp.zeros((1, lanes), jnp.float32))
            )
            acc_real = acc_real + jnp.where(first, edge, 0.0)
            acc_imag = jnp.where(first, edge, acc_imag)
            spectrum = jnp.concatenate([acc_real, acc_imag], axis=0)
            if not finish:
                out_ref[table] = spectrum
                continue
            spectrum = spectrum + spec_in_ref[table]
            spec_hi, spec_lo = split_bf16(spectrum)
            conv = dot(inv_ref[...], jnp.concatenate([spec_hi, spec_lo, spec_hi], axis=0))
            gated = query_ref[table] * (conv + skip * carried_ref[table].astype(jnp.float32))
            out_ref[table] = gated.astype(out_ref.dtype)

    return kernel


def fused_conv(piece, basis_spec, out_cols, query_gate=None, carried=None, spec_in=None):
    block_total, tables, rows, width = piece.shape
    finish = spec_in is not None
    basis_hi, basis_lo = split_bf16(basis_spec)
    basis = jnp.concatenate([basis_hi, basis_hi, basis_lo], axis=2)
    fwd, inv = dft_tables(rows)
    fwd = np.concatenate([fwd[0], fwd[1]], axis=1)
    inv = np.concatenate([inv[0], inv[0], inv[1]], axis=1)
    lanes = width if block_total <= 4 or width % 768 else 768
    tile3 = lambda i: (0, 0, i)
    specs = [
        pl.BlockSpec((block_total, tables, rows, lanes), lambda i: (0, 0, 0, i)),
        pl.BlockSpec(basis.shape, lambda i: (0, 0, 0)),
        pl.BlockSpec((out_cols.shape[0], lanes), lambda i: (0, i)),
    ]
    operands = [piece, basis, out_cols]
    if finish:
        specs += [
            pl.BlockSpec((tables, 2 * rows, lanes), tile3),
            pl.BlockSpec((tables, rows, lanes), tile3),
            pl.BlockSpec((tables, rows, lanes), tile3),
        ]
        operands += [spec_in, query_gate, carried]
    specs.append(pl.BlockSpec(fwd.shape, lambda i: (0, 0)))
    operands.append(jnp.asarray(fwd))
    if finish:
        specs.append(pl.BlockSpec(inv.shape, lambda i: (0, 0)))
        operands.append(jnp.asarray(inv))
        out_block = (tables, rows, lanes)
        out_shape = jax.ShapeDtypeStruct((tables, rows, width), jnp.bfloat16)
    else:
        out_block = (tables, 2 * rows, lanes)
        out_shape = jax.ShapeDtypeStruct((tables, 2 * rows, width), jnp.float32)
    return pl.pallas_call(
        conv_body(finish),
        grid=(width // lanes,),
        in_specs=specs,
        out_specs=pl.BlockSpec(out_block, tile3),
        out_shape=out_shape,
        scratch_shapes=[pltpu.VMEM((block_total, 2 * rows, lanes), jnp.float32)],
        compiler_params=pltpu.CompilerParams(vmem_limit_bytes=48 * 1024 * 1024),
    )(*operands)


def shards(
    tokens,
    in_weight,
    short_weight,
    basis_in,
    basis_bias,
    basis_mid,
    basis_shift,
    response_out,
    skip_gain,
    block_counts,
):
    seq_dev, block_len, width = tokens.shape
    local_ch = skip_gain.shape[0]
    params = jnp.concatenate(
        [response_out.reshape(2 * response_out.shape[1], local_ch), skip_gain[None, :]], axis=0
    )
    parts = lax.axis_size("groups") * lax.axis_size("seq")
    part = lax.axis_index("groups") * lax.axis_size("seq") + lax.axis_index("seq")
    part_cols = local_ch // parts
    mine = lax.dynamic_slice_in_dim(params, part * part_cols, part_cols, axis=1)
    across = permute_gather(mine, "fsdp", lax.axis_size("fsdp"), lax.axis_index("fsdp"))
    seq_count = lax.axis_size("seq")
    position = lax.axis_index("seq")
    total_len = float(seq_count * block_len)
    forward = forward_table(block_len)
    forward_half = forward[:, :block_len]
    inverse = inverse_table(block_len)
    circular = jnp.arange(2 * block_len, dtype=jnp.int32)
    wrapped = jnp.where(circular < block_len, circular, circular - 2 * block_len)

    block_total = seq_count
    chips = seq_count // 2
    chip, core = position // 2, position % 2
    ring = (chip - jnp.arange(chips, dtype=jnp.int32)) % chips
    order = jnp.concatenate(
        [2 * ring[:1] + core, 2 * ring[:1] + 1 - core, 2 * ring[1:] + core, 2 * ring[1:] + 1 - core]
    )
    offsets = (position - order) * block_len
    lag_values = (offsets[:, None] + wrapped[None, :]).reshape(-1)
    basis_rows = filter_basis(lag_values, total_len, basis_in, basis_bias, basis_mid, basis_shift)
    ahead_mask = (lag_values >= 0).astype(jnp.float32)[:, None]
    paired = jnp.concatenate([basis_rows * ahead_mask, basis_rows * (1.0 - ahead_mask)], axis=1)
    paired = paired.reshape(block_total, 2 * block_len, paired.shape[-1])
    basis_spec = jnp.einsum("gf,bfk->bgk", forward, paired, precision=lax.Precision.HIGHEST)
    local_cols = in_weight.shape[1]

    def project(block):
        rows = jnp.dot(
            block.reshape(seq_dev * block_len, width),
            in_weight,
            preferred_element_type=jnp.float32,
        ).astype(jnp.bfloat16)
        return rows.reshape(seq_dev, block_len, local_cols)

    partial = relay_gather(tokens, "fsdp", project)
    partial, basis_spec, across = lax.optimization_barrier((partial, basis_spec, across))
    gathered = lax.all_gather(across, ("groups", "seq"), axis=0, tiled=False)
    gathered = jnp.transpose(gathered, (2, 1, 0, 3)).reshape(params.shape[0], width)
    projected = lax.all_to_all(partial, "fsdp", 0, 3, tiled=True)[0]
    projected, gathered = lax.optimization_barrier((projected, gathered))
    padded = padded_2(projected, (("seq", 1),), 1)
    shorted = (
        short_weight[0] * padded[:, :-2]
        + short_weight[1] * padded[:, 1:-1]
        + short_weight[2] * padded[:, 2:]
    )
    query_gate = shorted[:, :, :width]
    key_part = shorted[:, :, width : 2 * width]
    value_part = shorted[:, :, 2 * width :]
    valid_mask = (jnp.arange(block_len, dtype=jnp.int32)[None, :] < block_counts).astype(
        jnp.float32
    )
    carried = (key_part * value_part * valid_mask[:, :, None]).astype(jnp.bfloat16)
    partner = [(i, i ^ 1) for i in range(seq_count)]
    near = jnp.stack([carried, lax.ppermute(carried, "seq", partner)])
    far = []
    for shift in range(1, chips):
        far.append(
            lax.ppermute(
                carried, "seq", [(i, (i + 2 * shift) % seq_count) for i in range(seq_count)]
            )
        )
    far = jnp.stack(far)
    near_count = near.shape[0]
    spectrum = fused_conv(near, basis_spec[:near_count], gathered)
    far, spectrum = lax.optimization_barrier((far, spectrum))
    far = jnp.concatenate([far, lax.ppermute(far, "seq", partner)], axis=0)
    return fused_conv(far, basis_spec[near_count:], gathered, query_gate, carried, spectrum)


def solution(mesh):
    placed = (
        P(("groups", "fsdp"), "seq", None),
        P(None, "fsdp"),
        P(),
        P(),
        P(),
        P(),
        P(),
        P(None, None, "fsdp"),
        P("fsdp"),
        P(("groups", "fsdp"), "seq"),
    )
    return jax.shard_map(
        shards,
        mesh=mesh,
        in_specs=placed,
        out_specs=P(("groups", "fsdp"), "seq", None),
        check_vma=False,
    )
```

```python
import jax
import ml_dtypes
import numpy as np
import jax.numpy as jnp
from jax import lax
from jax.sharding import PartitionSpec as P
from jax.experimental import pallas as pl
from jax.experimental.pallas import tpu as pltpu


def padded_2(cells, sides, width):
    for axis, dim in sides:
        count = lax.axis_size(axis)
        ends = count - 1
        head = lax.slice_in_dim(cells, 0, width, axis=dim)
        tail = lax.slice_in_dim(cells, cells.shape[dim] - width, cells.shape[dim], axis=dim)
        cells = jnp.concatenate(
            [
                lax.ppermute(tail, axis, [(i, (i + 1) % count) for i in range(ends)]),
                cells,
                lax.ppermute(head, axis, [((i + 1) % count, i) for i in range(ends)]),
            ],
            axis=dim,
        )
    return cells


def gather_by_permutes(values, axis):
    count = lax.axis_size(axis)
    own = lax.axis_index(axis)
    received = [values]
    for shift in range(1, count):
        received.append(
            lax.ppermute(values, axis, [(i, (i + shift) % count) for i in range(count)])
        )
    stacked = jnp.stack(received)
    sources = (own - jnp.arange(count, dtype=jnp.int32)) % count
    order = jnp.argsort(sources)
    return jnp.take(stacked, order, axis=0)


def relay_gather(values, axis, apply=lambda block: block):
    count = lax.axis_size(axis)
    own = lax.axis_index(axis)
    from_left, from_right = [], []
    rightward, leftward = values, values
    for step in range(1, count):
        rightward = lax.ppermute(rightward, axis, [(j, j + 1) for j in range(step - 1, count - 1)])
        leftward = lax.ppermute(leftward, axis, [(j, j - 1) for j in range(1, count - step + 1)])
        from_left.append(rightward)
        from_right.append(leftward)
    values = apply(values)
    from_left = [apply(block) for block in from_left]
    from_right = [apply(block) for block in from_right]
    chunks = []
    for target in range(count):
        chunk = values
        for step in range(1, count):
            chunk = jnp.where(own - step == target, from_left[step - 1], chunk)
            chunk = jnp.where(own + step == target, from_right[step - 1], chunk)
        chunks.append(chunk)
    return jnp.concatenate(chunks, axis=0)


def permute_gather(values, axis, count, own):
    received = [values]
    for shift in range(1, count):
        received.append(
            lax.ppermute(values, axis, [(i, (i + shift) % count) for i in range(count)])
        )
    chunks = []
    for target in range(count):
        chunk = received[0]
        for shift in range(1, count):
            chunk = jnp.where((own - shift) % count == target, received[shift], chunk)
        chunks.append(chunk)
    return jnp.stack(chunks)


def filter_basis(lag_values, total_len, basis_in, basis_bias, basis_mid, basis_shift):
    band_count = (basis_in.shape[0] - 1) // 2
    distance = jnp.abs(lag_values)
    periods = (2 ** (jnp.arange(band_count, dtype=jnp.int32) + 2) + 1).astype(jnp.int32)
    angles = (
        2.0
        * jnp.pi
        * (distance[:, None] % periods[None, :]).astype(jnp.float32)
        / periods[None, :].astype(jnp.float32)
    )
    linear = distance.astype(jnp.float32)[:, None] / total_len
    encoded = jnp.concatenate([linear, jnp.cos(angles), jnp.sin(angles)], axis=1)
    hidden = jnp.sin(jnp.dot(encoded, basis_in, precision=lax.Precision.HIGHEST) + basis_bias)
    return jnp.sin(jnp.dot(hidden, basis_mid, precision=lax.Precision.HIGHEST) + basis_shift)


def forward_table(block_len):
    period = 2 * block_len
    frequency = jnp.arange(block_len, dtype=jnp.int32)[:, None]
    samples = jnp.arange(period, dtype=jnp.int32)[None, :]
    phases = 2.0 * jnp.pi / period * (frequency * samples % period).astype(jnp.float32)
    alternate = (1 - 2 * (samples % 2)).astype(jnp.float32)
    real_rows = jnp.cos(phases)
    imag_rows = jnp.where(frequency == 0, alternate, -jnp.sin(phases))
    return jnp.concatenate([real_rows, imag_rows], axis=0)


def inverse_table(block_len):
    period = 2 * block_len
    places = jnp.arange(block_len, dtype=jnp.int32)[:, None]
    frequency = jnp.arange(block_len, dtype=jnp.int32)[None, :]
    phases = 2.0 * jnp.pi / period * (places * frequency % period).astype(jnp.float32)
    alternate = (1 - 2 * (places % 2)).astype(jnp.float32)
    real_cols = jnp.where(frequency == 0, 1.0, 2.0 * jnp.cos(phases)) / period
    imag_cols = jnp.where(frequency == 0, alternate, -2.0 * jnp.sin(phases)) / period
    return jnp.concatenate([real_cols, imag_cols], axis=1)


def packed_product(response, signal, block_len):
    first_slot = (jnp.arange(block_len) == 0)[:, None]
    resp_real = response[..., :block_len, :]
    resp_imag = response[..., block_len:, :]
    sig_real = signal[..., :block_len, :]
    sig_imag = signal[..., block_len:, :]
    cross_term = resp_imag * sig_imag
    prod_real = resp_real * sig_real - jnp.where(first_slot, 0.0, cross_term)
    prod_imag = jnp.where(first_slot, cross_term, resp_real * sig_imag + resp_imag * sig_real)
    return jnp.concatenate([prod_real, prod_imag], axis=-2)


def split_bf16(values):
    high = values.astype(jnp.bfloat16)
    return high, (values - high.astype(jnp.float32)).astype(jnp.bfloat16)


def split_table(values):
    high = values.astype(ml_dtypes.bfloat16)
    low = (values - high.astype(np.float64)).astype(ml_dtypes.bfloat16)
    return np.stack([high, low])


def dft_tables(block_len):
    period = 2 * block_len
    frequency = np.arange(block_len)[:, None]
    samples = np.arange(block_len)[None, :]
    phases = 2.0 * np.pi / period * (frequency * samples % period)
    alternate = (1 - 2 * (samples % 2)).astype(np.float64)
    real_rows = np.cos(phases)
    imag_rows = np.where(frequency == 0, alternate, -np.sin(phases))
    forward = np.concatenate([real_rows, imag_rows], axis=0)
    places = np.arange(block_len)[:, None]
    freq = np.arange(block_len)[None, :]
    phases = 2.0 * np.pi / period * (places * freq % period)
    alt = (1 - 2 * (places % 2)).astype(np.float64)
    real_cols = np.where(freq == 0, 1.0, 2.0 * np.cos(phases)) / period
    imag_cols = np.where(freq == 0, alt, -2.0 * np.sin(phases)) / period
    inverse = np.concatenate([np.broadcast_to(real_cols, (block_len, block_len)), imag_cols], axis=1)
    return split_table(forward), split_table(inverse)


def conv_body(finish):
    def kernel(*refs):
        if finish:
            (piece_ref, basis_ref, out_cols_ref, spec_in_ref, query_ref, carried_ref,
             fwd_ref, inv_ref, out_ref, resp_ref) = refs
        else:
            piece_ref, basis_ref, out_cols_ref, fwd_ref, out_ref, resp_ref = refs
        block_total, tables, rows, lanes = piece_ref.shape
        out_cols = out_cols_ref[...]
        cols_hi, cols_lo = split_bf16(out_cols[:-1])
        skip = out_cols[out_cols.shape[0] - 1 :]
        cols = jnp.concatenate([cols_hi, cols_lo, cols_hi], axis=0)

        def dot(a, b):
            return jnp.dot(a, b, preferred_element_type=jnp.float32)

        def fill(block, carry):
            resp_ref[block] = dot(basis_ref[block], cols)
            return carry

        lax.fori_loop(0, block_total, fill, 0)
        first = lax.broadcasted_iota(jnp.int32, (rows, lanes), 0) == 0
        fwd = fwd_ref[...]

        for table in range(tables):

            def one_block(block, acc):
                acc_real, acc_imag, edge = acc
                block_rows = piece_ref[block, table]
                signal = dot(fwd, jnp.concatenate([block_rows, block_rows], axis=0))
                response = resp_ref[block]
                resp_real = response[:rows]
                resp_imag = response[rows:]
                sig_real = signal[:rows]
                sig_imag = signal[rows:]
                acc_real = acc_real + (resp_real * sig_real - resp_imag * sig_imag)
                acc_imag = acc_imag + (resp_real * sig_imag + resp_imag * sig_real)
                edge = edge + resp_imag[0:1] * sig_imag[0:1]
                return acc_real, acc_imag, edge

            zeros = jnp.zeros((rows, lanes), jnp.float32)
            acc_real, acc_imag, edge = lax.fori_loop(
                0, block_total, one_block, (zeros, zeros, jnp.zeros((1, lanes), jnp.float32))
            )
            acc_real = acc_real + jnp.where(first, edge, 0.0)
            acc_imag = jnp.where(first, edge, acc_imag)
            spectrum = jnp.concatenate([acc_real, acc_imag], axis=0)
            if not finish:
                out_ref[table] = spectrum
                continue
            spectrum = spectrum + spec_in_ref[table]
            spec_hi, spec_lo = split_bf16(spectrum)
            conv = dot(inv_ref[...], jnp.concatenate([spec_hi, spec_lo, spec_hi], axis=0))
            gated = query_ref[table] * (conv + skip * carried_ref[table].astype(jnp.float32))
            out_ref[table] = gated.astype(out_ref.dtype)

    return kernel


def fused_conv(piece, basis_spec, out_cols, query_gate=None, carried=None, spec_in=None):
    block_total, tables, rows, width = piece.shape
    finish = spec_in is not None
    basis_hi, basis_lo = split_bf16(basis_spec)
    basis = jnp.concatenate([basis_hi, basis_hi, basis_lo], axis=2)
    fwd, inv = dft_tables(rows)
    fwd = np.concatenate([fwd[0], fwd[1]], axis=1)
    inv = np.concatenate([inv[0], inv[0], inv[1]], axis=1)
    lanes = width if (block_total <= 4 and not finish) or width % 768 else 768
    tile3 = lambda i: (0, 0, i)
    specs = [
        pl.BlockSpec((block_total, tables, rows, lanes), lambda i: (0, 0, 0, i)),
        pl.BlockSpec(basis.shape, lambda i: (0, 0, 0)),
        pl.BlockSpec((out_cols.shape[0], lanes), lambda i: (0, i)),
    ]
    operands = [piece, basis, out_cols]
    if finish:
        specs += [
            pl.BlockSpec((tables, 2 * rows, lanes), tile3),
            pl.BlockSpec((tables, rows, lanes), tile3),
            pl.BlockSpec((tables, rows, lanes), tile3),
        ]
        operands += [spec_in, query_gate, carried]
    specs.append(pl.BlockSpec(fwd.shape, lambda i: (0, 0)))
    operands.append(jnp.asarray(fwd))
    if finish:
        specs.append(pl.BlockSpec(inv.shape, lambda i: (0, 0)))
        operands.append(jnp.asarray(inv))
        out_block = (tables, rows, lanes)
        out_shape = jax.ShapeDtypeStruct((tables, rows, width), jnp.bfloat16)
    else:
        out_block = (tables, 2 * rows, lanes)
        out_shape = jax.ShapeDtypeStruct((tables, 2 * rows, width), jnp.float32)
    return pl.pallas_call(
        conv_body(finish),
        grid=(width // lanes,),
        in_specs=specs,
        out_specs=pl.BlockSpec(out_block, tile3),
        out_shape=out_shape,
        scratch_shapes=[pltpu.VMEM((block_total, 2 * rows, lanes), jnp.float32)],
        compiler_params=pltpu.CompilerParams(vmem_limit_bytes=48 * 1024 * 1024),
    )(*operands)


def shards(
    tokens,
    in_weight,
    short_weight,
    basis_in,
    basis_bias,
    basis_mid,
    basis_shift,
    response_out,
    skip_gain,
    block_counts,
):
    seq_dev, block_len, width = tokens.shape
    local_ch = skip_gain.shape[0]
    params = jnp.concatenate(
        [response_out.reshape(2 * response_out.shape[1], local_ch), skip_gain[None, :]], axis=0
    )
    parts = lax.axis_size("groups") * lax.axis_size("seq")
    part = lax.axis_index("groups") * lax.axis_size("seq") + lax.axis_index("seq")
    part_cols = local_ch // parts
    mine = lax.dynamic_slice_in_dim(params, part * part_cols, part_cols, axis=1)
    across = permute_gather(mine, "fsdp", lax.axis_size("fsdp"), lax.axis_index("fsdp"))
    seq_count = lax.axis_size("seq")
    position = lax.axis_index("seq")
    total_len = float(seq_count * block_len)
    forward = forward_table(block_len)
    forward_half = forward[:, :block_len]
    inverse = inverse_table(block_len)
    circular = jnp.arange(2 * block_len, dtype=jnp.int32)
    wrapped = jnp.where(circular < block_len, circular, circular - 2 * block_len)

    block_total = seq_count
    chips = seq_count // 2
    chip, core = position // 2, position % 2
    ring = (chip - jnp.arange(chips, dtype=jnp.int32)) % chips
    order = jnp.concatenate(
        [2 * ring[:1] + core, 2 * ring[:1] + 1 - core, 2 * ring[1:] + core, 2 * ring[1:] + 1 - core]
    )
    offsets = (position - order) * block_len
    lag_values = (offsets[:, None] + wrapped[None, :]).reshape(-1)
    basis_rows = filter_basis(lag_values, total_len, basis_in, basis_bias, basis_mid, basis_shift)
    ahead_mask = (lag_values >= 0).astype(jnp.float32)[:, None]
    paired = jnp.concatenate([basis_rows * ahead_mask, basis_rows * (1.0 - ahead_mask)], axis=1)
    paired = paired.reshape(block_total, 2 * block_len, paired.shape[-1])
    basis_spec = jnp.einsum("gf,bfk->bgk", forward, paired, precision=lax.Precision.HIGHEST)
    local_cols = in_weight.shape[1]

    def project(block):
        rows = jnp.dot(
            block.reshape(seq_dev * block_len, width),
            in_weight,
            preferred_element_type=jnp.float32,
        ).astype(jnp.bfloat16)
        return rows.reshape(seq_dev, block_len, local_cols)

    partial = relay_gather(tokens, "fsdp", project)
    partial, basis_spec, across = lax.optimization_barrier((partial, basis_spec, across))
    gathered = lax.all_gather(across, ("groups", "seq"), axis=0, tiled=False)
    gathered = jnp.transpose(gathered, (2, 1, 0, 3)).reshape(params.shape[0], width)
    projected = lax.all_to_all(partial, "fsdp", 0, 2, tiled=True)
    projected, gathered = lax.optimization_barrier((projected, gathered))
    padded = padded_2(projected, (("seq", 1),), 1)
    shorted = (
        short_weight[0] * padded[:, :-2]
        + short_weight[1] * padded[:, 1:-1]
        + short_weight[2] * padded[:, 2:]
    )
    query_gate = shorted[:, :, :width]
    key_part = shorted[:, :, width : 2 * width]
    value_part = shorted[:, :, 2 * width :]
    valid_mask = (jnp.arange(block_len, dtype=jnp.int32)[None, :] < block_counts).astype(
        jnp.float32
    )
    carried = (key_part * value_part * valid_mask[:, :, None]).astype(jnp.bfloat16)
    partner = [(i, i ^ 1) for i in range(seq_count)]
    near = jnp.stack([carried, lax.ppermute(carried, "seq", partner)])
    far = []
    for shift in range(1, chips):
        far.append(
            lax.ppermute(
                carried, "seq", [(i, (i + 2 * shift) % seq_count) for i in range(seq_count)]
            )
        )
    far = jnp.stack(far)
    near_count = near.shape[0]
    spectrum = fused_conv(near, basis_spec[:near_count], gathered)
    far, spectrum = lax.optimization_barrier((far, spectrum))
    far = jnp.concatenate([far, lax.ppermute(far, "seq", partner)], axis=0)
    return fused_conv(far, basis_spec[near_count:], gathered, query_gate, carried, spectrum)


def solution(mesh):
    placed = (
        P(("groups", "fsdp"), "seq", None),
        P(None, "fsdp"),
        P(),
        P(),
        P(),
        P(),
        P(),
        P(None, None, "fsdp"),
        P("fsdp"),
        P(("groups", "fsdp"), "seq"),
    )
    return jax.shard_map(
        shards,
        mesh=mesh,
        in_specs=placed,
        out_specs=P(("groups", "fsdp"), "seq", None),
        check_vma=False,
    )
```
